768 devices in a mesh: gx: 96 (over z, x, core), gy: 8 (over y).
Axes of the slice: x: 4, y: 8, z: 12, core: 2. Of those that a mesh axis runs over, the one named last changes fastest.
Arguments:
- populations: float32 [19, 3, 3072, 1024], P(None, None, 'gx', 'gy'), may hold values from 0.2 to 1
- solid_flag: int32 [3, 3072, 1024], P(None, 'gx', 'gy'), may hold values 0 or 1
- cell_patch: int32 [3, 3072, 1024], P(None, 'gx', 'gy'), may hold values from 0 to 512
- patch_zone: int32 [393216], P(('gx', 'gy')), may hold values from 0 to 98303, as said below
- old_pressure: float32 [98304], P(('gx', 'gy')), may hold values from -6 to 6
- leakage: float32 [98304], P(('gx', 'gy')), may hold values from 0.1 to 1
- conductance: float32 [6, 98304], P(None, ('gx', 'gy')), may hold values from 0.05 to 0.5
- neighbour: int32 [6, 98304], P(None, ('gx', 'gy')), may hold values from 0 to 127
Outputs:
- new_populations: float32 [19, 3, 3072, 1024], P(None, None, 'gx', 'gy')
- zone_pressure: float32 [98304], P(('gx', 'gy'))
- opening_pressure: float32 [393216], P(('gx', 'gy'))
The draws below stay inside these ranges and needn't reach their ends.
Inputs may be any that keep to these rules, and one draw needn't show every extreme that they name: `patch_zone`: within each aligned block of 512 patches (one tile), at most 2 patches name zones of one block of 128 zones, and in every tile some block of zones receives exactly 2. `cell_patch`: the value 512 marks a cell in no opening.
All inputs are finite; a program needn't handle non-finite values. No bound on the sum of `solid_flag` on one device may be relied on, other than what follows from the above.
Results may differ from the reference program's by a relative error of at most 0.00002.
Values sent between devices are 32-bit elements; how exact they have to be, the bound alone decides.
No kernel may reach another device: no remote copies, remote signals or barrier semaphores. Data moves between devices by JAX's collectives and lax.ppermute only.
A program may use at most 32 MiB of HBM per device.

```python
import math
import jax
import jax.numpy as jnp
import numpy as np
from jax import lax

CX = 32
CY = 128
LEVELS = 3
P_DEV = 512
ZONE_DEV = 128
LINKS = 6
CAP = 2
NX = 3072
NY = 1024
ZONES = 98304
N_GY = 8
DEVICES = 768


def draw_patch_zone(key, part):
    key_hot = jax.random.fold_in(key, 11)
    key_score = jax.random.fold_in(key, 12)
    key_extra = jax.random.fold_in(key, 13)
    key_local = jax.random.fold_in(key, 14)
    key_order = jax.random.fold_in(key, 15)
    groups = (P_DEV + CAP - 1) // CAP
    hot_owner = (jax.random.permutation(key_hot, DEVICES) < DEVICES // 8).astype(jnp.int32)
    base_score = jax.random.randint(key_score, (DEVICES, DEVICES), 0, 4096)
    extra_score = jax.random.randint(key_extra, (DEVICES, DEVICES), 0, 1024) * hot_owner[None, :]
    score = (base_score + extra_score) * DEVICES + jnp.arange(DEVICES, dtype=jnp.int32)[None, :]
    chosen = lax.top_k(score, groups)[1].astype(jnp.int32)
    owners = jnp.repeat(chosen, CAP, axis=1)[:, :P_DEV]
    order_score = jax.random.randint(key_order, (DEVICES, P_DEV), 0, 65536) * P_DEV + jnp.arange(P_DEV, dtype=jnp.int32)[None, :]
    shuffle = jnp.argsort(order_score, axis=1)
    owners = jnp.take_along_axis(owners, shuffle, axis=1)
    local_zone = jax.random.randint(key_local, (DEVICES, P_DEV), 0, ZONE_DEV)
    return (owners * ZONE_DEV + local_zone).reshape(-1).astype(jnp.int32)


def place_ends(values, own_key, smallest, high):
    dims = values.shape
    index_at = [jax.random.randint(jax.random.fold_in(own_key, axis), (), 0, dims[axis]) for axis in range(len(dims))]
    values = values.at[tuple(index_at)].set(smallest)
    longest = dims.index(max(dims))
    index_at[longest] = (index_at[longest] + 1) % dims[longest]
    return values.at[tuple(index_at)].set(high)


def levels(stream_key, shape, cuts, low, largest):
    factor_of, own = 1.0, jax.random.fold_in(stream_key, 6)
    for axis_at, parts in cuts:
        heights = jnp.exp(jax.random.uniform(jax.random.fold_in(own, axis_at), (parts,), jnp.float32, low / len(cuts), largest / len(cuts)))
        factor_of = factor_of * jnp.repeat(heights, shape[axis_at] // parts).reshape([-1 if axis == axis_at else 1 for axis in range(len(shape))])
    return factor_of


def normal_values(stream_key, shape, scale, limit, split=(), held_as=jnp.bfloat16):
    drawn = scale * jax.random.normal(stream_key, shape, jnp.float32)
    if split:
        drawn = drawn * levels(stream_key, shape, split, -0.22, 0.18)
    return jnp.clip(drawn, -limit, limit).astype(held_as)


def setup_inputs(seed: int = 0) -> dict:
    key_list = jax.random.split(jax.random.key(seed), 9)
    return {
        "populations": jnp.clip(0.2 + 0.8 * jax.random.uniform(key_list[0], (19, LEVELS, NX, NY), jnp.float32) ** levels(key_list[0], (19, LEVELS, NX, NY), ((2, 96), (3, 8)), -0.2, 0.2), 0.2, 1.0),
        "solid_flag": place_ends((jax.random.randint(key_list[1], (LEVELS, NX, NY), 0, 8) < 1).astype(jnp.int32), jax.random.fold_in(key_list[1], 1), 0, 1),
        "cell_patch": place_ends(jax.random.randint(key_list[2], (LEVELS, NX, NY), 0, P_DEV + 1), jax.random.fold_in(key_list[2], 1), 0, P_DEV).astype(jnp.int32),
        "patch_zone": draw_patch_zone(jax.random.fold_in(key_list[8], 71), 0),
        "old_pressure": normal_values(key_list[4], (ZONES,), 1.0, 6.0, ((0, 768),), jnp.float32),
        "leakage": jnp.clip(jnp.exp(math.log(1.0) - 2.3025851 * jax.random.uniform(key_list[5], (ZONES,), jnp.float32) ** levels(key_list[5], (ZONES,), ((0, 768),), -0.2, 0.2)), 0.1, 1.0),
        "conductance": jnp.clip(jnp.exp(math.log(0.5) - 2.3025851 * jax.random.uniform(key_list[6], (LINKS, ZONES), jnp.float32) ** levels(key_list[6], (LINKS, ZONES), ((1, 768),), -0.2, 0.2)), 0.05, 0.5),
        "neighbour": place_ends(jax.random.randint(key_list[7], (LINKS, ZONES), 0, ZONE_DEV), jax.random.fold_in(key_list[7], 1), 0, ZONE_DEV - 1).astype(jnp.int32),
    }


DIRECTIONS = np.array([[0, 0, 0], [1, 0, 0], [-1, 0, 0], [0, 1, 0], [0, -1, 0], [0, 0, 1], [0, 0, -1],
                       [1, 1, 0], [-1, -1, 0], [1, -1, 0], [-1, 1, 0], [1, 0, 1], [-1, 0, -1],
                       [1, 0, -1], [-1, 0, 1], [0, 1, 1], [0, -1, -1], [0, 1, -1], [0, -1, 1]])
OPPOSITE = [0, 2, 1, 4, 3, 6, 5, 8, 7, 10, 9, 12, 11, 14, 13, 16, 15, 18, 17]
LATTICE_WEIGHTS = [1.0 / 3.0] + [1.0 / 18.0] * 6 + [1.0 / 36.0] * 12
OMEGA = 1.25
FACE_AREA = 0.25


def moment(populations, component):
    total = jnp.zeros_like(populations[0])
    for direction in range(19):
        sign = int(DIRECTIONS[direction, component])
        if sign != 0:
            total = total + float(sign) * populations[direction]
    return total


def collide(populations):
    density = jnp.zeros_like(populations[0])
    for direction in range(19):
        density = density + populations[direction]
    velocity = [moment(populations, component) / density for component in range(3)]
    speed_sq = velocity[0] * velocity[0] + velocity[1] * velocity[1] + velocity[2] * velocity[2]
    relaxed = []
    for direction in range(19):
        along = jnp.zeros_like(density)
        for component in range(3):
            sign = int(DIRECTIONS[direction, component])
            if sign != 0:
                along = along + float(sign) * velocity[component]
        equilibrium = LATTICE_WEIGHTS[direction] * density * (1.0 + 3.0 * along + 4.5 * along * along - 1.5 * speed_sq)
        relaxed.append(populations[direction] - OMEGA * (populations[direction] - equilibrium))
    return jnp.stack(relaxed)


def stream(post_pad, flag_pad, relaxed, populations, solid_flag):
    depth, width_x, width_y = solid_flag.shape
    passed = []
    for direction in range(19):
        step_x = int(DIRECTIONS[direction, 0])
        step_y = int(DIRECTIONS[direction, 1])
        step_z = int(DIRECTIONS[direction, 2])
        source = post_pad[direction, 1 - step_z:1 - step_z + depth, 1 - step_x:1 - step_x + width_x, 1 - step_y:1 - step_y + width_y]
        open_source = flag_pad[1 - step_z:1 - step_z + depth, 1 - step_x:1 - step_x + width_x, 1 - step_y:1 - step_y + width_y]
        pulled = open_source * source + (1.0 - open_source) * relaxed[OPPOSITE[direction]]
        passed.append(jnp.where(solid_flag == 1, populations[direction], pulled))
    return jnp.stack(passed)


def relax(inflow, old_pressure, leakage, conductance, neighbour):
    coupled = jnp.zeros_like(inflow)
    total = leakage
    for link in range(conductance.shape[0]):
        coupled = coupled + conductance[link] * old_pressure[neighbour[link]]
        total = total + conductance[link]
    return (inflow + coupled) / total


def reference(populations, solid_flag, cell_patch, patch_zone, old_pressure, leakage, conductance, neighbour):
    relaxed = collide(populations)
    fluid = (1 - solid_flag).astype(jnp.float32)
    post_pad = jnp.pad(relaxed, ((0, 0), (1, 1), (0, 0), (1, 1)))
    post_pad = jnp.concatenate([post_pad[:, :, -1:], post_pad, post_pad[:, :, :1]], axis=2)
    flag_pad = jnp.pad(fluid, ((1, 1), (0, 0), (1, 1)))
    flag_pad = jnp.concatenate([flag_pad[:, -1:], flag_pad, flag_pad[:, :1]], axis=1)
    new_populations = stream(post_pad, flag_pad, relaxed, populations, solid_flag)
    momentum_x = moment(new_populations, 0)
    tile_x = jnp.arange(NX, dtype=jnp.int32) // CX
    tile_y = jnp.arange(NY, dtype=jnp.int32) // CY
    tile_index = tile_x[:, None] * N_GY + tile_y[None, :]
    segment = tile_index[None, :, :] * (P_DEV + 1) + cell_patch
    sums = jax.ops.segment_sum(momentum_x.reshape(-1), segment.reshape(-1), num_segments=DEVICES * (P_DEV + 1))
    patch_flux = FACE_AREA * sums.reshape(DEVICES, P_DEV + 1)[:, :P_DEV].reshape(-1)
    inflow = jax.ops.segment_sum(patch_flux, patch_zone, num_segments=ZONES)
    block_base = (jnp.arange(ZONES, dtype=jnp.int32) // ZONE_DEV) * ZONE_DEV
    zone_pressure = relax(inflow, old_pressure, leakage, conductance, neighbour + block_base[None, :])
    opening_pressure = zone_pressure[patch_zone]
    return new_populations, zone_pressure, opening_pressure
```

```python
import jax
import jax.numpy as jnp
import numpy as np
from jax import lax
from jax.sharding import PartitionSpec as P

DIRECTIONS = np.array(
    [
        [0, 0, 0],
        [1, 0, 0],
        [-1, 0, 0],
        [0, 1, 0],
        [0, -1, 0],
        [0, 0, 1],
        [0, 0, -1],
        [1, 1, 0],
        [-1, -1, 0],
        [1, -1, 0],
        [-1, 1, 0],
        [1, 0, 1],
        [-1, 0, -1],
        [1, 0, -1],
        [-1, 0, 1],
        [0, 1, 1],
        [0, -1, -1],
        [0, 1, -1],
        [0, -1, 1],
    ]
)
OPPOSITE = [0, 2, 1, 4, 3, 6, 5, 8, 7, 10, 9, 12, 11, 14, 13, 16, 15, 18, 17]
LATTICE_WEIGHTS = [1.0 / 3.0] + [1.0 / 18.0] * 6 + [1.0 / 36.0] * 12
OMEGA = 1.25
FACE_AREA = 0.25


def with_halo(cells, sides, width):
    for axis, dim in sides:
        count = lax.axis_size(axis)
        head = lax.slice_in_dim(cells, 0, width, axis=dim)
        tail = lax.slice_in_dim(cells, cells.shape[dim] - width, cells.shape[dim], axis=dim)
        cells = jnp.concatenate(
            [
                lax.ppermute(tail, axis, [(i, (i + 1) % count) for i in range(count)]),
                cells,
                lax.ppermute(head, axis, [((i + 1) % count, i) for i in range(count)]),
            ],
            axis=dim,
        )
    return cells


def moment(populations, component):
    total = jnp.zeros_like(populations[0])
    for direction in range(19):
        sign = int(DIRECTIONS[direction, component])
        if sign != 0:
            total = total + float(sign) * populations[direction]
    return total


def collide(populations):
    density = jnp.zeros_like(populations[0])
    for direction in range(19):
        density = density + populations[direction]
    velocity = [moment(populations, component) / density for component in range(3)]
    speed_sq = velocity[0] * velocity[0] + velocity[1] * velocity[1] + velocity[2] * velocity[2]
    relaxed = []
    for direction in range(19):
        along = jnp.zeros_like(density)
        for component in range(3):
            sign = int(DIRECTIONS[direction, component])
            if sign != 0:
                along = along + float(sign) * velocity[component]
        equilibrium = (
            LATTICE_WEIGHTS[direction]
            * density
            * (1.0 + 3.0 * along + 4.5 * along * along - 1.5 * speed_sq)
        )
        relaxed.append(populations[direction] - OMEGA * (populations[direction] - equilibrium))
    return jnp.stack(relaxed)


def stream(post_pad, flag_pad, relaxed, populations, solid_flag):
    depth, width_x, width_y = solid_flag.shape
    passed = []
    for direction in range(19):
        step_x = int(DIRECTIONS[direction, 0])
        step_y = int(DIRECTIONS[direction, 1])
        step_z = int(DIRECTIONS[direction, 2])
        source = post_pad[
            direction,
            1 - step_z : 1 - step_z + depth,
            1 - step_x : 1 - step_x + width_x,
            1 - step_y : 1 - step_y + width_y,
        ]
        open_source = flag_pad[
            1 - step_z : 1 - step_z + depth,
            1 - step_x : 1 - step_x + width_x,
            1 - step_y : 1 - step_y + width_y,
        ]
        pulled = open_source * source + (1.0 - open_source) * relaxed[OPPOSITE[direction]]
        passed.append(jnp.where(solid_flag == 1, populations[direction], pulled))
    return jnp.stack(passed)


def relax(inflow, old_pressure, leakage, conductance, neighbour):
    coupled = jnp.zeros_like(inflow)
    total = leakage
    for link in range(conductance.shape[0]):
        coupled = coupled + conductance[link] * old_pressure[neighbour[link]]
        total = total + conductance[link]
    return (inflow + coupled) / total


def on_device(
    populations, solid_flag, cell_patch, patch_zone, old_pressure, leakage, conductance, neighbour
):
    depth, width_x, width_y = solid_flag.shape
    relaxed = collide(populations)
    fluid = (1 - solid_flag).astype(jnp.float32)
    column = lax.axis_index("gy")
    lower_open = jnp.where(column > 0, 1.0, 0.0).astype(jnp.float32)
    upper_open = jnp.where(column < lax.axis_size("gy") - 1, 1.0, 0.0).astype(jnp.float32)
    places = jnp.arange(width_y + 2, dtype=jnp.int32)
    keeper = jnp.where(places == 0, lower_open, jnp.where(places == width_y + 1, upper_open, 1.0))
    stacked = jnp.concatenate([relaxed, fluid[None]], axis=0)
    widened = with_halo(stacked, (("gx", 2), ("gy", 3)), 1)
    widened = jnp.pad(widened, ((0, 0), (1, 1), (0, 0), (0, 0)))
    flag_pad = widened[19] * keeper
    post_pad = widened[:19]
    new_populations = stream(post_pad, flag_pad, relaxed, populations, solid_flag)
    momentum_x = moment(new_populations, 0)
    patch_flux = patch_sums(momentum_x, cell_patch, patch_zone.shape[0])
    zone_dev = old_pressure.shape[0]
    count_x = lax.axis_size("gx")
    count_y = lax.axis_size("gy")
    blocks = count_x * count_y
    own_block = lax.axis_index("gx") * count_y + lax.axis_index("gy")
    owner_block = patch_zone // zone_dev
    local_zone = patch_zone - owner_block * zone_dev
    in_block = owner_block[:, None] == jnp.arange(blocks, dtype=jnp.int32)[None, :]
    at_zone = local_zone[:, None] == jnp.arange(zone_dev, dtype=jnp.int32)[None, :]
    contributed = jnp.einsum(
        "pb,pl->bl",
        in_block.astype(jnp.float32),
        jnp.where(at_zone, patch_flux[:, None], 0.0),
        precision=lax.Precision.HIGHEST,
    )
    coupled, total = couple(old_pressure, leakage, conductance, neighbour)
    is_own = (jnp.arange(blocks, dtype=jnp.int32) == own_block)[:, None]
    numer = contributed + jnp.where(is_own, coupled[None, :], 0.0)
    denom = jnp.where(is_own, total[None, :], 0.0)
    summed = lax.psum(jnp.stack([numer, denom]), ("gx", "gy"))
    pressure = summed[0] / summed[1]
    zone_pressure = lax.dynamic_index_in_dim(pressure, own_block, axis=0, keepdims=False)
    picked = jnp.einsum(
        "pb,bl->pl", in_block.astype(jnp.float32), pressure, precision=lax.Precision.HIGHEST
    )
    opening_pressure = jnp.sum(jnp.where(at_zone, picked, 0.0), axis=1)
    return (new_populations, zone_pressure, opening_pressure)


def patch_sums(momentum_x, cell_patch, openings):
    depth, width_x, width_y = cell_patch.shape
    rows = depth * width_x
    momentum = momentum_x.reshape(rows, width_y)
    patch = cell_patch.reshape(rows, width_y)
    lanes = 128
    high = patch // lanes
    low = patch - high * lanes
    groups = openings // lanes
    picked = jnp.where(
        high[None] == jnp.arange(groups, dtype=jnp.int32)[:, None, None], momentum[None], 0.0
    )
    onehot = (low[:, :, None] == jnp.arange(lanes, dtype=jnp.int32)[None, None, :]).astype(
        jnp.float32
    )
    sums = jnp.einsum("hry,ryl->hl", picked, onehot, precision=lax.Precision.HIGHEST)
    return FACE_AREA * sums.reshape(openings)


def couple(old_pressure, leakage, conductance, neighbour):
    zone_dev = old_pressure.shape[0]
    chosen = neighbour[:, :, None] == jnp.arange(zone_dev, dtype=jnp.int32)[None, None, :]
    neighbour_pressure = jnp.sum(jnp.where(chosen, old_pressure[None, None, :], 0.0), axis=2)
    coupled = jnp.zeros_like(old_pressure)
    total = leakage
    for link in range(conductance.shape[0]):
        coupled = coupled + conductance[link] * neighbour_pressure[link]
        total = total + conductance[link]
    return coupled, total


def solution(mesh):
    placed = (
        P(None, None, "gx", "gy"),
        P(None, "gx", "gy"),
        P(None, "gx", "gy"),
        P(("gx", "gy")),
        P(("gx", "gy")),
        P(("gx", "gy")),
        P(None, ("gx", "gy")),
        P(None, ("gx", "gy")),
    )
    return jax.shard_map(
        on_device,
        mesh=mesh,
        in_specs=placed,
        out_specs=(P(None, None, "gx", "gy"), P(("gx", "gy")), P(("gx", "gy"))),
        check_vma=False,
    )
```

```python
import jax
import jax.numpy as jnp
import numpy as np
from jax import lax
from jax.sharding import PartitionSpec as P

DIRECTIONS = np.array(
    [
        [0, 0, 0],
        [1, 0, 0],
        [-1, 0, 0],
        [0, 1, 0],
        [0, -1, 0],
        [0, 0, 1],
        [0, 0, -1],
        [1, 1, 0],
        [-1, -1, 0],
        [1, -1, 0],
        [-1, 1, 0],
        [1, 0, 1],
        [-1, 0, -1],
        [1, 0, -1],
        [-1, 0, 1],
        [0, 1, 1],
        [0, -1, -1],
        [0, 1, -1],
        [0, -1, 1],
    ]
)
OPPOSITE = [0, 2, 1, 4, 3, 6, 5, 8, 7, 10, 9, 12, 11, 14, 13, 16, 15, 18, 17]
LATTICE_WEIGHTS = [1.0 / 3.0] + [1.0 / 18.0] * 6 + [1.0 / 36.0] * 12
OMEGA = 1.25
FACE_AREA = 0.25


def with_halo(cells, sides, width):
    for axis, dim in sides:
        count = lax.axis_size(axis)
        head = lax.slice_in_dim(cells, 0, width, axis=dim)
        tail = lax.slice_in_dim(cells, cells.shape[dim] - width, cells.shape[dim], axis=dim)
        cells = jnp.concatenate(
            [
                lax.ppermute(tail, axis, [(i, (i + 1) % count) for i in range(count)]),
                cells,
                lax.ppermute(head, axis, [((i + 1) % count, i) for i in range(count)]),
            ],
            axis=dim,
        )
    return cells


def moment(populations, component):
    total = jnp.zeros_like(populations[0])
    for direction in range(19):
        sign = int(DIRECTIONS[direction, component])
        if sign != 0:
            total = total + float(sign) * populations[direction]
    return total


def collide(populations):
    density = jnp.zeros_like(populations[0])
    for direction in range(19):
        density = density + populations[direction]
    velocity = [moment(populations, component) / density for component in range(3)]
    speed_sq = velocity[0] * velocity[0] + velocity[1] * velocity[1] + velocity[2] * velocity[2]
    relaxed = []
    for direction in range(19):
        along = jnp.zeros_like(density)
        for component in range(3):
            sign = int(DIRECTIONS[direction, component])
            if sign != 0:
                along = along + float(sign) * velocity[component]
        equilibrium = (
            LATTICE_WEIGHTS[direction]
            * density
            * (1.0 + 3.0 * along + 4.5 * along * along - 1.5 * speed_sq)
        )
        relaxed.append(populations[direction] - OMEGA * (populations[direction] - equilibrium))
    return jnp.stack(relaxed)


def stream(post_pad, flag_pad, relaxed, populations, solid_flag):
    depth, width_x, width_y = solid_flag.shape
    passed = []
    for direction in range(19):
        step_x = int(DIRECTIONS[direction, 0])
        step_y = int(DIRECTIONS[direction, 1])
        step_z = int(DIRECTIONS[direction, 2])
        source = post_pad[
            direction,
            1 - step_z : 1 - step_z + depth,
            1 - step_x : 1 - step_x + width_x,
            1 - step_y : 1 - step_y + width_y,
        ]
        open_source = flag_pad[
            1 - step_z : 1 - step_z + depth,
            1 - step_x : 1 - step_x + width_x,
            1 - step_y : 1 - step_y + width_y,
        ]
        pulled = open_source * source + (1.0 - open_source) * relaxed[OPPOSITE[direction]]
        passed.append(jnp.where(solid_flag == 1, populations[direction], pulled))
    return jnp.stack(passed)


def relax(inflow, old_pressure, leakage, conductance, neighbour):
    coupled = jnp.zeros_like(inflow)
    total = leakage
    for link in range(conductance.shape[0]):
        coupled = coupled + conductance[link] * old_pressure[neighbour[link]]
        total = total + conductance[link]
    return (inflow + coupled) / total


def on_device(
    populations, solid_flag, cell_patch, patch_zone, old_pressure, leakage, conductance, neighbour
):
    depth, width_x, width_y = solid_flag.shape
    relaxed = collide(populations)
    fluid = (1 - solid_flag).astype(jnp.float32)
    column = lax.axis_index("gy")
    lower_open = jnp.where(column > 0, 1.0, 0.0).astype(jnp.float32)
    upper_open = jnp.where(column < lax.axis_size("gy") - 1, 1.0, 0.0).astype(jnp.float32)
    places = jnp.arange(width_y + 2, dtype=jnp.int32)
    keeper = jnp.where(places == 0, lower_open, jnp.where(places == width_y + 1, upper_open, 1.0))
    stacked = jnp.concatenate([relaxed, fluid[None]], axis=0)
    widened = with_halo(stacked, (("gx", 2), ("gy", 3)), 1)
    widened = jnp.pad(widened, ((0, 0), (1, 1), (0, 0), (0, 0)))
    flag_pad = widened[19] * keeper
    post_pad = widened[:19]
    new_populations = stream(post_pad, flag_pad, relaxed, populations, solid_flag)
    momentum_x = moment(new_populations, 0)
    patch_flux = patch_sums(momentum_x, cell_patch, patch_zone.shape[0])
    zone_dev = old_pressure.shape[0]
    openings = patch_zone.shape[0]
    devices = lax.axis_size("gx") * lax.axis_size("gy")
    capacity = max(2, (2 * openings + devices - 1) // devices)
    owner_block = patch_zone // zone_dev
    local_zone = patch_zone - owner_block * zone_dev
    patch_order = jnp.arange(openings, dtype=jnp.int32)
    earlier_same = (owner_block[:, None] == owner_block[None, :]) & (
        patch_order[:, None] > patch_order[None, :]
    )
    slot_rank = jnp.sum(earlier_same.astype(jnp.int32), axis=1)
    slot_index = owner_block * capacity + slot_rank
    targets = jnp.arange(devices * capacity, dtype=jnp.int32)
    placed = slot_index[:, None] == targets[None, :]
    send_flux = jnp.sum(jnp.where(placed, patch_flux[:, None], 0.0), axis=0)
    send_zone = jnp.sum(jnp.where(placed, local_zone.astype(jnp.float32)[:, None], 0.0), axis=0)
    outgoing = jnp.stack([send_flux, send_zone]).reshape(2, devices, capacity)
    arrived = lax.all_to_all(
        outgoing, ("gx", "gy"), split_axis=1, concat_axis=1, tiled=True
    ).reshape(2, devices * capacity)
    matched = arrived[1][None, :] == jnp.arange(zone_dev, dtype=jnp.float32)[:, None]
    inflow = jnp.sum(jnp.where(matched, arrived[0][None, :], 0.0), axis=1)
    coupled, total = couple(old_pressure, leakage, conductance, neighbour)
    zone_pressure = (inflow + coupled) / total
    answered = jnp.sum(jnp.where(matched, zone_pressure[:, None], 0.0), axis=0).reshape(
        devices, capacity
    )
    returned = lax.all_to_all(
        answered, ("gx", "gy"), split_axis=0, concat_axis=0, tiled=True
    ).reshape(-1)
    opening_pressure = jnp.sum(jnp.where(placed, returned[None, :], 0.0), axis=1)
    return (new_populations, zone_pressure, opening_pressure)


def patch_sums(momentum_x, cell_patch, openings):
    depth, width_x, width_y = cell_patch.shape
    rows = depth * width_x
    momentum = momentum_x.reshape(rows, width_y)
    patch = cell_patch.reshape(rows, width_y)
    lanes = 128
    high = patch // lanes
    low = patch - high * lanes
    groups = openings // lanes
    picked = jnp.where(
        high[None] == jnp.arange(groups, dtype=jnp.int32)[:, None, None], momentum[None], 0.0
    )
    onehot = (low[:, :, None] == jnp.arange(lanes, dtype=jnp.int32)[None, None, :]).astype(
        jnp.float32
    )
    sums = jnp.einsum("hry,ryl->hl", picked, onehot, precision=lax.Precision.HIGHEST)
    return FACE_AREA * sums.reshape(openings)


def couple(old_pressure, leakage, conductance, neighbour):
    zone_dev = old_pressure.shape[0]
    chosen = neighbour[:, :, None] == jnp.arange(zone_dev, dtype=jnp.int32)[None, None, :]
    neighbour_pressure = jnp.sum(jnp.where(chosen, old_pressure[None, None, :], 0.0), axis=2)
    coupled = jnp.zeros_like(old_pressure)
    total = leakage
    for link in range(conductance.shape[0]):
        coupled = coupled + conductance[link] * neighbour_pressure[link]
        total = total + conductance[link]
    return coupled, total


def solution(mesh):
    placed = (
        P(None, None, "gx", "gy"),
        P(None, "gx", "gy"),
        P(None, "gx", "gy"),
        P(("gx", "gy")),
        P(("gx", "gy")),
        P(("gx", "gy")),
        P(None, ("gx", "gy")),
        P(None, ("gx", "gy")),
    )
    return jax.shard_map(
        on_device,
        mesh=mesh,
        in_specs=placed,
        out_specs=(P(None, None, "gx", "gy"), P(("gx", "gy")), P(("gx", "gy"))),
        check_vma=False,
    )
```

```python
import jax
import jax.numpy as jnp
import numpy as np
from jax import lax
from jax.sharding import PartitionSpec as P

DIRECTIONS = np.array(
    [
        [0, 0, 0],
        [1, 0, 0],
        [-1, 0, 0],
        [0, 1, 0],
        [0, -1, 0],
        [0, 0, 1],
        [0, 0, -1],
        [1, 1, 0],
        [-1, -1, 0],
        [1, -1, 0],
        [-1, 1, 0],
        [1, 0, 1],
        [-1, 0, -1],
        [1, 0, -1],
        [-1, 0, 1],
        [0, 1, 1],
        [0, -1, -1],
        [0, 1, -1],
        [0, -1, 1],
    ]
)
OPPOSITE = [0, 2, 1, 4, 3, 6, 5, 8, 7, 10, 9, 12, 11, 14, 13, 16, 15, 18, 17]
LATTICE_WEIGHTS = [1.0 / 3.0] + [1.0 / 18.0] * 6 + [1.0 / 36.0] * 12
OMEGA = 1.25
FACE_AREA = 0.25


def with_halo(cells, sides, width):
    for axis, dim in sides:
        count = lax.axis_size(axis)
        head = lax.slice_in_dim(cells, 0, width, axis=dim)
        tail = lax.slice_in_dim(cells, cells.shape[dim] - width, cells.shape[dim], axis=dim)
        cells = jnp.concatenate(
            [
                lax.ppermute(tail, axis, [(i, (i + 1) % count) for i in range(count)]),
                cells,
                lax.ppermute(head, axis, [((i + 1) % count, i) for i in range(count)]),
            ],
            axis=dim,
        )
    return cells


def moment(populations, component):
    total = jnp.zeros_like(populations[0])
    for direction in range(19):
        sign = int(DIRECTIONS[direction, component])
        if sign != 0:
            total = total + float(sign) * populations[direction]
    return total


def collide(populations):
    density = jnp.zeros_like(populations[0])
    for direction in range(19):
        density = density + populations[direction]
    velocity = [moment(populations, component) / density for component in range(3)]
    speed_sq = velocity[0] * velocity[0] + velocity[1] * velocity[1] + velocity[2] * velocity[2]
    relaxed = []
    for direction in range(19):
        along = jnp.zeros_like(density)
        for component in range(3):
            sign = int(DIRECTIONS[direction, component])
            if sign != 0:
                along = along + float(sign) * velocity[component]
        equilibrium = (
            LATTICE_WEIGHTS[direction]
            * density
            * (1.0 + 3.0 * along + 4.5 * along * along - 1.5 * speed_sq)
        )
        relaxed.append(populations[direction] - OMEGA * (populations[direction] - equilibrium))
    return jnp.stack(relaxed)


def stream(post_pad, flag_pad, relaxed, populations, solid_flag):
    depth, width_x, width_y = solid_flag.shape
    passed = []
    for direction in range(19):
        step_x = int(DIRECTIONS[direction, 0])
        step_y = int(DIRECTIONS[direction, 1])
        step_z = int(DIRECTIONS[direction, 2])
        source = post_pad[
            direction,
            1 - step_z : 1 - step_z + depth,
            1 - step_x : 1 - step_x + width_x,
            1 - step_y : 1 - step_y + width_y,
        ]
        open_source = flag_pad[
            1 - step_z : 1 - step_z + depth,
            1 - step_x : 1 - step_x + width_x,
            1 - step_y : 1 - step_y + width_y,
        ]
        pulled = open_source * source + (1.0 - open_source) * relaxed[OPPOSITE[direction]]
        passed.append(jnp.where(solid_flag == 1, populations[direction], pulled))
    return jnp.stack(passed)


def relax(inflow, old_pressure, leakage, conductance, neighbour):
    coupled = jnp.zeros_like(inflow)
    total = leakage
    for link in range(conductance.shape[0]):
        coupled = coupled + conductance[link] * old_pressure[neighbour[link]]
        total = total + conductance[link]
    return (inflow + coupled) / total


def on_device(
    populations, solid_flag, cell_patch, patch_zone, old_pressure, leakage, conductance, neighbour
):
    depth, width_x, width_y = solid_flag.shape
    relaxed = collide(populations)
    fluid = (1 - solid_flag).astype(jnp.float32)
    column = lax.axis_index("gy")
    lower_open = jnp.where(column > 0, 1.0, 0.0).astype(jnp.float32)
    upper_open = jnp.where(column < lax.axis_size("gy") - 1, 1.0, 0.0).astype(jnp.float32)
    places = jnp.arange(width_y + 2, dtype=jnp.int32)
    keeper = jnp.where(places == 0, lower_open, jnp.where(places == width_y + 1, upper_open, 1.0))
    stacked = jnp.concatenate([relaxed, fluid[None]], axis=0)
    widened = with_halo(stacked, (("gx", 2), ("gy", 3)), 1)
    widened = jnp.pad(widened, ((0, 0), (1, 1), (0, 0), (0, 0)))
    flag_pad = widened[19] * keeper
    post_pad = widened[:19]
    new_populations = stream(post_pad, flag_pad, relaxed, populations, solid_flag)
    momentum_x = moment(new_populations, 0)
    patch_flux = patch_sums(momentum_x, cell_patch, patch_zone.shape[0])
    zone_dev = old_pressure.shape[0]
    openings = patch_zone.shape[0]
    devices = lax.axis_size("gx") * lax.axis_size("gy")
    capacity = max(2, (2 * openings + devices - 1) // devices)
    owner_block = patch_zone // zone_dev
    local_zone = patch_zone - owner_block * zone_dev
    patch_order = jnp.arange(openings, dtype=jnp.int32)
    earlier_same = (owner_block[:, None] == owner_block[None, :]) & (
        patch_order[:, None] > patch_order[None, :]
    )
    slot_rank = jnp.sum(earlier_same.astype(jnp.int32), axis=1)
    slot_index = owner_block * capacity + slot_rank
    targets = jnp.arange(devices * capacity, dtype=jnp.int32)
    placed = slot_index[:, None] == targets[None, :]
    send_flux = jnp.sum(jnp.where(placed, patch_flux[:, None], 0.0), axis=0)
    send_zone = jnp.sum(jnp.where(placed, local_zone.astype(jnp.float32)[:, None], 0.0), axis=0)
    count_x = lax.axis_size("gx")
    count_y = lax.axis_size("gy")
    outgoing = jnp.stack([send_flux, send_zone]).reshape(2, count_x, count_y, capacity)
    arrived = lax.all_to_all(
        lax.all_to_all(outgoing, "gx", split_axis=1, concat_axis=1, tiled=True),
        "gy",
        split_axis=2,
        concat_axis=2,
        tiled=True,
    ).reshape(2, devices * capacity)
    matched = arrived[1][None, :] == jnp.arange(zone_dev, dtype=jnp.float32)[:, None]
    inflow = jnp.sum(jnp.where(matched, arrived[0][None, :], 0.0), axis=1)
    coupled, total = couple(old_pressure, leakage, conductance, neighbour)
    zone_pressure = (inflow + coupled) / total
    answered = jnp.sum(jnp.where(matched, zone_pressure[:, None], 0.0), axis=0).reshape(
        count_x, count_y, capacity
    )
    returned = lax.all_to_all(
        lax.all_to_all(answered, "gx", split_axis=0, concat_axis=0, tiled=True),
        "gy",
        split_axis=1,
        concat_axis=1,
        tiled=True,
    ).reshape(-1)
    opening_pressure = jnp.sum(jnp.where(placed, returned[None, :], 0.0), axis=1)
    return (new_populations, zone_pressure, opening_pressure)


def patch_sums(momentum_x, cell_patch, openings):
    depth, width_x, width_y = cell_patch.shape
    rows = depth * width_x
    momentum = momentum_x.reshape(rows, width_y)
    patch = cell_patch.reshape(rows, width_y)
    lanes = 128
    high = patch // lanes
    low = patch - high * lanes
    groups = openings // lanes
    picked = jnp.where(
        high[None] == jnp.arange(groups, dtype=jnp.int32)[:, None, None], momentum[None], 0.0
    )
    onehot = (low[:, :, None] == jnp.arange(lanes, dtype=jnp.int32)[None, None, :]).astype(
        jnp.float32
    )
    sums = jnp.einsum("hry,ryl->hl", picked, onehot, precision=lax.Precision.HIGHEST)
    return FACE_AREA * sums.reshape(openings)


def couple(old_pressure, leakage, conductance, neighbour):
    zone_dev = old_pressure.shape[0]
    chosen = neighbour[:, :, None] == jnp.arange(zone_dev, dtype=jnp.int32)[None, None, :]
    neighbour_pressure = jnp.sum(jnp.where(chosen, old_pressure[None, None, :], 0.0), axis=2)
    coupled = jnp.zeros_like(old_pressure)
    total = leakage
    for link in range(conductance.shape[0]):
        coupled = coupled + conductance[link] * neighbour_pressure[link]
        total = total + conductance[link]
    return coupled, total


def solution(mesh):
    placed = (
        P(None, None, "gx", "gy"),
        P(None, "gx", "gy"),
        P(None, "gx", "gy"),
        P(("gx", "gy")),
        P(("gx", "gy")),
        P(("gx", "gy")),
        P(None, ("gx", "gy")),
        P(None, ("gx", "gy")),
    )
    return jax.shard_map(
        on_device,
        mesh=mesh,
        in_specs=placed,
        out_specs=(P(None, None, "gx", "gy"), P(("gx", "gy")), P(("gx", "gy"))),
        check_vma=False,
    )
```

```python
import jax
import jax.numpy as jnp
import numpy as np
from jax import lax
from jax.experimental import pallas as pl
from jax.experimental.pallas import tpu as pltpu
from jax.sharding import PartitionSpec as P

DIRECTIONS = np.array(
    [
        [0, 0, 0],
        [1, 0, 0],
        [-1, 0, 0],
        [0, 1, 0],
        [0, -1, 0],
        [0, 0, 1],
        [0, 0, -1],
        [1, 1, 0],
        [-1, -1, 0],
        [1, -1, 0],
        [-1, 1, 0],
        [1, 0, 1],
        [-1, 0, -1],
        [1, 0, -1],
        [-1, 0, 1],
        [0, 1, 1],
        [0, -1, -1],
        [0, 1, -1],
        [0, -1, 1],
    ]
)
OPPOSITE = [0, 2, 1, 4, 3, 6, 5, 8, 7, 10, 9, 12, 11, 14, 13, 16, 15, 18, 17]
LATTICE_WEIGHTS = [1.0 / 3.0] + [1.0 / 18.0] * 6 + [1.0 / 36.0] * 12
OMEGA = 1.25
FACE_AREA = 0.25


def with_halo(cells, sides, width):
    for axis, dim in sides:
        count = lax.axis_size(axis)
        head = lax.slice_in_dim(cells, 0, width, axis=dim)
        tail = lax.slice_in_dim(cells, cells.shape[dim] - width, cells.shape[dim], axis=dim)
        cells = jnp.concatenate(
            [
                lax.ppermute(tail, axis, [(i, (i + 1) % count) for i in range(count)]),
                cells,
                lax.ppermute(head, axis, [((i + 1) % count, i) for i in range(count)]),
            ],
            axis=dim,
        )
    return cells


def moment(populations, component):
    total = jnp.zeros_like(populations[0])
    for direction in range(19):
        sign = int(DIRECTIONS[direction, component])
        if sign != 0:
            total = total + float(sign) * populations[direction]
    return total


def collide(populations):
    density = jnp.zeros_like(populations[0])
    for direction in range(19):
        density = density + populations[direction]
    velocity = [moment(populations, component) / density for component in range(3)]
    speed_sq = velocity[0] * velocity[0] + velocity[1] * velocity[1] + velocity[2] * velocity[2]
    relaxed = []
    for direction in range(19):
        along = jnp.zeros_like(density)
        for component in range(3):
            sign = int(DIRECTIONS[direction, component])
            if sign != 0:
                along = along + float(sign) * velocity[component]
        equilibrium = (
            LATTICE_WEIGHTS[direction]
            * density
            * (1.0 + 3.0 * along + 4.5 * along * along - 1.5 * speed_sq)
        )
        relaxed.append(populations[direction] - OMEGA * (populations[direction] - equilibrium))
    return jnp.stack(relaxed)


def stream(post_pad, flag_pad, relaxed, populations, solid_flag):
    depth, width_x, width_y = solid_flag.shape
    passed = []
    for direction in range(19):
        step_x = int(DIRECTIONS[direction, 0])
        step_y = int(DIRECTIONS[direction, 1])
        step_z = int(DIRECTIONS[direction, 2])
        source = post_pad[
            direction,
            1 - step_z : 1 - step_z + depth,
            1 - step_x : 1 - step_x + width_x,
            1 - step_y : 1 - step_y + width_y,
        ]
        open_source = flag_pad[
            1 - step_z : 1 - step_z + depth,
            1 - step_x : 1 - step_x + width_x,
            1 - step_y : 1 - step_y + width_y,
        ]
        pulled = open_source * source + (1.0 - open_source) * relaxed[OPPOSITE[direction]]
        passed.append(jnp.where(solid_flag == 1, populations[direction], pulled))
    return jnp.stack(passed)


def relax(inflow, old_pressure, leakage, conductance, neighbour):
    coupled = jnp.zeros_like(inflow)
    total = leakage
    for link in range(conductance.shape[0]):
        coupled = coupled + conductance[link] * old_pressure[neighbour[link]]
        total = total + conductance[link]
    return (inflow + coupled) / total


def exchange_halos(populations, fluid):
    count_x = lax.axis_size("gx")
    count_y = lax.axis_size("gy")
    stacked_x = [
        jnp.concatenate([populations[:, :, at, None, :], fluid[None, :, at, None, :]], axis=0)
        for at in (0, -1)
    ]
    stacked_y = [
        jnp.concatenate([populations[:, :, :, at, None], fluid[None, :, :, at, None]], axis=0)
        for at in (0, -1)
    ]
    corner = {
        (cx, cy): jnp.concatenate(
            [populations[:, :, cx, None, cy, None], fluid[None, :, cx, None, cy, None]], axis=0
        )
        for cx in (0, -1)
        for cy in (0, -1)
    }
    ring_up = [(i, (i + 1) % count_x) for i in range(count_x)]
    ring_down = [((i + 1) % count_x, i) for i in range(count_x)]
    line_up = [(j, j + 1) for j in range(count_y - 1)]
    line_down = [(j + 1, j) for j in range(count_y - 1)]

    def diagonal(step_x, step_y):
        pairs = []
        for i in range(count_x):
            for j in range(count_y):
                if 0 <= j + step_y < count_y:
                    pairs.append((i * count_y + j, ((i + step_x) % count_x) * count_y + j + step_y))
        return pairs

    both = ("gx", "gy")
    x_low = lax.ppermute(stacked_x[1], "gx", ring_up)
    x_high = lax.ppermute(stacked_x[0], "gx", ring_down)
    y_low = lax.ppermute(stacked_y[1], "gy", line_up)
    y_high = lax.ppermute(stacked_y[0], "gy", line_down)
    c_ll = lax.ppermute(corner[(-1, -1)], both, diagonal(1, 1))
    c_hl = lax.ppermute(corner[(0, -1)], both, diagonal(-1, 1))
    c_lh = lax.ppermute(corner[(-1, 0)], both, diagonal(1, -1))
    c_hh = lax.ppermute(corner[(0, 0)], both, diagonal(-1, -1))
    return (x_low, x_high, y_low, y_high, c_ll, c_hl, c_lh, c_hh)


def on_device(
    populations, solid_flag, cell_patch, patch_zone, old_pressure, leakage, conductance, neighbour
):
    fluid = (1 - solid_flag).astype(jnp.float32)
    halos = exchange_halos(populations, fluid)
    new_populations, momentum_x = lbm_step(populations, solid_flag, halos)
    patch_flux = patch_sums(momentum_x, cell_patch, patch_zone.shape[0])
    zone_dev = old_pressure.shape[0]
    openings = patch_zone.shape[0]
    devices = lax.axis_size("gx") * lax.axis_size("gy")
    capacity = max(2, (2 * openings + devices - 1) // devices)
    owner_block = patch_zone // zone_dev
    local_zone = patch_zone - owner_block * zone_dev
    patch_order = jnp.arange(openings, dtype=jnp.int32)
    earlier_same = (owner_block[:, None] == owner_block[None, :]) & (
        patch_order[:, None] > patch_order[None, :]
    )
    slot_rank = jnp.sum(earlier_same.astype(jnp.int32), axis=1)
    slot_index = owner_block * capacity + slot_rank
    targets = jnp.arange(devices * capacity, dtype=jnp.int32)
    placed = slot_index[:, None] == targets[None, :]
    send_flux = jnp.sum(jnp.where(placed, patch_flux[:, None], 0.0), axis=0)
    send_zone = jnp.sum(jnp.where(placed, local_zone.astype(jnp.float32)[:, None], 0.0), axis=0)
    count_x = lax.axis_size("gx")
    count_y = lax.axis_size("gy")
    outgoing = jnp.stack([send_flux, send_zone]).reshape(2, count_x, count_y, capacity)
    arrived = lax.all_to_all(
        lax.all_to_all(outgoing, "gx", split_axis=1, concat_axis=1, tiled=True),
        "gy",
        split_axis=2,
        concat_axis=2,
        tiled=True,
    ).reshape(2, devices * capacity)
    matched = arrived[1][None, :] == jnp.arange(zone_dev, dtype=jnp.float32)[:, None]
    inflow = jnp.sum(jnp.where(matched, arrived[0][None, :], 0.0), axis=1)
    coupled, total = couple(old_pressure, leakage, conductance, neighbour)
    zone_pressure = (inflow + coupled) / total
    answered = jnp.sum(jnp.where(matched, zone_pressure[:, None], 0.0), axis=0).reshape(
        count_x, count_y, capacity
    )
    returned = lax.all_to_all(
        lax.all_to_all(answered, "gx", split_axis=0, concat_axis=0, tiled=True),
        "gy",
        split_axis=1,
        concat_axis=1,
        tiled=True,
    ).reshape(-1)
    opening_pressure = jnp.sum(jnp.where(placed, returned[None, :], 0.0), axis=1)
    return (new_populations, zone_pressure, opening_pressure)


def patch_sums(momentum_x, cell_patch, openings):
    depth, width_x, width_y = cell_patch.shape
    rows = depth * width_x
    momentum = momentum_x.reshape(rows, width_y)
    patch = cell_patch.reshape(rows, width_y)
    lanes = 128
    high = patch // lanes
    low = patch - high * lanes
    groups = openings // lanes
    picked = jnp.where(
        high[None] == jnp.arange(groups, dtype=jnp.int32)[:, None, None], momentum[None], 0.0
    )
    onehot = (low[:, :, None] == jnp.arange(lanes, dtype=jnp.int32)[None, None, :]).astype(
        jnp.float32
    )
    sums = jnp.einsum("hry,ryl->hl", picked, onehot, precision=lax.Precision.HIGHEST)
    return FACE_AREA * sums.reshape(openings)


def couple(old_pressure, leakage, conductance, neighbour):
    zone_dev = old_pressure.shape[0]
    chosen = neighbour[:, :, None] == jnp.arange(zone_dev, dtype=jnp.int32)[None, None, :]
    neighbour_pressure = jnp.sum(jnp.where(chosen, old_pressure[None, None, :], 0.0), axis=2)
    coupled = jnp.zeros_like(old_pressure)
    total = leakage
    for link in range(conductance.shape[0]):
        coupled = coupled + conductance[link] * neighbour_pressure[link]
        total = total + conductance[link]
    return coupled, total


def collide_list(planes):
    density = jnp.zeros_like(planes[0])
    for direction in range(19):
        density = density + planes[direction]
    velocity = []
    for component in range(3):
        total = jnp.zeros_like(planes[0])
        for direction in range(19):
            sign = int(DIRECTIONS[direction, component])
            if sign != 0:
                total = total + float(sign) * planes[direction]
        velocity.append(total / density)
    speed_sq = velocity[0] * velocity[0] + velocity[1] * velocity[1] + velocity[2] * velocity[2]
    relaxed = []
    for direction in range(19):
        along = jnp.zeros_like(density)
        for component in range(3):
            sign = int(DIRECTIONS[direction, component])
            if sign != 0:
                along = along + float(sign) * velocity[component]
        equilibrium = (
            LATTICE_WEIGHTS[direction]
            * density
            * (1.0 + 3.0 * along + 4.5 * along * along - 1.5 * speed_sq)
        )
        relaxed.append(planes[direction] - OMEGA * (planes[direction] - equilibrium))
    return relaxed


def shift_x(plane, step, edge, xi, width_x):
    if step == 1:
        return jnp.where(xi == 0, edge, pltpu.roll(plane, 1, 0))
    if step == -1:
        return jnp.where(xi == width_x - 1, edge, pltpu.roll(plane, width_x - 1, 0))
    return plane


def shift_plane(plane, step_x, step_y, row, column, corner, xi, yi, width_x, width_y):
    moved = shift_x(plane, step_x, row, xi, width_x)
    if step_y == 0:
        return moved
    edge = shift_x(column, step_x, corner, xi, width_x)
    if step_y == 1:
        return jnp.where(yi == 0, edge, pltpu.roll(moved, 1, 1))
    return jnp.where(yi == width_y - 1, edge, pltpu.roll(moved, width_y - 1, 1))


def lbm_kernel(
    pop_ref, solid_ref, xlo_ref, xhi_ref, ylo_ref, yhi_ref,
    cll_ref, chl_ref, clh_ref, chh_ref,
    new_ref, mom_ref, rel_ref,
):
    _, depth, width_x, width_y = pop_ref.shape
    shape = (width_x, width_y)
    xi = lax.broadcasted_iota(jnp.int32, shape, 0)
    yi = lax.broadcasted_iota(jnp.int32, shape, 1)
    for level in range(depth):
        relaxed = collide_list([pop_ref[d, level] for d in range(19)])
        for d in range(19):
            rel_ref[d, level] = relaxed[d]

    def halo(ref):
        values = [ref[d] for d in range(20)]
        return collide_list(values[:19]), values[19]

    xlo, xlo_f = halo(xlo_ref)
    xhi, xhi_f = halo(xhi_ref)
    ylo, ylo_f = halo(ylo_ref)
    yhi, yhi_f = halo(yhi_ref)
    cll, cll_f = halo(cll_ref)
    chl, chl_f = halo(chl_ref)
    clh, clh_f = halo(clh_ref)
    chh, chh_f = halo(chh_ref)

    def pieces(step_x, step_y, level, direction):
        if direction is None:
            x_lo, x_hi, y_lo, y_hi = xlo_f, xhi_f, ylo_f, yhi_f
            c_ll, c_hl, c_lh, c_hh = cll_f, chl_f, clh_f, chh_f
        else:
            x_lo, x_hi, y_lo, y_hi = xlo[direction], xhi[direction], ylo[direction], yhi[direction]
            c_ll, c_hl, c_lh, c_hh = cll[direction], chl[direction], clh[direction], chh[direction]
        row = x_lo[level] if step_x == 1 else x_hi[level]
        column = y_lo[level] if step_y == 1 else y_hi[level]
        if step_y == 1:
            corner = c_ll[level] if step_x == 1 else c_hl[level]
        else:
            corner = c_lh[level] if step_x == 1 else c_hh[level]
        row = jnp.broadcast_to(row, shape)
        column = jnp.broadcast_to(column, shape)
        corner = jnp.broadcast_to(corner, shape)
        return row, column, corner

    for level in range(depth):
        solid = solid_ref[level] == 1
        momentum = jnp.zeros(shape, jnp.float32)
        for d in range(19):
            step_x, step_y, step_z = (int(v) for v in DIRECTIONS[d])
            source_level = level - step_z
            kept = pop_ref[d, level]
            bounced = rel_ref[OPPOSITE[d], level]
            if 0 <= source_level < depth:
                row, column, corner = pieces(step_x, step_y, source_level, d)
                source = shift_plane(
                    rel_ref[d, source_level], step_x, step_y, row, column, corner,
                    xi, yi, width_x, width_y,
                )
                frow, fcolumn, fcorner = pieces(step_x, step_y, source_level, None)
                fluid = 1.0 - solid_ref[source_level].astype(jnp.float32)
                open_source = shift_plane(
                    fluid, step_x, step_y, frow, fcolumn, fcorner,
                    xi, yi, width_x, width_y,
                )
                pulled = jnp.where(open_source > 0.5, source, bounced)
            else:
                pulled = bounced
            value = jnp.where(solid, kept, pulled)
            new_ref[d, level] = value
            if step_x != 0:
                momentum = momentum + float(step_x) * value
        mom_ref[level] = momentum


def lbm_step(populations, solid_flag, halos, interpret=False):
    depth, width_x, width_y = solid_flag.shape
    return pl.pallas_call(
        lbm_kernel,
        out_shape=(
            jax.ShapeDtypeStruct(populations.shape, jnp.float32),
            jax.ShapeDtypeStruct(solid_flag.shape, jnp.float32),
        ),
        scratch_shapes=[pltpu.VMEM(populations.shape, jnp.float32)],
        interpret=interpret,
    )(populations, solid_flag, *halos)


def solution(mesh):
    placed = (
        P(None, None, "gx", "gy"),
        P(None, "gx", "gy"),
        P(None, "gx", "gy"),
        P(("gx", "gy")),
        P(("gx", "gy")),
        P(("gx", "gy")),
        P(None, ("gx", "gy")),
        P(None, ("gx", "gy")),
    )
    return jax.shard_map(
        on_device,
        mesh=mesh,
        in_specs=placed,
        out_specs=(P(None, None, "gx", "gy"), P(("gx", "gy")), P(("gx", "gy"))),
        check_vma=False,
    )
```

```python
import jax
import jax.numpy as jnp
import numpy as np
from jax import lax
from jax.experimental import pallas as pl
from jax.experimental.pallas import tpu as pltpu
from jax.sharding import PartitionSpec as P

DIRECTIONS = np.array(
    [
        [0, 0, 0],
        [1, 0, 0],
        [-1, 0, 0],
        [0, 1, 0],
        [0, -1, 0],
        [0, 0, 1],
        [0, 0, -1],
        [1, 1, 0],
        [-1, -1, 0],
        [1, -1, 0],
        [-1, 1, 0],
        [1, 0, 1],
        [-1, 0, -1],
        [1, 0, -1],
        [-1, 0, 1],
        [0, 1, 1],
        [0, -1, -1],
        [0, 1, -1],
        [0, -1, 1],
    ]
)
OPPOSITE = [0, 2, 1, 4, 3, 6, 5, 8, 7, 10, 9, 12, 11, 14, 13, 16, 15, 18, 17]
LATTICE_WEIGHTS = [1.0 / 3.0] + [1.0 / 18.0] * 6 + [1.0 / 36.0] * 12
OMEGA = 1.25
FACE_AREA = 0.25


def with_halo(cells, sides, width):
    for axis, dim in sides:
        count = lax.axis_size(axis)
        head = lax.slice_in_dim(cells, 0, width, axis=dim)
        tail = lax.slice_in_dim(cells, cells.shape[dim] - width, cells.shape[dim], axis=dim)
        cells = jnp.concatenate(
            [
                lax.ppermute(tail, axis, [(i, (i + 1) % count) for i in range(count)]),
                cells,
                lax.ppermute(head, axis, [((i + 1) % count, i) for i in range(count)]),
            ],
            axis=dim,
        )
    return cells


def moment(populations, component):
    total = jnp.zeros_like(populations[0])
    for direction in range(19):
        sign = int(DIRECTIONS[direction, component])
        if sign != 0:
            total = total + float(sign) * populations[direction]
    return total


def collide(populations):
    density = jnp.zeros_like(populations[0])
    for direction in range(19):
        density = density + populations[direction]
    velocity = [moment(populations, component) / density for component in range(3)]
    speed_sq = velocity[0] * velocity[0] + velocity[1] * velocity[1] + velocity[2] * velocity[2]
    relaxed = []
    for direction in range(19):
        along = jnp.zeros_like(density)
        for component in range(3):
            sign = int(DIRECTIONS[direction, component])
            if sign != 0:
                along = along + float(sign) * velocity[component]
        equilibrium = (
            LATTICE_WEIGHTS[direction]
            * density
            * (1.0 + 3.0 * along + 4.5 * along * along - 1.5 * speed_sq)
        )
        relaxed.append(populations[direction] - OMEGA * (populations[direction] - equilibrium))
    return jnp.stack(relaxed)


def stream(post_pad, flag_pad, relaxed, populations, solid_flag):
    depth, width_x, width_y = solid_flag.shape
    passed = []
    for direction in range(19):
        step_x = int(DIRECTIONS[direction, 0])
        step_y = int(DIRECTIONS[direction, 1])
        step_z = int(DIRECTIONS[direction, 2])
        source = post_pad[
            direction,
            1 - step_z : 1 - step_z + depth,
            1 - step_x : 1 - step_x + width_x,
            1 - step_y : 1 - step_y + width_y,
        ]
        open_source = flag_pad[
            1 - step_z : 1 - step_z + depth,
            1 - step_x : 1 - step_x + width_x,
            1 - step_y : 1 - step_y + width_y,
        ]
        pulled = open_source * source + (1.0 - open_source) * relaxed[OPPOSITE[direction]]
        passed.append(jnp.where(solid_flag == 1, populations[direction], pulled))
    return jnp.stack(passed)


def relax(inflow, old_pressure, leakage, conductance, neighbour):
    coupled = jnp.zeros_like(inflow)
    total = leakage
    for link in range(conductance.shape[0]):
        coupled = coupled + conductance[link] * old_pressure[neighbour[link]]
        total = total + conductance[link]
    return (inflow + coupled) / total


def exchange_halos(populations, fluid):
    count_x = lax.axis_size("gx")
    count_y = lax.axis_size("gy")
    stacked_x = [
        jnp.concatenate([populations[:, :, at, None, :], fluid[None, :, at, None, :]], axis=0)
        for at in (0, -1)
    ]
    stacked_y = [
        jnp.concatenate([populations[:, :, :, at, None], fluid[None, :, :, at, None]], axis=0)
        for at in (0, -1)
    ]
    corner = {
        (cx, cy): jnp.concatenate(
            [populations[:, :, cx, None, cy, None], fluid[None, :, cx, None, cy, None]], axis=0
        )
        for cx in (0, -1)
        for cy in (0, -1)
    }
    ring_up = [(i, (i + 1) % count_x) for i in range(count_x)]
    ring_down = [((i + 1) % count_x, i) for i in range(count_x)]
    line_up = [(j, j + 1) for j in range(count_y - 1)]
    line_down = [(j + 1, j) for j in range(count_y - 1)]

    def diagonal(step_x, step_y):
        pairs = []
        for i in range(count_x):
            for j in range(count_y):
                if 0 <= j + step_y < count_y:
                    pairs.append((i * count_y + j, ((i + step_x) % count_x) * count_y + j + step_y))
        return pairs

    both = ("gx", "gy")
    x_low = lax.ppermute(stacked_x[1], "gx", ring_up)
    x_high = lax.ppermute(stacked_x[0], "gx", ring_down)
    y_low = lax.ppermute(stacked_y[1], "gy", line_up)
    y_high = lax.ppermute(stacked_y[0], "gy", line_down)
    c_ll = lax.ppermute(corner[(-1, -1)], both, diagonal(1, 1))
    c_hl = lax.ppermute(corner[(0, -1)], both, diagonal(-1, 1))
    c_lh = lax.ppermute(corner[(-1, 0)], both, diagonal(1, -1))
    c_hh = lax.ppermute(corner[(0, 0)], both, diagonal(-1, -1))
    return (x_low, x_high, y_low, y_high, c_ll, c_hl, c_lh, c_hh)


def on_device(
    populations, solid_flag, cell_patch, patch_zone, old_pressure, leakage, conductance, neighbour
):
    fluid = (1 - solid_flag).astype(jnp.float32)
    halos = exchange_halos(populations, fluid)
    new_populations, momentum_x = lbm_step(populations, solid_flag, halos)
    patch_flux = patch_sums(momentum_x, cell_patch, patch_zone.shape[0])
    zone_dev = old_pressure.shape[0]
    openings = patch_zone.shape[0]
    devices = lax.axis_size("gx") * lax.axis_size("gy")
    capacity = max(2, (2 * openings + devices - 1) // devices)
    owner_block = patch_zone // zone_dev
    local_zone = patch_zone - owner_block * zone_dev
    patch_order = jnp.arange(openings, dtype=jnp.int32)
    earlier_same = (owner_block[:, None] == owner_block[None, :]) & (
        patch_order[:, None] > patch_order[None, :]
    )
    slot_rank = jnp.sum(earlier_same.astype(jnp.int32), axis=1)
    slot_index = owner_block * capacity + slot_rank
    targets = jnp.arange(devices * capacity, dtype=jnp.int32)
    placed = slot_index[:, None] == targets[None, :]
    send_flux = jnp.sum(jnp.where(placed, patch_flux[:, None], 0.0), axis=0)
    send_zone = jnp.sum(jnp.where(placed, local_zone.astype(jnp.float32)[:, None], 0.0), axis=0)
    count_x = lax.axis_size("gx")
    count_y = lax.axis_size("gy")
    outgoing = jnp.stack([send_flux, send_zone]).reshape(2, count_x, count_y * capacity)
    arrived = lax.all_to_all(outgoing, "gx", split_axis=1, concat_axis=1, tiled=True)
    arrived = arrived.reshape(2, count_x, count_y, capacity)
    zones = jnp.arange(zone_dev, dtype=jnp.float32)
    matched = arrived[1][..., None] == zones
    gathered = jnp.sum(jnp.where(matched, arrived[0][..., None], 0.0), axis=(0, 2))
    inflow = lax.psum_scatter(gathered, "gy", scatter_dimension=0, tiled=True).reshape(zone_dev)
    coupled, total = couple(old_pressure, leakage, conductance, neighbour)
    zone_pressure = (inflow + coupled) / total
    row_pressure = lax.all_gather(zone_pressure, "gy", axis=0, tiled=False)
    answered = jnp.sum(jnp.where(matched, row_pressure[None, :, None, :], 0.0), axis=3)
    returned = lax.all_to_all(
        answered.reshape(count_x, count_y * capacity), "gx", split_axis=0, concat_axis=0, tiled=True
    ).reshape(-1)
    opening_pressure = jnp.sum(jnp.where(placed, returned[None, :], 0.0), axis=1)
    return (new_populations, zone_pressure, opening_pressure)


def patch_sums(momentum_x, cell_patch, openings):
    depth, width_x, width_y = cell_patch.shape
    rows = depth * width_x
    momentum = momentum_x.reshape(rows, width_y)
    patch = cell_patch.reshape(rows, width_y)
    lanes = 128
    high = patch // lanes
    low = patch - high * lanes
    groups = openings // lanes
    picked = jnp.where(
        high[None] == jnp.arange(groups, dtype=jnp.int32)[:, None, None], momentum[None], 0.0
    )
    onehot = (low[:, :, None] == jnp.arange(lanes, dtype=jnp.int32)[None, None, :]).astype(
        jnp.float32
    )
    sums = jnp.einsum("hry,ryl->hl", picked, onehot, precision=lax.Precision.HIGHEST)
    return FACE_AREA * sums.reshape(openings)


def couple(old_pressure, leakage, conductance, neighbour):
    zone_dev = old_pressure.shape[0]
    chosen = neighbour[:, :, None] == jnp.arange(zone_dev, dtype=jnp.int32)[None, None, :]
    neighbour_pressure = jnp.sum(jnp.where(chosen, old_pressure[None, None, :], 0.0), axis=2)
    coupled = jnp.zeros_like(old_pressure)
    total = leakage
    for link in range(conductance.shape[0]):
        coupled = coupled + conductance[link] * neighbour_pressure[link]
        total = total + conductance[link]
    return coupled, total


def collide_list(planes):
    density = jnp.zeros_like(planes[0])
    for direction in range(19):
        density = density + planes[direction]
    velocity = []
    for component in range(3):
        total = jnp.zeros_like(planes[0])
        for direction in range(19):
            sign = int(DIRECTIONS[direction, component])
            if sign != 0:
                total = total + float(sign) * planes[direction]
        velocity.append(total / density)
    speed_sq = velocity[0] * velocity[0] + velocity[1] * velocity[1] + velocity[2] * velocity[2]
    relaxed = []
    for direction in range(19):
        along = jnp.zeros_like(density)
        for component in range(3):
            sign = int(DIRECTIONS[direction, component])
            if sign != 0:
                along = along + float(sign) * velocity[component]
        equilibrium = (
            LATTICE_WEIGHTS[direction]
            * density
            * (1.0 + 3.0 * along + 4.5 * along * along - 1.5 * speed_sq)
        )
        relaxed.append(planes[direction] - OMEGA * (planes[direction] - equilibrium))
    return relaxed


def shift_x(plane, step, edge, xi, width_x):
    if step == 1:
        return jnp.where(xi == 0, edge, pltpu.roll(plane, 1, 0))
    if step == -1:
        return jnp.where(xi == width_x - 1, edge, pltpu.roll(plane, width_x - 1, 0))
    return plane


def shift_plane(plane, step_x, step_y, row, column, corner, xi, yi, width_x, width_y):
    moved = shift_x(plane, step_x, row, xi, width_x)
    if step_y == 0:
        return moved
    edge = shift_x(column, step_x, corner, xi, width_x)
    if step_y == 1:
        return jnp.where(yi == 0, edge, pltpu.roll(moved, 1, 1))
    return jnp.where(yi == width_y - 1, edge, pltpu.roll(moved, width_y - 1, 1))


def lbm_kernel(
    pop_ref, solid_ref, xlo_ref, xhi_ref, ylo_ref, yhi_ref,
    cll_ref, chl_ref, clh_ref, chh_ref,
    new_ref, mom_ref, rel_ref,
):
    _, depth, width_x, width_y = pop_ref.shape
    shape = (width_x, width_y)
    xi = lax.broadcasted_iota(jnp.int32, shape, 0)
    yi = lax.broadcasted_iota(jnp.int32, shape, 1)
    for level in range(depth):
        relaxed = collide_list([pop_ref[d, level] for d in range(19)])
        for d in range(19):
            rel_ref[d, level] = relaxed[d]

    def halo(ref):
        values = [ref[d] for d in range(20)]
        return collide_list(values[:19]), values[19]

    xlo, xlo_f = halo(xlo_ref)
    xhi, xhi_f = halo(xhi_ref)
    ylo, ylo_f = halo(ylo_ref)
    yhi, yhi_f = halo(yhi_ref)
    cll, cll_f = halo(cll_ref)
    chl, chl_f = halo(chl_ref)
    clh, clh_f = halo(clh_ref)
    chh, chh_f = halo(chh_ref)

    def pieces(step_x, step_y, level, direction):
        if direction is None:
            x_lo, x_hi, y_lo, y_hi = xlo_f, xhi_f, ylo_f, yhi_f
            c_ll, c_hl, c_lh, c_hh = cll_f, chl_f, clh_f, chh_f
        else:
            x_lo, x_hi, y_lo, y_hi = xlo[direction], xhi[direction], ylo[direction], yhi[direction]
            c_ll, c_hl, c_lh, c_hh = cll[direction], chl[direction], clh[direction], chh[direction]
        row = x_lo[level] if step_x == 1 else x_hi[level]
        column = y_lo[level] if step_y == 1 else y_hi[level]
        if step_y == 1:
            corner = c_ll[level] if step_x == 1 else c_hl[level]
        else:
            corner = c_lh[level] if step_x == 1 else c_hh[level]
        row = jnp.broadcast_to(row, shape)
        column = jnp.broadcast_to(column, shape)
        corner = jnp.broadcast_to(corner, shape)
        return row, column, corner

    for level in range(depth):
        solid = solid_ref[level] == 1
        momentum = jnp.zeros(shape, jnp.float32)
        for d in range(19):
            step_x, step_y, step_z = (int(v) for v in DIRECTIONS[d])
            source_level = level - step_z
            kept = pop_ref[d, level]
            bounced = rel_ref[OPPOSITE[d], level]
            if 0 <= source_level < depth:
                row, column, corner = pieces(step_x, step_y, source_level, d)
                source = shift_plane(
                    rel_ref[d, source_level], step_x, step_y, row, column, corner,
                    xi, yi, width_x, width_y,
                )
                frow, fcolumn, fcorner = pieces(step_x, step_y, source_level, None)
                fluid = 1.0 - solid_ref[source_level].astype(jnp.float32)
                open_source = shift_plane(
                    fluid, step_x, step_y, frow, fcolumn, fcorner,
                    xi, yi, width_x, width_y,
                )
                pulled = jnp.where(open_source > 0.5, source, bounced)
            else:
                pulled = bounced
            value = jnp.where(solid, kept, pulled)
            new_ref[d, level] = value
            if step_x != 0:
                momentum = momentum + float(step_x) * value
        mom_ref[level] = momentum


def lbm_step(populations, solid_flag, halos, interpret=False):
    depth, width_x, width_y = solid_flag.shape
    return pl.pallas_call(
        lbm_kernel,
        out_shape=(
            jax.ShapeDtypeStruct(populations.shape, jnp.float32),
            jax.ShapeDtypeStruct(solid_flag.shape, jnp.float32),
        ),
        scratch_shapes=[pltpu.VMEM(populations.shape, jnp.float32)],
        interpret=interpret,
    )(populations, solid_flag, *halos)


def solution(mesh):
    placed = (
        P(None, None, "gx", "gy"),
        P(None, "gx", "gy"),
        P(None, "gx", "gy"),
        P(("gx", "gy")),
        P(("gx", "gy")),
        P(("gx", "gy")),
        P(None, ("gx", "gy")),
        P(None, ("gx", "gy")),
    )
    return jax.shard_map(
        on_device,
        mesh=mesh,
        in_specs=placed,
        out_specs=(P(None, None, "gx", "gy"), P(("gx", "gy")), P(("gx", "gy"))),
        check_vma=False,
    )
```

```python
import jax
import jax.numpy as jnp
import numpy as np
from jax import lax
from jax.experimental import pallas as pl
from jax.experimental.pallas import tpu as pltpu
from jax.sharding import PartitionSpec as P

DIRECTIONS = np.array(
    [
        [0, 0, 0],
        [1, 0, 0],
        [-1, 0, 0],
        [0, 1, 0],
        [0, -1, 0],
        [0, 0, 1],
        [0, 0, -1],
        [1, 1, 0],
        [-1, -1, 0],
        [1, -1, 0],
        [-1, 1, 0],
        [1, 0, 1],
        [-1, 0, -1],
        [1, 0, -1],
        [-1, 0, 1],
        [0, 1, 1],
        [0, -1, -1],
        [0, 1, -1],
        [0, -1, 1],
    ]
)
OPPOSITE = [0, 2, 1, 4, 3, 6, 5, 8, 7, 10, 9, 12, 11, 14, 13, 16, 15, 18, 17]
LATTICE_WEIGHTS = [1.0 / 3.0] + [1.0 / 18.0] * 6 + [1.0 / 36.0] * 12
OMEGA = 1.25
FACE_AREA = 0.25


def with_halo(cells, sides, width):
    for axis, dim in sides:
        count = lax.axis_size(axis)
        head = lax.slice_in_dim(cells, 0, width, axis=dim)
        tail = lax.slice_in_dim(cells, cells.shape[dim] - width, cells.shape[dim], axis=dim)
        cells = jnp.concatenate(
            [
                lax.ppermute(tail, axis, [(i, (i + 1) % count) for i in range(count)]),
                cells,
                lax.ppermute(head, axis, [((i + 1) % count, i) for i in range(count)]),
            ],
            axis=dim,
        )
    return cells


def moment(populations, component):
    total = jnp.zeros_like(populations[0])
    for direction in range(19):
        sign = int(DIRECTIONS[direction, component])
        if sign != 0:
            total = total + float(sign) * populations[direction]
    return total


def collide(populations):
    density = jnp.zeros_like(populations[0])
    for direction in range(19):
        density = density + populations[direction]
    velocity = [moment(populations, component) / density for component in range(3)]
    speed_sq = velocity[0] * velocity[0] + velocity[1] * velocity[1] + velocity[2] * velocity[2]
    relaxed = []
    for direction in range(19):
        along = jnp.zeros_like(density)
        for component in range(3):
            sign = int(DIRECTIONS[direction, component])
            if sign != 0:
                along = along + float(sign) * velocity[component]
        equilibrium = (
            LATTICE_WEIGHTS[direction]
            * density
            * (1.0 + 3.0 * along + 4.5 * along * along - 1.5 * speed_sq)
        )
        relaxed.append(populations[direction] - OMEGA * (populations[direction] - equilibrium))
    return jnp.stack(relaxed)


def stream(post_pad, flag_pad, relaxed, populations, solid_flag):
    depth, width_x, width_y = solid_flag.shape
    passed = []
    for direction in range(19):
        step_x = int(DIRECTIONS[direction, 0])
        step_y = int(DIRECTIONS[direction, 1])
        step_z = int(DIRECTIONS[direction, 2])
        source = post_pad[
            direction,
            1 - step_z : 1 - step_z + depth,
            1 - step_x : 1 - step_x + width_x,
            1 - step_y : 1 - step_y + width_y,
        ]
        open_source = flag_pad[
            1 - step_z : 1 - step_z + depth,
            1 - step_x : 1 - step_x + width_x,
            1 - step_y : 1 - step_y + width_y,
        ]
        pulled = open_source * source + (1.0 - open_source) * relaxed[OPPOSITE[direction]]
        passed.append(jnp.where(solid_flag == 1, populations[direction], pulled))
    return jnp.stack(passed)


def relax(inflow, old_pressure, leakage, conductance, neighbour):
    coupled = jnp.zeros_like(inflow)
    total = leakage
    for link in range(conductance.shape[0]):
        coupled = coupled + conductance[link] * old_pressure[neighbour[link]]
        total = total + conductance[link]
    return (inflow + coupled) / total


def exchange_halos(populations, fluid):
    count_x = lax.axis_size("gx")
    count_y = lax.axis_size("gy")
    stacked_x = [
        jnp.concatenate([populations[:, :, at, None, :], fluid[None, :, at, None, :]], axis=0)
        for at in (0, -1)
    ]
    stacked_y = [
        jnp.concatenate([populations[:, :, :, at, None], fluid[None, :, :, at, None]], axis=0)
        for at in (0, -1)
    ]
    corner = {
        (cx, cy): jnp.concatenate(
            [populations[:, :, cx, None, cy, None], fluid[None, :, cx, None, cy, None]], axis=0
        )
        for cx in (0, -1)
        for cy in (0, -1)
    }
    ring_up = [(i, (i + 1) % count_x) for i in range(count_x)]
    ring_down = [((i + 1) % count_x, i) for i in range(count_x)]
    line_up = [(j, j + 1) for j in range(count_y - 1)]
    line_down = [(j + 1, j) for j in range(count_y - 1)]

    def diagonal(step_x, step_y):
        pairs = []
        for i in range(count_x):
            for j in range(count_y):
                if 0 <= j + step_y < count_y:
                    pairs.append((i * count_y + j, ((i + step_x) % count_x) * count_y + j + step_y))
        return pairs

    both = ("gx", "gy")
    x_low = lax.ppermute(stacked_x[1], "gx", ring_up)
    x_high = lax.ppermute(stacked_x[0], "gx", ring_down)
    y_low = lax.ppermute(stacked_y[1], "gy", line_up)
    y_high = lax.ppermute(stacked_y[0], "gy", line_down)
    c_ll = lax.ppermute(corner[(-1, -1)], both, diagonal(1, 1))
    c_hl = lax.ppermute(corner[(0, -1)], both, diagonal(-1, 1))
    c_lh = lax.ppermute(corner[(-1, 0)], both, diagonal(1, -1))
    c_hh = lax.ppermute(corner[(0, 0)], both, diagonal(-1, -1))
    return (x_low, x_high, y_low, y_high, c_ll, c_hl, c_lh, c_hh)


def on_device(
    populations, solid_flag, cell_patch, patch_zone, old_pressure, leakage, conductance, neighbour
):
    fluid = (1 - solid_flag).astype(jnp.float32)
    halos = exchange_halos(populations, fluid)
    new_populations, momentum_x = lbm_step(populations, solid_flag, halos)
    patch_flux = patch_sums(momentum_x, cell_patch, patch_zone.shape[0])
    zone_dev = old_pressure.shape[0]
    openings = patch_zone.shape[0]
    devices = lax.axis_size("gx") * lax.axis_size("gy")
    capacity = max(2, (2 * openings + devices - 1) // devices)
    owner_block = patch_zone // zone_dev
    local_zone = patch_zone - owner_block * zone_dev
    patch_order = jnp.arange(openings, dtype=jnp.int32)
    earlier_same = (owner_block[:, None] == owner_block[None, :]) & (
        patch_order[:, None] > patch_order[None, :]
    )
    slot_rank = jnp.sum(earlier_same.astype(jnp.int32), axis=1)
    slot_index = owner_block * capacity + slot_rank
    targets = jnp.arange(devices * capacity, dtype=jnp.int32)
    placed = slot_index[:, None] == targets[None, :]
    send_flux = jnp.sum(jnp.where(placed, patch_flux[:, None], 0.0), axis=0)
    send_zone = jnp.sum(jnp.where(placed, local_zone.astype(jnp.float32)[:, None], 0.0), axis=0)
    count_x = lax.axis_size("gx")
    count_y = lax.axis_size("gy")
    outgoing = jnp.stack([send_flux, send_zone]).reshape(2, count_x, count_y, capacity)
    arrived = lax.all_to_all(
        lax.all_to_all(outgoing, "gx", split_axis=1, concat_axis=1, tiled=True),
        "gy",
        split_axis=2,
        concat_axis=2,
        tiled=True,
    ).reshape(2, devices * capacity)
    matched = arrived[1][None, :] == jnp.arange(zone_dev, dtype=jnp.float32)[:, None]
    inflow = jnp.sum(jnp.where(matched, arrived[0][None, :], 0.0), axis=1)
    coupled, total = couple(old_pressure, leakage, conductance, neighbour)
    zone_pressure = (inflow + coupled) / total
    answered = jnp.sum(jnp.where(matched, zone_pressure[:, None], 0.0), axis=0).reshape(
        count_x, count_y, capacity
    )
    returned = lax.all_to_all(
        lax.all_to_all(answered, "gx", split_axis=0, concat_axis=0, tiled=True),
        "gy",
        split_axis=1,
        concat_axis=1,
        tiled=True,
    ).reshape(-1)
    opening_pressure = jnp.sum(jnp.where(placed, returned[None, :], 0.0), axis=1)
    return (new_populations, zone_pressure, opening_pressure)


def patch_sums(momentum_x, cell_patch, openings):
    depth, width_x, width_y = cell_patch.shape
    rows = depth * width_x
    momentum = momentum_x.reshape(rows, width_y)
    patch = cell_patch.reshape(rows, width_y)
    lanes = 128
    high = patch // lanes
    low = patch - high * lanes
    groups = openings // lanes
    upper = lax.reduce_precision(momentum, exponent_bits=8, mantissa_bits=7)
    rest = momentum - upper
    middle = lax.reduce_precision(rest, exponent_bits=8, mantissa_bits=7)
    lower = rest - middle
    parts = jnp.stack([upper, middle, lower])
    picked = jnp.where(
        high[None, None] == jnp.arange(groups, dtype=jnp.int32)[None, :, None, None],
        parts[:, None],
        0.0,
    ).astype(jnp.bfloat16)
    onehot = (low[:, :, None] == jnp.arange(lanes, dtype=jnp.int32)[None, None, :]).astype(
        jnp.bfloat16
    )
    sums = jnp.einsum("khry,ryl->khl", picked, onehot, preferred_element_type=jnp.float32)
    return FACE_AREA * (sums[0] + sums[1] + sums[2]).reshape(openings)


def couple(old_pressure, leakage, conductance, neighbour):
    zone_dev = old_pressure.shape[0]
    chosen = neighbour[:, :, None] == jnp.arange(zone_dev, dtype=jnp.int32)[None, None, :]
    neighbour_pressure = jnp.sum(jnp.where(chosen, old_pressure[None, None, :], 0.0), axis=2)
    coupled = jnp.zeros_like(old_pressure)
    total = leakage
    for link in range(conductance.shape[0]):
        coupled = coupled + conductance[link] * neighbour_pressure[link]
        total = total + conductance[link]
    return coupled, total


def collide_list(planes):
    density = jnp.zeros_like(planes[0])
    for direction in range(19):
        density = density + planes[direction]
    velocity = []
    for component in range(3):
        total = jnp.zeros_like(planes[0])
        for direction in range(19):
            sign = int(DIRECTIONS[direction, component])
            if sign != 0:
                total = total + float(sign) * planes[direction]
        velocity.append(total / density)
    speed_sq = velocity[0] * velocity[0] + velocity[1] * velocity[1] + velocity[2] * velocity[2]
    relaxed = []
    for direction in range(19):
        along = jnp.zeros_like(density)
        for component in range(3):
            sign = int(DIRECTIONS[direction, component])
            if sign != 0:
                along = along + float(sign) * velocity[component]
        equilibrium = (
            LATTICE_WEIGHTS[direction]
            * density
            * (1.0 + 3.0 * along + 4.5 * along * along - 1.5 * speed_sq)
        )
        relaxed.append(planes[direction] - OMEGA * (planes[direction] - equilibrium))
    return relaxed


def shift_x(plane, step, edge, xi, width_x):
    if step == 1:
        return jnp.where(xi == 0, edge, pltpu.roll(plane, 1, 0))
    if step == -1:
        return jnp.where(xi == width_x - 1, edge, pltpu.roll(plane, width_x - 1, 0))
    return plane


def shift_plane(plane, step_x, step_y, row, column, corner, xi, yi, width_x, width_y):
    moved = shift_x(plane, step_x, row, xi, width_x)
    if step_y == 0:
        return moved
    edge = shift_x(column, step_x, corner, xi, width_x)
    if step_y == 1:
        return jnp.where(yi == 0, edge, pltpu.roll(moved, 1, 1))
    return jnp.where(yi == width_y - 1, edge, pltpu.roll(moved, width_y - 1, 1))


def lbm_kernel(
    pop_ref, solid_ref, xlo_ref, xhi_ref, ylo_ref, yhi_ref,
    cll_ref, chl_ref, clh_ref, chh_ref,
    new_ref, mom_ref, rel_ref,
):
    _, depth, width_x, width_y = pop_ref.shape
    shape = (width_x, width_y)
    xi = lax.broadcasted_iota(jnp.int32, shape, 0)
    yi = lax.broadcasted_iota(jnp.int32, shape, 1)
    for level in range(depth):
        relaxed = collide_list([pop_ref[d, level] for d in range(19)])
        for d in range(19):
            rel_ref[d, level] = relaxed[d]

    def halo(ref):
        values = [ref[d] for d in range(20)]
        return collide_list(values[:19]), values[19]

    xlo, xlo_f = halo(xlo_ref)
    xhi, xhi_f = halo(xhi_ref)
    ylo, ylo_f = halo(ylo_ref)
    yhi, yhi_f = halo(yhi_ref)
    cll, cll_f = halo(cll_ref)
    chl, chl_f = halo(chl_ref)
    clh, clh_f = halo(clh_ref)
    chh, chh_f = halo(chh_ref)

    def pieces(step_x, step_y, level, direction):
        if direction is None:
            x_lo, x_hi, y_lo, y_hi = xlo_f, xhi_f, ylo_f, yhi_f
            c_ll, c_hl, c_lh, c_hh = cll_f, chl_f, clh_f, chh_f
        else:
            x_lo, x_hi, y_lo, y_hi = xlo[direction], xhi[direction], ylo[direction], yhi[direction]
            c_ll, c_hl, c_lh, c_hh = cll[direction], chl[direction], clh[direction], chh[direction]
        row = x_lo[level] if step_x == 1 else x_hi[level]
        column = y_lo[level] if step_y == 1 else y_hi[level]
        if step_y == 1:
            corner = c_ll[level] if step_x == 1 else c_hl[level]
        else:
            corner = c_lh[level] if step_x == 1 else c_hh[level]
        row = jnp.broadcast_to(row, shape)
        column = jnp.broadcast_to(column, shape)
        corner = jnp.broadcast_to(corner, shape)
        return row, column, corner

    for level in range(depth):
        solid = solid_ref[level] == 1
        momentum = jnp.zeros(shape, jnp.float32)
        for d in range(19):
            step_x, step_y, step_z = (int(v) for v in DIRECTIONS[d])
            source_level = level - step_z
            kept = pop_ref[d, level]
            bounced = rel_ref[OPPOSITE[d], level]
            if 0 <= source_level < depth:
                row, column, corner = pieces(step_x, step_y, source_level, d)
                source = shift_plane(
                    rel_ref[d, source_level], step_x, step_y, row, column, corner,
                    xi, yi, width_x, width_y,
                )
                frow, fcolumn, fcorner = pieces(step_x, step_y, source_level, None)
                fluid = 1.0 - solid_ref[source_level].astype(jnp.float32)
                open_source = shift_plane(
                    fluid, step_x, step_y, frow, fcolumn, fcorner,
                    xi, yi, width_x, width_y,
                )
                pulled = jnp.where(open_source > 0.5, source, bounced)
            else:
                pulled = bounced
            value = jnp.where(solid, kept, pulled)
            new_ref[d, level] = value
            if step_x != 0:
                momentum = momentum + float(step_x) * value
        mom_ref[level] = momentum


def lbm_step(populations, solid_flag, halos, interpret=False):
    depth, width_x, width_y = solid_flag.shape
    return pl.pallas_call(
        lbm_kernel,
        out_shape=(
            jax.ShapeDtypeStruct(populations.shape, jnp.float32),
            jax.ShapeDtypeStruct(solid_flag.shape, jnp.float32),
        ),
        scratch_shapes=[pltpu.VMEM(populations.shape, jnp.float32)],
        interpret=interpret,
    )(populations, solid_flag, *halos)


def solution(mesh):
    placed = (
        P(None, None, "gx", "gy"),
        P(None, "gx", "gy"),
        P(None, "gx", "gy"),
        P(("gx", "gy")),
        P(("gx", "gy")),
        P(("gx", "gy")),
        P(None, ("gx", "gy")),
        P(None, ("gx", "gy")),
    )
    return jax.shard_map(
        on_device,
        mesh=mesh,
        in_specs=placed,
        out_specs=(P(None, None, "gx", "gy"), P(("gx", "gy")), P(("gx", "gy"))),
        check_vma=False,
    )
```

```python
import jax
import jax.numpy as jnp
import numpy as np
from jax import lax
from jax.experimental import pallas as pl
from jax.experimental.pallas import tpu as pltpu
from jax.sharding import PartitionSpec as P

DIRECTIONS = np.array(
    [
        [0, 0, 0],
        [1, 0, 0],
        [-1, 0, 0],
        [0, 1, 0],
        [0, -1, 0],
        [0, 0, 1],
        [0, 0, -1],
        [1, 1, 0],
        [-1, -1, 0],
        [1, -1, 0],
        [-1, 1, 0],
        [1, 0, 1],
        [-1, 0, -1],
        [1, 0, -1],
        [-1, 0, 1],
        [0, 1, 1],
        [0, -1, -1],
        [0, 1, -1],
        [0, -1, 1],
    ]
)
OPPOSITE = [0, 2, 1, 4, 3, 6, 5, 8, 7, 10, 9, 12, 11, 14, 13, 16, 15, 18, 17]
LATTICE_WEIGHTS = [1.0 / 3.0] + [1.0 / 18.0] * 6 + [1.0 / 36.0] * 12
OMEGA = 1.25
FACE_AREA = 0.25


def with_halo(cells, sides, width):
    for axis, dim in sides:
        count = lax.axis_size(axis)
        head = lax.slice_in_dim(cells, 0, width, axis=dim)
        tail = lax.slice_in_dim(cells, cells.shape[dim] - width, cells.shape[dim], axis=dim)
        cells = jnp.concatenate(
            [
                lax.ppermute(tail, axis, [(i, (i + 1) % count) for i in range(count)]),
                cells,
                lax.ppermute(head, axis, [((i + 1) % count, i) for i in range(count)]),
            ],
            axis=dim,
        )
    return cells


def moment(populations, component):
    total = jnp.zeros_like(populations[0])
    for direction in range(19):
        sign = int(DIRECTIONS[direction, component])
        if sign != 0:
            total = total + float(sign) * populations[direction]
    return total


def collide(populations):
    density = jnp.zeros_like(populations[0])
    for direction in range(19):
        density = density + populations[direction]
    velocity = [moment(populations, component) / density for component in range(3)]
    speed_sq = velocity[0] * velocity[0] + velocity[1] * velocity[1] + velocity[2] * velocity[2]
    relaxed = []
    for direction in range(19):
        along = jnp.zeros_like(density)
        for component in range(3):
            sign = int(DIRECTIONS[direction, component])
            if sign != 0:
                along = along + float(sign) * velocity[component]
        equilibrium = (
            LATTICE_WEIGHTS[direction]
            * density
            * (1.0 + 3.0 * along + 4.5 * along * along - 1.5 * speed_sq)
        )
        relaxed.append(populations[direction] - OMEGA * (populations[direction] - equilibrium))
    return jnp.stack(relaxed)


def stream(post_pad, flag_pad, relaxed, populations, solid_flag):
    depth, width_x, width_y = solid_flag.shape
    passed = []
    for direction in range(19):
        step_x = int(DIRECTIONS[direction, 0])
        step_y = int(DIRECTIONS[direction, 1])
        step_z = int(DIRECTIONS[direction, 2])
        source = post_pad[
            direction,
            1 - step_z : 1 - step_z + depth,
            1 - step_x : 1 - step_x + width_x,
            1 - step_y : 1 - step_y + width_y,
        ]
        open_source = flag_pad[
            1 - step_z : 1 - step_z + depth,
            1 - step_x : 1 - step_x + width_x,
            1 - step_y : 1 - step_y + width_y,
        ]
        pulled = open_source * source + (1.0 - open_source) * relaxed[OPPOSITE[direction]]
        passed.append(jnp.where(solid_flag == 1, populations[direction], pulled))
    return jnp.stack(passed)


def relax(inflow, old_pressure, leakage, conductance, neighbour):
    coupled = jnp.zeros_like(inflow)
    total = leakage
    for link in range(conductance.shape[0]):
        coupled = coupled + conductance[link] * old_pressure[neighbour[link]]
        total = total + conductance[link]
    return (inflow + coupled) / total


def exchange_halos(populations, fluid):
    count_x = lax.axis_size("gx")
    count_y = lax.axis_size("gy")
    faces_x = [
        jnp.concatenate([populations[:, :, at, None, :], fluid[None, :, at, None, :]], axis=0)
        for at in (0, -1)
    ]
    x_low = lax.ppermute(faces_x[1], "gx", [(i, (i + 1) % count_x) for i in range(count_x)])
    x_high = lax.ppermute(faces_x[0], "gx", [((i + 1) % count_x, i) for i in range(count_x)])
    faces_y = [
        jnp.concatenate(
            [
                x_low[:, :, :, at, None],
                jnp.concatenate(
                    [populations[:, :, :, at, None], fluid[None, :, :, at, None]], axis=0
                ),
                x_high[:, :, :, at, None],
            ],
            axis=2,
        )
        for at in (0, -1)
    ]
    y_low = lax.ppermute(faces_y[1], "gy", [(j, j + 1) for j in range(count_y - 1)])
    y_high = lax.ppermute(faces_y[0], "gy", [(j + 1, j) for j in range(count_y - 1)])
    return (
        x_low,
        x_high,
        y_low[:, :, 1:-1],
        y_high[:, :, 1:-1],
        y_low[:, :, :1],
        y_low[:, :, -1:],
        y_high[:, :, :1],
        y_high[:, :, -1:],
    )


def on_device(
    populations, solid_flag, cell_patch, patch_zone, old_pressure, leakage, conductance, neighbour
):
    fluid = (1 - solid_flag).astype(jnp.float32)
    halos = exchange_halos(populations, fluid)
    new_populations, momentum_x = lbm_step(populations, solid_flag, halos)
    patch_flux = patch_sums(momentum_x, cell_patch, patch_zone.shape[0])
    zone_dev = old_pressure.shape[0]
    openings = patch_zone.shape[0]
    devices = lax.axis_size("gx") * lax.axis_size("gy")
    capacity = max(2, (2 * openings + devices - 1) // devices)
    owner_block = patch_zone // zone_dev
    local_zone = patch_zone - owner_block * zone_dev
    patch_order = jnp.arange(openings, dtype=jnp.int32)
    earlier_same = (owner_block[:, None] == owner_block[None, :]) & (
        patch_order[:, None] > patch_order[None, :]
    )
    slot_rank = jnp.sum(earlier_same.astype(jnp.int32), axis=1)
    slot_index = owner_block * capacity + slot_rank
    targets = jnp.arange(devices * capacity, dtype=jnp.int32)
    placed = slot_index[:, None] == targets[None, :]
    send_flux = jnp.sum(jnp.where(placed, patch_flux[:, None], 0.0), axis=0)
    send_zone = jnp.sum(jnp.where(placed, local_zone.astype(jnp.float32)[:, None], 0.0), axis=0)
    count_x = lax.axis_size("gx")
    count_y = lax.axis_size("gy")
    outgoing = jnp.stack([send_flux, send_zone]).reshape(2, count_x, count_y, capacity)
    arrived = lax.all_to_all(
        lax.all_to_all(outgoing, "gx", split_axis=1, concat_axis=1, tiled=True),
        "gy",
        split_axis=2,
        concat_axis=2,
        tiled=True,
    ).reshape(2, devices * capacity)
    matched = arrived[1][None, :] == jnp.arange(zone_dev, dtype=jnp.float32)[:, None]
    inflow = jnp.sum(jnp.where(matched, arrived[0][None, :], 0.0), axis=1)
    coupled, total = couple(old_pressure, leakage, conductance, neighbour)
    zone_pressure = (inflow + coupled) / total
    answered = jnp.sum(jnp.where(matched, zone_pressure[:, None], 0.0), axis=0).reshape(
        count_x, count_y, capacity
    )
    returned = lax.all_to_all(
        lax.all_to_all(answered, "gx", split_axis=0, concat_axis=0, tiled=True),
        "gy",
        split_axis=1,
        concat_axis=1,
        tiled=True,
    ).reshape(-1)
    opening_pressure = jnp.sum(jnp.where(placed, returned[None, :], 0.0), axis=1)
    return (new_populations, zone_pressure, opening_pressure)


def patch_sums(momentum_x, cell_patch, openings):
    depth, width_x, width_y = cell_patch.shape
    rows = depth * width_x
    momentum = momentum_x.reshape(rows, width_y)
    patch = cell_patch.reshape(rows, width_y)
    lanes = 128
    high = patch // lanes
    low = patch - high * lanes
    groups = openings // lanes
    upper = lax.reduce_precision(momentum, exponent_bits=8, mantissa_bits=7)
    rest = momentum - upper
    middle = lax.reduce_precision(rest, exponent_bits=8, mantissa_bits=7)
    lower = rest - middle
    parts = jnp.stack([upper, middle, lower])
    picked = jnp.where(
        high[None, None] == jnp.arange(groups, dtype=jnp.int32)[None, :, None, None],
        parts[:, None],
        0.0,
    ).astype(jnp.bfloat16)
    onehot = (low[:, :, None] == jnp.arange(lanes, dtype=jnp.int32)[None, None, :]).astype(
        jnp.bfloat16
    )
    sums = jnp.einsum("khry,ryl->khl", picked, onehot, preferred_element_type=jnp.float32)
    return FACE_AREA * (sums[0] + sums[1] + sums[2]).reshape(openings)


def couple(old_pressure, leakage, conductance, neighbour):
    zone_dev = old_pressure.shape[0]
    chosen = neighbour[:, :, None] == jnp.arange(zone_dev, dtype=jnp.int32)[None, None, :]
    neighbour_pressure = jnp.sum(jnp.where(chosen, old_pressure[None, None, :], 0.0), axis=2)
    coupled = jnp.zeros_like(old_pressure)
    total = leakage
    for link in range(conductance.shape[0]):
        coupled = coupled + conductance[link] * neighbour_pressure[link]
        total = total + conductance[link]
    return coupled, total


def collide_list(planes):
    density = jnp.zeros_like(planes[0])
    for direction in range(19):
        density = density + planes[direction]
    velocity = []
    for component in range(3):
        total = jnp.zeros_like(planes[0])
        for direction in range(19):
            sign = int(DIRECTIONS[direction, component])
            if sign != 0:
                total = total + float(sign) * planes[direction]
        velocity.append(total / density)
    speed_sq = velocity[0] * velocity[0] + velocity[1] * velocity[1] + velocity[2] * velocity[2]
    relaxed = []
    for direction in range(19):
        along = jnp.zeros_like(density)
        for component in range(3):
            sign = int(DIRECTIONS[direction, component])
            if sign != 0:
                along = along + float(sign) * velocity[component]
        equilibrium = (
            LATTICE_WEIGHTS[direction]
            * density
            * (1.0 + 3.0 * along + 4.5 * along * along - 1.5 * speed_sq)
        )
        relaxed.append(planes[direction] - OMEGA * (planes[direction] - equilibrium))
    return relaxed


def shift_x(plane, step, edge, xi, width_x):
    if step == 1:
        return jnp.where(xi == 0, edge, pltpu.roll(plane, 1, 0))
    if step == -1:
        return jnp.where(xi == width_x - 1, edge, pltpu.roll(plane, width_x - 1, 0))
    return plane


def shift_plane(plane, step_x, step_y, row, column, corner, xi, yi, width_x, width_y):
    moved = shift_x(plane, step_x, row, xi, width_x)
    if step_y == 0:
        return moved
    edge = shift_x(column, step_x, corner, xi, width_x)
    if step_y == 1:
        return jnp.where(yi == 0, edge, pltpu.roll(moved, 1, 1))
    return jnp.where(yi == width_y - 1, edge, pltpu.roll(moved, width_y - 1, 1))


def lbm_kernel(
    pop_ref, solid_ref, xlo_ref, xhi_ref, ylo_ref, yhi_ref,
    cll_ref, chl_ref, clh_ref, chh_ref,
    new_ref, mom_ref, rel_ref,
):
    _, depth, width_x, width_y = pop_ref.shape
    shape = (width_x, width_y)
    xi = lax.broadcasted_iota(jnp.int32, shape, 0)
    yi = lax.broadcasted_iota(jnp.int32, shape, 1)
    for level in range(depth):
        relaxed = collide_list([pop_ref[d, level] for d in range(19)])
        for d in range(19):
            rel_ref[d, level] = relaxed[d]

    def halo(ref):
        values = [ref[d] for d in range(20)]
        return collide_list(values[:19]), values[19]

    xlo, xlo_f = halo(xlo_ref)
    xhi, xhi_f = halo(xhi_ref)
    ylo, ylo_f = halo(ylo_ref)
    yhi, yhi_f = halo(yhi_ref)
    cll, cll_f = halo(cll_ref)
    chl, chl_f = halo(chl_ref)
    clh, clh_f = halo(clh_ref)
    chh, chh_f = halo(chh_ref)

    def pieces(step_x, step_y, level, direction):
        if direction is None:
            x_lo, x_hi, y_lo, y_hi = xlo_f, xhi_f, ylo_f, yhi_f
            c_ll, c_hl, c_lh, c_hh = cll_f, chl_f, clh_f, chh_f
        else:
            x_lo, x_hi, y_lo, y_hi = xlo[direction], xhi[direction], ylo[direction], yhi[direction]
            c_ll, c_hl, c_lh, c_hh = cll[direction], chl[direction], clh[direction], chh[direction]
        row = x_lo[level] if step_x == 1 else x_hi[level]
        column = y_lo[level] if step_y == 1 else y_hi[level]
        if step_y == 1:
            corner = c_ll[level] if step_x == 1 else c_hl[level]
        else:
            corner = c_lh[level] if step_x == 1 else c_hh[level]
        row = jnp.broadcast_to(row, shape)
        column = jnp.broadcast_to(column, shape)
        corner = jnp.broadcast_to(corner, shape)
        return row, column, corner

    for level in range(depth):
        solid = solid_ref[level] == 1
        momentum = jnp.zeros(shape, jnp.float32)
        for d in range(19):
            step_x, step_y, step_z = (int(v) for v in DIRECTIONS[d])
            source_level = level - step_z
            kept = pop_ref[d, level]
            bounced = rel_ref[OPPOSITE[d], level]
            if 0 <= source_level < depth:
                row, column, corner = pieces(step_x, step_y, source_level, d)
                source = shift_plane(
                    rel_ref[d, source_level], step_x, step_y, row, column, corner,
                    xi, yi, width_x, width_y,
                )
                frow, fcolumn, fcorner = pieces(step_x, step_y, source_level, None)
                fluid = 1.0 - solid_ref[source_level].astype(jnp.float32)
                open_source = shift_plane(
                    fluid, step_x, step_y, frow, fcolumn, fcorner,
                    xi, yi, width_x, width_y,
                )
                pulled = jnp.where(open_source > 0.5, source, bounced)
            else:
                pulled = bounced
            value = jnp.where(solid, kept, pulled)
            new_ref[d, level] = value
            if step_x != 0:
                momentum = momentum + float(step_x) * value
        mom_ref[level] = momentum


def lbm_step(populations, solid_flag, halos, interpret=False):
    depth, width_x, width_y = solid_flag.shape
    return pl.pallas_call(
        lbm_kernel,
        out_shape=(
            jax.ShapeDtypeStruct(populations.shape, jnp.float32),
            jax.ShapeDtypeStruct(solid_flag.shape, jnp.float32),
        ),
        scratch_shapes=[pltpu.VMEM(populations.shape, jnp.float32)],
        interpret=interpret,
    )(populations, solid_flag, *halos)


def solution(mesh):
    placed = (
        P(None, None, "gx", "gy"),
        P(None, "gx", "gy"),
        P(None, "gx", "gy"),
        P(("gx", "gy")),
        P(("gx", "gy")),
        P(("gx", "gy")),
        P(None, ("gx", "gy")),
        P(None, ("gx", "gy")),
    )
    return jax.shard_map(
        on_device,
        mesh=mesh,
        in_specs=placed,
        out_specs=(P(None, None, "gx", "gy"), P(("gx", "gy")), P(("gx", "gy"))),
        check_vma=False,
    )
```

```python
import jax
import jax.numpy as jnp
import numpy as np
from jax import lax
from jax.experimental import pallas as pl
from jax.experimental.pallas import tpu as pltpu
from jax.sharding import PartitionSpec as P

DIRECTIONS = np.array(
    [
        [0, 0, 0],
        [1, 0, 0],
        [-1, 0, 0],
        [0, 1, 0],
        [0, -1, 0],
        [0, 0, 1],
        [0, 0, -1],
        [1, 1, 0],
        [-1, -1, 0],
        [1, -1, 0],
        [-1, 1, 0],
        [1, 0, 1],
        [-1, 0, -1],
        [1, 0, -1],
        [-1, 0, 1],
        [0, 1, 1],
        [0, -1, -1],
        [0, 1, -1],
        [0, -1, 1],
    ]
)
OPPOSITE = [0, 2, 1, 4, 3, 6, 5, 8, 7, 10, 9, 12, 11, 14, 13, 16, 15, 18, 17]
LATTICE_WEIGHTS = [1.0 / 3.0] + [1.0 / 18.0] * 6 + [1.0 / 36.0] * 12
OMEGA = 1.25
FACE_AREA = 0.25


def with_halo(cells, sides, width):
    for axis, dim in sides:
        count = lax.axis_size(axis)
        head = lax.slice_in_dim(cells, 0, width, axis=dim)
        tail = lax.slice_in_dim(cells, cells.shape[dim] - width, cells.shape[dim], axis=dim)
        cells = jnp.concatenate(
            [
                lax.ppermute(tail, axis, [(i, (i + 1) % count) for i in range(count)]),
                cells,
                lax.ppermute(head, axis, [((i + 1) % count, i) for i in range(count)]),
            ],
            axis=dim,
        )
    return cells


def moment(populations, component):
    total = jnp.zeros_like(populations[0])
    for direction in range(19):
        sign = int(DIRECTIONS[direction, component])
        if sign != 0:
            total = total + float(sign) * populations[direction]
    return total


def collide(populations):
    density = jnp.zeros_like(populations[0])
    for direction in range(19):
        density = density + populations[direction]
    velocity = [moment(populations, component) / density for component in range(3)]
    speed_sq = velocity[0] * velocity[0] + velocity[1] * velocity[1] + velocity[2] * velocity[2]
    relaxed = []
    for direction in range(19):
        along = jnp.zeros_like(density)
        for component in range(3):
            sign = int(DIRECTIONS[direction, component])
            if sign != 0:
                along = along + float(sign) * velocity[component]
        equilibrium = (
            LATTICE_WEIGHTS[direction]
            * density
            * (1.0 + 3.0 * along + 4.5 * along * along - 1.5 * speed_sq)
        )
        relaxed.append(populations[direction] - OMEGA * (populations[direction] - equilibrium))
    return jnp.stack(relaxed)


def stream(post_pad, flag_pad, relaxed, populations, solid_flag):
    depth, width_x, width_y = solid_flag.shape
    passed = []
    for direction in range(19):
        step_x = int(DIRECTIONS[direction, 0])
        step_y = int(DIRECTIONS[direction, 1])
        step_z = int(DIRECTIONS[direction, 2])
        source = post_pad[
            direction,
            1 - step_z : 1 - step_z + depth,
            1 - step_x : 1 - step_x + width_x,
            1 - step_y : 1 - step_y + width_y,
        ]
        open_source = flag_pad[
            1 - step_z : 1 - step_z + depth,
            1 - step_x : 1 - step_x + width_x,
            1 - step_y : 1 - step_y + width_y,
        ]
        pulled = open_source * source + (1.0 - open_source) * relaxed[OPPOSITE[direction]]
        passed.append(jnp.where(solid_flag == 1, populations[direction], pulled))
    return jnp.stack(passed)


def relax(inflow, old_pressure, leakage, conductance, neighbour):
    coupled = jnp.zeros_like(inflow)
    total = leakage
    for link in range(conductance.shape[0]):
        coupled = coupled + conductance[link] * old_pressure[neighbour[link]]
        total = total + conductance[link]
    return (inflow + coupled) / total


def exchange_halos(populations, fluid):
    count_x = lax.axis_size("gx")
    count_y = lax.axis_size("gy")
    faces_x = [
        jnp.concatenate([populations[:, :, at, None, :], fluid[None, :, at, None, :]], axis=0)
        for at in (0, -1)
    ]
    x_low = lax.ppermute(faces_x[1], "gx", [(i, (i + 1) % count_x) for i in range(count_x)])
    x_high = lax.ppermute(faces_x[0], "gx", [((i + 1) % count_x, i) for i in range(count_x)])
    faces_y = [
        jnp.concatenate(
            [
                x_low[:, :, :, at, None],
                jnp.concatenate(
                    [populations[:, :, :, at, None], fluid[None, :, :, at, None]], axis=0
                ),
                x_high[:, :, :, at, None],
            ],
            axis=2,
        )
        for at in (0, -1)
    ]
    y_low = lax.ppermute(faces_y[1], "gy", [(j, j + 1) for j in range(count_y - 1)])
    y_high = lax.ppermute(faces_y[0], "gy", [(j + 1, j) for j in range(count_y - 1)])
    return (
        x_low,
        x_high,
        y_low[:, :, 1:-1],
        y_high[:, :, 1:-1],
        y_low[:, :, :1],
        y_low[:, :, -1:],
        y_high[:, :, :1],
        y_high[:, :, -1:],
    )


def on_device(
    populations, solid_flag, cell_patch, patch_zone, old_pressure, leakage, conductance, neighbour
):
    fluid = (1 - solid_flag).astype(jnp.float32)
    halos = exchange_halos(populations, fluid)
    new_populations, momentum_x = lbm_step(populations, solid_flag, halos)
    patch_flux = patch_sums(momentum_x, cell_patch, patch_zone.shape[0])
    zone_dev = old_pressure.shape[0]
    openings = patch_zone.shape[0]
    devices = lax.axis_size("gx") * lax.axis_size("gy")
    capacity = max(2, (2 * openings + devices - 1) // devices)
    owner_block = patch_zone // zone_dev
    local_zone = patch_zone - owner_block * zone_dev
    patch_order = jnp.arange(openings, dtype=jnp.int32)
    earlier_same = (owner_block[:, None] == owner_block[None, :]) & (
        patch_order[:, None] > patch_order[None, :]
    )
    slot_rank = jnp.sum(earlier_same.astype(jnp.int32), axis=1)
    slot_index = owner_block * capacity + slot_rank
    targets = jnp.arange(devices * capacity, dtype=jnp.int32)
    placed = slot_index[:, None] == targets[None, :]
    send_flux = jnp.sum(jnp.where(placed, patch_flux[:, None], 0.0), axis=0)
    send_zone = jnp.sum(jnp.where(placed, local_zone.astype(jnp.float32)[:, None], 0.0), axis=0)
    count_x = lax.axis_size("gx")
    count_y = lax.axis_size("gy")
    outgoing = jnp.stack([send_flux, send_zone]).reshape(2, count_x, count_y * capacity)
    arrived = lax.all_to_all(outgoing, "gx", split_axis=1, concat_axis=1, tiled=True)
    arrived = arrived.reshape(2, count_x, count_y, capacity)
    zones = jnp.arange(zone_dev, dtype=jnp.float32)
    matched = arrived[1][..., None] == zones
    gathered = jnp.sum(jnp.where(matched, arrived[0][..., None], 0.0), axis=(0, 2))
    coupled, total = couple(old_pressure, leakage, conductance, neighbour)
    column = lax.axis_index("gy")
    is_own = (jnp.arange(count_y, dtype=jnp.int32) == column)[:, None]
    numer = gathered + jnp.where(is_own, coupled[None, :], 0.0)
    denom = jnp.where(is_own, total[None, :], 0.0)
    summed = row_sum(jnp.stack([numer, denom]), "gy", count_y)
    row_pressure = summed[0] / summed[1]
    zone_pressure = lax.dynamic_index_in_dim(row_pressure, column, axis=0, keepdims=False)
    answered = jnp.sum(jnp.where(matched, row_pressure[None, :, None, :], 0.0), axis=3)
    returned = lax.all_to_all(
        answered.reshape(count_x, count_y * capacity), "gx", split_axis=0, concat_axis=0, tiled=True
    ).reshape(-1)
    opening_pressure = jnp.sum(jnp.where(placed, returned[None, :], 0.0), axis=1)
    return (new_populations, zone_pressure, opening_pressure)


def row_sum(values, axis, count):
    if count & (count - 1):
        return lax.psum(values, axis)
    step = 1
    while step < count:
        values = values + lax.ppermute(values, axis, [(j, j ^ step) for j in range(count)])
        step *= 2
    return values


def patch_sums(momentum_x, cell_patch, openings):
    depth, width_x, width_y = cell_patch.shape
    rows = depth * width_x
    momentum = momentum_x.reshape(rows, width_y)
    patch = cell_patch.reshape(rows, width_y)
    lanes = 128
    high = patch // lanes
    low = patch - high * lanes
    groups = openings // lanes
    upper = lax.reduce_precision(momentum, exponent_bits=8, mantissa_bits=7)
    rest = momentum - upper
    middle = lax.reduce_precision(rest, exponent_bits=8, mantissa_bits=7)
    lower = rest - middle
    parts = jnp.stack([upper, middle, lower])
    picked = jnp.where(
        high[None, None] == jnp.arange(groups, dtype=jnp.int32)[None, :, None, None],
        parts[:, None],
        0.0,
    ).astype(jnp.bfloat16)
    onehot = (low[:, :, None] == jnp.arange(lanes, dtype=jnp.int32)[None, None, :]).astype(
        jnp.bfloat16
    )
    sums = jnp.einsum("khry,ryl->khl", picked, onehot, preferred_element_type=jnp.float32)
    return FACE_AREA * (sums[0] + sums[1] + sums[2]).reshape(openings)


def couple(old_pressure, leakage, conductance, neighbour):
    zone_dev = old_pressure.shape[0]
    chosen = neighbour[:, :, None] == jnp.arange(zone_dev, dtype=jnp.int32)[None, None, :]
    neighbour_pressure = jnp.sum(jnp.where(chosen, old_pressure[None, None, :], 0.0), axis=2)
    coupled = jnp.zeros_like(old_pressure)
    total = leakage
    for link in range(conductance.shape[0]):
        coupled = coupled + conductance[link] * neighbour_pressure[link]
        total = total + conductance[link]
    return coupled, total


def collide_list(planes):
    density = jnp.zeros_like(planes[0])
    for direction in range(19):
        density = density + planes[direction]
    velocity = []
    for component in range(3):
        total = jnp.zeros_like(planes[0])
        for direction in range(19):
            sign = int(DIRECTIONS[direction, component])
            if sign != 0:
                total = total + float(sign) * planes[direction]
        velocity.append(total / density)
    speed_sq = velocity[0] * velocity[0] + velocity[1] * velocity[1] + velocity[2] * velocity[2]
    relaxed = []
    for direction in range(19):
        along = jnp.zeros_like(density)
        for component in range(3):
            sign = int(DIRECTIONS[direction, component])
            if sign != 0:
                along = along + float(sign) * velocity[component]
        equilibrium = (
            LATTICE_WEIGHTS[direction]
            * density
            * (1.0 + 3.0 * along + 4.5 * along * along - 1.5 * speed_sq)
        )
        relaxed.append(planes[direction] - OMEGA * (planes[direction] - equilibrium))
    return relaxed


def shift_x(plane, step, edge, xi, width_x):
    if step == 1:
        return jnp.where(xi == 0, edge, pltpu.roll(plane, 1, 0))
    if step == -1:
        return jnp.where(xi == width_x - 1, edge, pltpu.roll(plane, width_x - 1, 0))
    return plane


def shift_plane(plane, step_x, step_y, row, column, corner, xi, yi, width_x, width_y):
    moved = shift_x(plane, step_x, row, xi, width_x)
    if step_y == 0:
        return moved
    edge = shift_x(column, step_x, corner, xi, width_x)
    if step_y == 1:
        return jnp.where(yi == 0, edge, pltpu.roll(moved, 1, 1))
    return jnp.where(yi == width_y - 1, edge, pltpu.roll(moved, width_y - 1, 1))


def lbm_kernel(
    pop_ref, solid_ref, xlo_ref, xhi_ref, ylo_ref, yhi_ref,
    cll_ref, chl_ref, clh_ref, chh_ref,
    new_ref, mom_ref, rel_ref,
):
    _, depth, width_x, width_y = pop_ref.shape
    shape = (width_x, width_y)
    xi = lax.broadcasted_iota(jnp.int32, shape, 0)
    yi = lax.broadcasted_iota(jnp.int32, shape, 1)
    for level in range(depth):
        relaxed = collide_list([pop_ref[d, level] for d in range(19)])
        for d in range(19):
            rel_ref[d, level] = relaxed[d]

    def halo(ref):
        values = [ref[d] for d in range(20)]
        return collide_list(values[:19]), values[19]

    xlo, xlo_f = halo(xlo_ref)
    xhi, xhi_f = halo(xhi_ref)
    ylo, ylo_f = halo(ylo_ref)
    yhi, yhi_f = halo(yhi_ref)
    cll, cll_f = halo(cll_ref)
    chl, chl_f = halo(chl_ref)
    clh, clh_f = halo(clh_ref)
    chh, chh_f = halo(chh_ref)

    def pieces(step_x, step_y, level, direction):
        if direction is None:
            x_lo, x_hi, y_lo, y_hi = xlo_f, xhi_f, ylo_f, yhi_f
            c_ll, c_hl, c_lh, c_hh = cll_f, chl_f, clh_f, chh_f
        else:
            x_lo, x_hi, y_lo, y_hi = xlo[direction], xhi[direction], ylo[direction], yhi[direction]
            c_ll, c_hl, c_lh, c_hh = cll[direction], chl[direction], clh[direction], chh[direction]
        row = x_lo[level] if step_x == 1 else x_hi[level]
        column = y_lo[level] if step_y == 1 else y_hi[level]
        if step_y == 1:
            corner = c_ll[level] if step_x == 1 else c_hl[level]
        else:
            corner = c_lh[level] if step_x == 1 else c_hh[level]
        row = jnp.broadcast_to(row, shape)
        column = jnp.broadcast_to(column, shape)
        corner = jnp.broadcast_to(corner, shape)
        return row, column, corner

    for level in range(depth):
        solid = solid_ref[level] == 1
        momentum = jnp.zeros(shape, jnp.float32)
        for d in range(19):
            step_x, step_y, step_z = (int(v) for v in DIRECTIONS[d])
            source_level = level - step_z
            kept = pop_ref[d, level]
            bounced = rel_ref[OPPOSITE[d], level]
            if 0 <= source_level < depth:
                row, column, corner = pieces(step_x, step_y, source_level, d)
                source = shift_plane(
                    rel_ref[d, source_level], step_x, step_y, row, column, corner,
                    xi, yi, width_x, width_y,
                )
                frow, fcolumn, fcorner = pieces(step_x, step_y, source_level, None)
                fluid = 1.0 - solid_ref[source_level].astype(jnp.float32)
                open_source = shift_plane(
                    fluid, step_x, step_y, frow, fcolumn, fcorner,
                    xi, yi, width_x, width_y,
                )
                pulled = jnp.where(open_source > 0.5, source, bounced)
            else:
                pulled = bounced
            value = jnp.where(solid, kept, pulled)
            new_ref[d, level] = value
            if step_x != 0:
                momentum = momentum + float(step_x) * value
        mom_ref[level] = momentum


def lbm_step(populations, solid_flag, halos, interpret=False):
    depth, width_x, width_y = solid_flag.shape
    return pl.pallas_call(
        lbm_kernel,
        out_shape=(
            jax.ShapeDtypeStruct(populations.shape, jnp.float32),
            jax.ShapeDtypeStruct(solid_flag.shape, jnp.float32),
        ),
        scratch_shapes=[pltpu.VMEM(populations.shape, jnp.float32)],
        interpret=interpret,
    )(populations, solid_flag, *halos)


def solution(mesh):
    placed = (
        P(None, None, "gx", "gy"),
        P(None, "gx", "gy"),
        P(None, "gx", "gy"),
        P(("gx", "gy")),
        P(("gx", "gy")),
        P(("gx", "gy")),
        P(None, ("gx", "gy")),
        P(None, ("gx", "gy")),
    )
    return jax.shard_map(
        on_device,
        mesh=mesh,
        in_specs=placed,
        out_specs=(P(None, None, "gx", "gy"), P(("gx", "gy")), P(("gx", "gy"))),
        check_vma=False,
    )
```

```python
import jax
import jax.numpy as jnp
import numpy as np
from jax import lax
from jax.experimental import pallas as pl
from jax.experimental.pallas import tpu as pltpu
from jax.sharding import PartitionSpec as P

DIRECTIONS = np.array(
    [
        [0, 0, 0],
        [1, 0, 0],
        [-1, 0, 0],
        [0, 1, 0],
        [0, -1, 0],
        [0, 0, 1],
        [0, 0, -1],
        [1, 1, 0],
        [-1, -1, 0],
        [1, -1, 0],
        [-1, 1, 0],
        [1, 0, 1],
        [-1, 0, -1],
        [1, 0, -1],
        [-1, 0, 1],
        [0, 1, 1],
        [0, -1, -1],
        [0, 1, -1],
        [0, -1, 1],
    ]
)
OPPOSITE = [0, 2, 1, 4, 3, 6, 5, 8, 7, 10, 9, 12, 11, 14, 13, 16, 15, 18, 17]
LATTICE_WEIGHTS = [1.0 / 3.0] + [1.0 / 18.0] * 6 + [1.0 / 36.0] * 12
OMEGA = 1.25
FACE_AREA = 0.25


def with_halo(cells, sides, width):
    for axis, dim in sides:
        count = lax.axis_size(axis)
        head = lax.slice_in_dim(cells, 0, width, axis=dim)
        tail = lax.slice_in_dim(cells, cells.shape[dim] - width, cells.shape[dim], axis=dim)
        cells = jnp.concatenate(
            [
                lax.ppermute(tail, axis, [(i, (i + 1) % count) for i in range(count)]),
                cells,
                lax.ppermute(head, axis, [((i + 1) % count, i) for i in range(count)]),
            ],
            axis=dim,
        )
    return cells


def moment(populations, component):
    total = jnp.zeros_like(populations[0])
    for direction in range(19):
        sign = int(DIRECTIONS[direction, component])
        if sign != 0:
            total = total + float(sign) * populations[direction]
    return total


def collide(populations):
    density = jnp.zeros_like(populations[0])
    for direction in range(19):
        density = density + populations[direction]
    velocity = [moment(populations, component) / density for component in range(3)]
    speed_sq = velocity[0] * velocity[0] + velocity[1] * velocity[1] + velocity[2] * velocity[2]
    relaxed = []
    for direction in range(19):
        along = jnp.zeros_like(density)
        for component in range(3):
            sign = int(DIRECTIONS[direction, component])
            if sign != 0:
                along = along + float(sign) * velocity[component]
        equilibrium = (
            LATTICE_WEIGHTS[direction]
            * density
            * (1.0 + 3.0 * along + 4.5 * along * along - 1.5 * speed_sq)
        )
        relaxed.append(populations[direction] - OMEGA * (populations[direction] - equilibrium))
    return jnp.stack(relaxed)


def stream(post_pad, flag_pad, relaxed, populations, solid_flag):
    depth, width_x, width_y = solid_flag.shape
    passed = []
    for direction in range(19):
        step_x = int(DIRECTIONS[direction, 0])
        step_y = int(DIRECTIONS[direction, 1])
        step_z = int(DIRECTIONS[direction, 2])
        source = post_pad[
            direction,
            1 - step_z : 1 - step_z + depth,
            1 - step_x : 1 - step_x + width_x,
            1 - step_y : 1 - step_y + width_y,
        ]
        open_source = flag_pad[
            1 - step_z : 1 - step_z + depth,
            1 - step_x : 1 - step_x + width_x,
            1 - step_y : 1 - step_y + width_y,
        ]
        pulled = open_source * source + (1.0 - open_source) * relaxed[OPPOSITE[direction]]
        passed.append(jnp.where(solid_flag == 1, populations[direction], pulled))
    return jnp.stack(passed)


def relax(inflow, old_pressure, leakage, conductance, neighbour):
    coupled = jnp.zeros_like(inflow)
    total = leakage
    for link in range(conductance.shape[0]):
        coupled = coupled + conductance[link] * old_pressure[neighbour[link]]
        total = total + conductance[link]
    return (inflow + coupled) / total


def exchange_halos(populations, fluid):
    count_x = lax.axis_size("gx")
    count_y = lax.axis_size("gy")
    faces_x = [
        jnp.concatenate([populations[:, :, at, None, :], fluid[None, :, at, None, :]], axis=0)
        for at in (0, -1)
    ]
    x_low = lax.ppermute(faces_x[1], "gx", [(i, (i + 1) % count_x) for i in range(count_x)])
    x_high = lax.ppermute(faces_x[0], "gx", [((i + 1) % count_x, i) for i in range(count_x)])
    faces_y = [
        jnp.concatenate(
            [
                x_low[:, :, :, at, None],
                jnp.concatenate(
                    [populations[:, :, :, at, None], fluid[None, :, :, at, None]], axis=0
                ),
                x_high[:, :, :, at, None],
            ],
            axis=2,
        )
        for at in (0, -1)
    ]
    y_low = lax.ppermute(faces_y[1], "gy", [(j, j + 1) for j in range(count_y - 1)])
    y_high = lax.ppermute(faces_y[0], "gy", [(j + 1, j) for j in range(count_y - 1)])
    return (
        x_low,
        x_high,
        y_low[:, :, 1:-1],
        y_high[:, :, 1:-1],
        y_low[:, :, :1],
        y_low[:, :, -1:],
        y_high[:, :, :1],
        y_high[:, :, -1:],
    )


def on_device(
    populations, solid_flag, cell_patch, patch_zone, old_pressure, leakage, conductance, neighbour
):
    fluid = (1 - solid_flag).astype(jnp.float32)
    halos = exchange_halos(populations, fluid)
    new_populations, momentum_x = lbm_step(populations, solid_flag, halos)
    patch_flux = patch_sums(momentum_x, cell_patch, patch_zone.shape[0])
    zone_dev = old_pressure.shape[0]
    openings = patch_zone.shape[0]
    devices = lax.axis_size("gx") * lax.axis_size("gy")
    capacity = max(2, (2 * openings + devices - 1) // devices)
    owner_block = patch_zone // zone_dev
    local_zone = patch_zone - owner_block * zone_dev
    patch_order = jnp.arange(openings, dtype=jnp.int32)
    earlier_same = (owner_block[:, None] == owner_block[None, :]) & (
        patch_order[:, None] > patch_order[None, :]
    )
    slot_rank = jnp.sum(earlier_same.astype(jnp.int32), axis=1)
    slot_index = owner_block * capacity + slot_rank
    targets = jnp.arange(devices * capacity, dtype=jnp.int32)
    placed = slot_index[:, None] == targets[None, :]
    send_flux = jnp.sum(jnp.where(placed, patch_flux[:, None], 0.0), axis=0)
    send_zone = jnp.sum(jnp.where(placed, local_zone.astype(jnp.float32)[:, None], 0.0), axis=0)
    count_x = lax.axis_size("gx")
    count_y = lax.axis_size("gy")
    outgoing = jnp.stack([send_flux, send_zone]).reshape(2, count_x, count_y * capacity)
    arrived = lax.all_to_all(outgoing, "gx", split_axis=1, concat_axis=1, tiled=True)
    arrived = arrived.reshape(2, count_x, count_y, capacity)
    zones = jnp.arange(zone_dev, dtype=jnp.float32)
    matched = arrived[1][..., None] == zones
    gathered = jnp.sum(jnp.where(matched, arrived[0][..., None], 0.0), axis=(0, 2))
    coupled, total = couple(old_pressure, leakage, conductance, neighbour)
    column = lax.axis_index("gy")
    is_own = (jnp.arange(count_y, dtype=jnp.int32) == column)[:, None]
    numer = gathered + jnp.where(is_own, coupled[None, :], 0.0)
    denom = jnp.where(is_own, total[None, :], 0.0)
    summed = row_sum(jnp.stack([numer, denom]), "gy", count_y)
    row_pressure = summed[0] / summed[1]
    zone_pressure = lax.dynamic_index_in_dim(row_pressure, column, axis=0, keepdims=False)
    answered = jnp.sum(jnp.where(matched, row_pressure[None, :, None, :], 0.0), axis=3)
    returned = lax.all_to_all(
        answered.reshape(count_x, count_y * capacity), "gx", split_axis=0, concat_axis=0, tiled=True
    ).reshape(-1)
    opening_pressure = jnp.sum(jnp.where(placed, returned[None, :], 0.0), axis=1)
    return (new_populations, zone_pressure, opening_pressure)


def row_sum(values, axis, count):
    received = [
        lax.ppermute(values, axis, [(j, (j + shift) % count) for j in range(count)])
        for shift in range(1, count)
    ]
    for part in received:
        values = values + part
    return values


def patch_sums(momentum_x, cell_patch, openings):
    depth, width_x, width_y = cell_patch.shape
    rows = depth * width_x
    momentum = momentum_x.reshape(rows, width_y)
    patch = cell_patch.reshape(rows, width_y)
    lanes = 128
    high = patch // lanes
    low = patch - high * lanes
    groups = openings // lanes
    upper = lax.reduce_precision(momentum, exponent_bits=8, mantissa_bits=7)
    rest = momentum - upper
    middle = lax.reduce_precision(rest, exponent_bits=8, mantissa_bits=7)
    lower = rest - middle
    parts = jnp.stack([upper, middle, lower])
    picked = jnp.where(
        high[None, None] == jnp.arange(groups, dtype=jnp.int32)[None, :, None, None],
        parts[:, None],
        0.0,
    ).astype(jnp.bfloat16)
    onehot = (low[:, :, None] == jnp.arange(lanes, dtype=jnp.int32)[None, None, :]).astype(
        jnp.bfloat16
    )
    sums = jnp.einsum("khry,ryl->khl", picked, onehot, preferred_element_type=jnp.float32)
    return FACE_AREA * (sums[0] + sums[1] + sums[2]).reshape(openings)


def couple(old_pressure, leakage, conductance, neighbour):
    zone_dev = old_pressure.shape[0]
    chosen = neighbour[:, :, None] == jnp.arange(zone_dev, dtype=jnp.int32)[None, None, :]
    neighbour_pressure = jnp.sum(jnp.where(chosen, old_pressure[None, None, :], 0.0), axis=2)
    coupled = jnp.zeros_like(old_pressure)
    total = leakage
    for link in range(conductance.shape[0]):
        coupled = coupled + conductance[link] * neighbour_pressure[link]
        total = total + conductance[link]
    return coupled, total


def collide_list(planes):
    density = jnp.zeros_like(planes[0])
    for direction in range(19):
        density = density + planes[direction]
    velocity = []
    for component in range(3):
        total = jnp.zeros_like(planes[0])
        for direction in range(19):
            sign = int(DIRECTIONS[direction, component])
            if sign != 0:
                total = total + float(sign) * planes[direction]
        velocity.append(total / density)
    speed_sq = velocity[0] * velocity[0] + velocity[1] * velocity[1] + velocity[2] * velocity[2]
    relaxed = []
    for direction in range(19):
        along = jnp.zeros_like(density)
        for component in range(3):
            sign = int(DIRECTIONS[direction, component])
            if sign != 0:
                along = along + float(sign) * velocity[component]
        equilibrium = (
            LATTICE_WEIGHTS[direction]
            * density
            * (1.0 + 3.0 * along + 4.5 * along * along - 1.5 * speed_sq)
        )
        relaxed.append(planes[direction] - OMEGA * (planes[direction] - equilibrium))
    return relaxed


def shift_x(plane, step, edge, xi, width_x):
    if step == 1:
        return jnp.where(xi == 0, edge, pltpu.roll(plane, 1, 0))
    if step == -1:
        return jnp.where(xi == width_x - 1, edge, pltpu.roll(plane, width_x - 1, 0))
    return plane


def shift_plane(plane, step_x, step_y, row, column, corner, xi, yi, width_x, width_y):
    moved = shift_x(plane, step_x, row, xi, width_x)
    if step_y == 0:
        return moved
    edge = shift_x(column, step_x, corner, xi, width_x)
    if step_y == 1:
        return jnp.where(yi == 0, edge, pltpu.roll(moved, 1, 1))
    return jnp.where(yi == width_y - 1, edge, pltpu.roll(moved, width_y - 1, 1))


def lbm_kernel(
    pop_ref, solid_ref, xlo_ref, xhi_ref, ylo_ref, yhi_ref,
    cll_ref, chl_ref, clh_ref, chh_ref,
    new_ref, mom_ref, rel_ref,
):
    _, depth, width_x, width_y = pop_ref.shape
    shape = (width_x, width_y)
    xi = lax.broadcasted_iota(jnp.int32, shape, 0)
    yi = lax.broadcasted_iota(jnp.int32, shape, 1)
    for level in range(depth):
        relaxed = collide_list([pop_ref[d, level] for d in range(19)])
        for d in range(19):
            rel_ref[d, level] = relaxed[d]

    def halo(ref):
        values = [ref[d] for d in range(20)]
        return collide_list(values[:19]), values[19]

    xlo, xlo_f = halo(xlo_ref)
    xhi, xhi_f = halo(xhi_ref)
    ylo, ylo_f = halo(ylo_ref)
    yhi, yhi_f = halo(yhi_ref)
    cll, cll_f = halo(cll_ref)
    chl, chl_f = halo(chl_ref)
    clh, clh_f = halo(clh_ref)
    chh, chh_f = halo(chh_ref)

    def pieces(step_x, step_y, level, direction):
        if direction is None:
            x_lo, x_hi, y_lo, y_hi = xlo_f, xhi_f, ylo_f, yhi_f
            c_ll, c_hl, c_lh, c_hh = cll_f, chl_f, clh_f, chh_f
        else:
            x_lo, x_hi, y_lo, y_hi = xlo[direction], xhi[direction], ylo[direction], yhi[direction]
            c_ll, c_hl, c_lh, c_hh = cll[direction], chl[direction], clh[direction], chh[direction]
        row = x_lo[level] if step_x == 1 else x_hi[level]
        column = y_lo[level] if step_y == 1 else y_hi[level]
        if step_y == 1:
            corner = c_ll[level] if step_x == 1 else c_hl[level]
        else:
            corner = c_lh[level] if step_x == 1 else c_hh[level]
        row = jnp.broadcast_to(row, shape)
        column = jnp.broadcast_to(column, shape)
        corner = jnp.broadcast_to(corner, shape)
        return row, column, corner

    for level in range(depth):
        solid = solid_ref[level] == 1
        momentum = jnp.zeros(shape, jnp.float32)
        for d in range(19):
            step_x, step_y, step_z = (int(v) for v in DIRECTIONS[d])
            source_level = level - step_z
            kept = pop_ref[d, level]
            bounced = rel_ref[OPPOSITE[d], level]
            if 0 <= source_level < depth:
                row, column, corner = pieces(step_x, step_y, source_level, d)
                source = shift_plane(
                    rel_ref[d, source_level], step_x, step_y, row, column, corner,
                    xi, yi, width_x, width_y,
                )
                frow, fcolumn, fcorner = pieces(step_x, step_y, source_level, None)
                fluid = 1.0 - solid_ref[source_level].astype(jnp.float32)
                open_source = shift_plane(
                    fluid, step_x, step_y, frow, fcolumn, fcorner,
                    xi, yi, width_x, width_y,
                )
                pulled = jnp.where(open_source > 0.5, source, bounced)
            else:
                pulled = bounced
            value = jnp.where(solid, kept, pulled)
            new_ref[d, level] = value
            if step_x != 0:
                momentum = momentum + float(step_x) * value
        mom_ref[level] = momentum


def lbm_step(populations, solid_flag, halos, interpret=False):
    depth, width_x, width_y = solid_flag.shape
    return pl.pallas_call(
        lbm_kernel,
        out_shape=(
            jax.ShapeDtypeStruct(populations.shape, jnp.float32),
            jax.ShapeDtypeStruct(solid_flag.shape, jnp.float32),
        ),
        scratch_shapes=[pltpu.VMEM(populations.shape, jnp.float32)],
        interpret=interpret,
    )(populations, solid_flag, *halos)


def solution(mesh):
    placed = (
        P(None, None, "gx", "gy"),
        P(None, "gx", "gy"),
        P(None, "gx", "gy"),
        P(("gx", "gy")),
        P(("gx", "gy")),
        P(("gx", "gy")),
        P(None, ("gx", "gy")),
        P(None, ("gx", "gy")),
    )
    return jax.shard_map(
        on_device,
        mesh=mesh,
        in_specs=placed,
        out_specs=(P(None, None, "gx", "gy"), P(("gx", "gy")), P(("gx", "gy"))),
        check_vma=False,
    )
```

```python
import jax
import jax.numpy as jnp
import numpy as np
from jax import lax
from jax.experimental import pallas as pl
from jax.experimental.pallas import tpu as pltpu
from jax.sharding import PartitionSpec as P

DIRECTIONS = np.array(
    [
        [0, 0, 0],
        [1, 0, 0],
        [-1, 0, 0],
        [0, 1, 0],
        [0, -1, 0],
        [0, 0, 1],
        [0, 0, -1],
        [1, 1, 0],
        [-1, -1, 0],
        [1, -1, 0],
        [-1, 1, 0],
        [1, 0, 1],
        [-1, 0, -1],
        [1, 0, -1],
        [-1, 0, 1],
        [0, 1, 1],
        [0, -1, -1],
        [0, 1, -1],
        [0, -1, 1],
    ]
)
OPPOSITE = [0, 2, 1, 4, 3, 6, 5, 8, 7, 10, 9, 12, 11, 14, 13, 16, 15, 18, 17]
LATTICE_WEIGHTS = [1.0 / 3.0] + [1.0 / 18.0] * 6 + [1.0 / 36.0] * 12
OMEGA = 1.25
FACE_AREA = 0.25


def with_halo(cells, sides, width):
    for axis, dim in sides:
        count = lax.axis_size(axis)
        head = lax.slice_in_dim(cells, 0, width, axis=dim)
        tail = lax.slice_in_dim(cells, cells.shape[dim] - width, cells.shape[dim], axis=dim)
        cells = jnp.concatenate(
            [
                lax.ppermute(tail, axis, [(i, (i + 1) % count) for i in range(count)]),
                cells,
                lax.ppermute(head, axis, [((i + 1) % count, i) for i in range(count)]),
            ],
            axis=dim,
        )
    return cells


def moment(populations, component):
    total = jnp.zeros_like(populations[0])
    for direction in range(19):
        sign = int(DIRECTIONS[direction, component])
        if sign != 0:
            total = total + float(sign) * populations[direction]
    return total


def collide(populations):
    density = jnp.zeros_like(populations[0])
    for direction in range(19):
        density = density + populations[direction]
    velocity = [moment(populations, component) / density for component in range(3)]
    speed_sq = velocity[0] * velocity[0] + velocity[1] * velocity[1] + velocity[2] * velocity[2]
    relaxed = []
    for direction in range(19):
        along = jnp.zeros_like(density)
        for component in range(3):
            sign = int(DIRECTIONS[direction, component])
            if sign != 0:
                along = along + float(sign) * velocity[component]
        equilibrium = (
            LATTICE_WEIGHTS[direction]
            * density
            * (1.0 + 3.0 * along + 4.5 * along * along - 1.5 * speed_sq)
        )
        relaxed.append(populations[direction] - OMEGA * (populations[direction] - equilibrium))
    return jnp.stack(relaxed)


def stream(post_pad, flag_pad, relaxed, populations, solid_flag):
    depth, width_x, width_y = solid_flag.shape
    passed = []
    for direction in range(19):
        step_x = int(DIRECTIONS[direction, 0])
        step_y = int(DIRECTIONS[direction, 1])
        step_z = int(DIRECTIONS[direction, 2])
        source = post_pad[
            direction,
            1 - step_z : 1 - step_z + depth,
            1 - step_x : 1 - step_x + width_x,
            1 - step_y : 1 - step_y + width_y,
        ]
        open_source = flag_pad[
            1 - step_z : 1 - step_z + depth,
            1 - step_x : 1 - step_x + width_x,
            1 - step_y : 1 - step_y + width_y,
        ]
        pulled = open_source * source + (1.0 - open_source) * relaxed[OPPOSITE[direction]]
        passed.append(jnp.where(solid_flag == 1, populations[direction], pulled))
    return jnp.stack(passed)


def relax(inflow, old_pressure, leakage, conductance, neighbour):
    coupled = jnp.zeros_like(inflow)
    total = leakage
    for link in range(conductance.shape[0]):
        coupled = coupled + conductance[link] * old_pressure[neighbour[link]]
        total = total + conductance[link]
    return (inflow + coupled) / total


def exchange_halos(populations, solid_flag):
    count_x = lax.axis_size("gx")
    count_y = lax.axis_size("gy")

    def fluid(*at):
        return (1 - solid_flag[at]).astype(jnp.float32)

    faces_x = [
        jnp.concatenate([populations[:, :, at, None, :], fluid(None, slice(None), at, None, slice(None))], axis=0)
        for at in (0, -1)
    ]
    x_low = lax.ppermute(faces_x[1], "gx", [(i, (i + 1) % count_x) for i in range(count_x)])
    x_high = lax.ppermute(faces_x[0], "gx", [((i + 1) % count_x, i) for i in range(count_x)])
    faces_y = [
        jnp.concatenate(
            [
                x_low[:, :, :, at, None],
                jnp.concatenate(
                    [populations[:, :, :, at, None], fluid(None, slice(None), slice(None), at, None)], axis=0
                ),
                x_high[:, :, :, at, None],
            ],
            axis=2,
        )
        for at in (0, -1)
    ]
    y_low = lax.ppermute(faces_y[1], "gy", [(j, j + 1) for j in range(count_y - 1)])
    y_high = lax.ppermute(faces_y[0], "gy", [(j + 1, j) for j in range(count_y - 1)])
    return (
        x_low,
        x_high,
        y_low[:, :, 1:-1],
        y_high[:, :, 1:-1],
        y_low[:, :, :1],
        y_low[:, :, -1:],
        y_high[:, :, :1],
        y_high[:, :, -1:],
    )


def on_device(
    populations, solid_flag, cell_patch, patch_zone, old_pressure, leakage, conductance, neighbour
):
    halos = exchange_halos(populations, solid_flag)
    new_populations, momentum_parts = lbm_step(populations, solid_flag, halos)
    patch_flux = patch_sums(momentum_parts, cell_patch, patch_zone.shape[0])
    zone_dev = old_pressure.shape[0]
    openings = patch_zone.shape[0]
    devices = lax.axis_size("gx") * lax.axis_size("gy")
    capacity = max(2, (2 * openings + devices - 1) // devices)
    owner_block = patch_zone // zone_dev
    local_zone = patch_zone - owner_block * zone_dev
    patch_order = jnp.arange(openings, dtype=jnp.int32)
    earlier_same = (owner_block[:, None] == owner_block[None, :]) & (
        patch_order[:, None] > patch_order[None, :]
    )
    slot_rank = jnp.sum(earlier_same.astype(jnp.int32), axis=1)
    slot_index = owner_block * capacity + slot_rank
    targets = jnp.arange(devices * capacity, dtype=jnp.int32)
    placed = slot_index[:, None] == targets[None, :]
    send_flux = jnp.sum(jnp.where(placed, patch_flux[:, None], 0.0), axis=0)
    send_zone = jnp.sum(jnp.where(placed, local_zone.astype(jnp.float32)[:, None], 0.0), axis=0)
    count_x = lax.axis_size("gx")
    count_y = lax.axis_size("gy")
    outgoing = jnp.stack([send_flux, send_zone]).reshape(2, count_x, count_y * capacity)
    arrived = lax.all_to_all(outgoing, "gx", split_axis=1, concat_axis=1, tiled=True)
    arrived = arrived.reshape(2, count_x, count_y, capacity)
    zones = jnp.arange(zone_dev, dtype=jnp.float32)
    matched = arrived[1][..., None] == zones
    gathered = jnp.sum(jnp.where(matched, arrived[0][..., None], 0.0), axis=(0, 2))
    coupled, total = couple(old_pressure, leakage, conductance, neighbour)
    column = lax.axis_index("gy")
    is_own = (jnp.arange(count_y, dtype=jnp.int32) == column)[:, None]
    numer = gathered + jnp.where(is_own, coupled[None, :], 0.0)
    denom = jnp.where(is_own, total[None, :], 0.0)
    summed = row_sum(jnp.stack([numer, denom]), "gy", count_y)
    row_pressure = summed[0] / summed[1]
    zone_pressure = lax.dynamic_index_in_dim(row_pressure, column, axis=0, keepdims=False)
    answered = jnp.sum(jnp.where(matched, row_pressure[None, :, None, :], 0.0), axis=3)
    returned = lax.all_to_all(
        answered.reshape(count_x, count_y * capacity), "gx", split_axis=0, concat_axis=0, tiled=True
    ).reshape(-1)
    opening_pressure = jnp.sum(jnp.where(placed, returned[None, :], 0.0), axis=1)
    return (new_populations, zone_pressure, opening_pressure)


def row_sum(values, axis, count):
    if count & (count - 1):
        return lax.psum(values, axis)
    step = 1
    while step < count:
        values = values + lax.ppermute(values, axis, [(j, j ^ step) for j in range(count)])
        step *= 2
    return values


def patch_sums(momentum_parts, cell_patch, openings):
    depth, width_x, width_y = cell_patch.shape
    rows = depth * width_x
    parts = momentum_parts.reshape(3, rows, width_y)
    patch = cell_patch.reshape(rows, width_y)
    lanes = 128
    high = patch // lanes
    low = patch - high * lanes
    groups = openings // lanes
    picked = jnp.where(
        high[None, None] == jnp.arange(groups, dtype=jnp.int32)[None, :, None, None],
        parts[:, None],
        jnp.zeros((), jnp.bfloat16),
    )
    onehot = (low[:, :, None] == jnp.arange(lanes, dtype=jnp.int32)[None, None, :]).astype(
        jnp.bfloat16
    )
    sums = jnp.einsum("khry,ryl->khl", picked, onehot, preferred_element_type=jnp.float32)
    return FACE_AREA * (sums[0] + sums[1] + sums[2]).reshape(openings)


def couple(old_pressure, leakage, conductance, neighbour):
    zone_dev = old_pressure.shape[0]
    chosen = neighbour[:, :, None] == jnp.arange(zone_dev, dtype=jnp.int32)[None, None, :]
    neighbour_pressure = jnp.sum(jnp.where(chosen, old_pressure[None, None, :], 0.0), axis=2)
    coupled = jnp.zeros_like(old_pressure)
    total = leakage
    for link in range(conductance.shape[0]):
        coupled = coupled + conductance[link] * neighbour_pressure[link]
        total = total + conductance[link]
    return coupled, total


def collide_list(planes):
    density = jnp.zeros_like(planes[0])
    for direction in range(19):
        density = density + planes[direction]
    velocity = []
    for component in range(3):
        total = jnp.zeros_like(planes[0])
        for direction in range(19):
            sign = int(DIRECTIONS[direction, component])
            if sign != 0:
                total = total + float(sign) * planes[direction]
        velocity.append(total / density)
    speed_sq = velocity[0] * velocity[0] + velocity[1] * velocity[1] + velocity[2] * velocity[2]
    relaxed = []
    for direction in range(19):
        along = jnp.zeros_like(density)
        for component in range(3):
            sign = int(DIRECTIONS[direction, component])
            if sign != 0:
                along = along + float(sign) * velocity[component]
        equilibrium = (
            LATTICE_WEIGHTS[direction]
            * density
            * (1.0 + 3.0 * along + 4.5 * along * along - 1.5 * speed_sq)
        )
        relaxed.append(planes[direction] - OMEGA * (planes[direction] - equilibrium))
    return relaxed


def shift_x(plane, step, edge, xi, width_x):
    if step == 1:
        return jnp.where(xi == 0, edge, pltpu.roll(plane, 1, 0))
    if step == -1:
        return jnp.where(xi == width_x - 1, edge, pltpu.roll(plane, width_x - 1, 0))
    return plane


def shift_plane(plane, step_x, step_y, row, column, corner, xi, yi, width_x, width_y):
    moved = shift_x(plane, step_x, row, xi, width_x)
    if step_y == 0:
        return moved
    edge = shift_x(column, step_x, corner, xi, width_x)
    if step_y == 1:
        return jnp.where(yi == 0, edge, pltpu.roll(moved, 1, 1))
    return jnp.where(yi == width_y - 1, edge, pltpu.roll(moved, width_y - 1, 1))


def lbm_kernel(
    pop_ref, solid_ref, xlo_ref, xhi_ref, ylo_ref, yhi_ref,
    cll_ref, chl_ref, clh_ref, chh_ref,
    new_ref, mom_ref, rel_ref,
):
    _, depth, width_x, width_y = pop_ref.shape
    shape = (width_x, width_y)
    xi = lax.broadcasted_iota(jnp.int32, shape, 0)
    yi = lax.broadcasted_iota(jnp.int32, shape, 1)
    for level in range(depth):
        relaxed = collide_list([pop_ref[d, level] for d in range(19)])
        for d in range(19):
            rel_ref[d, level] = relaxed[d]

    def halo(ref):
        values = [ref[d] for d in range(20)]
        return collide_list(values[:19]), values[19]

    xlo, xlo_f = halo(xlo_ref)
    xhi, xhi_f = halo(xhi_ref)
    ylo, ylo_f = halo(ylo_ref)
    yhi, yhi_f = halo(yhi_ref)
    cll, cll_f = halo(cll_ref)
    chl, chl_f = halo(chl_ref)
    clh, clh_f = halo(clh_ref)
    chh, chh_f = halo(chh_ref)

    def pieces(step_x, step_y, level, direction):
        if direction is None:
            x_lo, x_hi, y_lo, y_hi = xlo_f, xhi_f, ylo_f, yhi_f
            c_ll, c_hl, c_lh, c_hh = cll_f, chl_f, clh_f, chh_f
        else:
            x_lo, x_hi, y_lo, y_hi = xlo[direction], xhi[direction], ylo[direction], yhi[direction]
            c_ll, c_hl, c_lh, c_hh = cll[direction], chl[direction], clh[direction], chh[direction]
        row = x_lo[level] if step_x == 1 else x_hi[level]
        column = y_lo[level] if step_y == 1 else y_hi[level]
        if step_y == 1:
            corner = c_ll[level] if step_x == 1 else c_hl[level]
        else:
            corner = c_lh[level] if step_x == 1 else c_hh[level]
        row = jnp.broadcast_to(row, shape)
        column = jnp.broadcast_to(column, shape)
        corner = jnp.broadcast_to(corner, shape)
        return row, column, corner

    for level in range(depth):
        solid = solid_ref[level] == 1
        momentum = jnp.zeros(shape, jnp.float32)
        for d in range(19):
            step_x, step_y, step_z = (int(v) for v in DIRECTIONS[d])
            source_level = level - step_z
            kept = pop_ref[d, level]
            bounced = rel_ref[OPPOSITE[d], level]
            if 0 <= source_level < depth:
                row, column, corner = pieces(step_x, step_y, source_level, d)
                source = shift_plane(
                    rel_ref[d, source_level], step_x, step_y, row, column, corner,
                    xi, yi, width_x, width_y,
                )
                frow, fcolumn, fcorner = pieces(step_x, step_y, source_level, None)
                fluid = 1.0 - solid_ref[source_level].astype(jnp.float32)
                open_source = shift_plane(
                    fluid, step_x, step_y, frow, fcolumn, fcorner,
                    xi, yi, width_x, width_y,
                )
                pulled = jnp.where(open_source > 0.5, source, bounced)
            else:
                pulled = bounced
            value = jnp.where(solid, kept, pulled)
            new_ref[d, level] = value
            if step_x != 0:
                momentum = momentum + float(step_x) * value
        upper = momentum.astype(jnp.bfloat16)
        rest = momentum - upper.astype(jnp.float32)
        middle = rest.astype(jnp.bfloat16)
        lower = (rest - middle.astype(jnp.float32)).astype(jnp.bfloat16)
        mom_ref[0, level] = upper
        mom_ref[1, level] = middle
        mom_ref[2, level] = lower


def lbm_step(populations, solid_flag, halos, interpret=False):
    depth, width_x, width_y = solid_flag.shape
    return pl.pallas_call(
        lbm_kernel,
        out_shape=(
            jax.ShapeDtypeStruct(populations.shape, jnp.float32),
            jax.ShapeDtypeStruct((3,) + solid_flag.shape, jnp.bfloat16),
        ),
        scratch_shapes=[pltpu.VMEM(populations.shape, jnp.float32)],
        interpret=interpret,
    )(populations, solid_flag, *halos)


def solution(mesh):
    placed = (
        P(None, None, "gx", "gy"),
        P(None, "gx", "gy"),
        P(None, "gx", "gy"),
        P(("gx", "gy")),
        P(("gx", "gy")),
        P(("gx", "gy")),
        P(None, ("gx", "gy")),
        P(None, ("gx", "gy")),
    )
    return jax.shard_map(
        on_device,
        mesh=mesh,
        in_specs=placed,
        out_specs=(P(None, None, "gx", "gy"), P(("gx", "gy")), P(("gx", "gy"))),
        check_vma=False,
    )
```

```python
import jax
import jax.numpy as jnp
import numpy as np
from jax import lax
from jax.experimental import pallas as pl
from jax.experimental.pallas import tpu as pltpu
from jax.sharding import PartitionSpec as P

DIRECTIONS = np.array(
    [
        [0, 0, 0],
        [1, 0, 0],
        [-1, 0, 0],
        [0, 1, 0],
        [0, -1, 0],
        [0, 0, 1],
        [0, 0, -1],
        [1, 1, 0],
        [-1, -1, 0],
        [1, -1, 0],
        [-1, 1, 0],
        [1, 0, 1],
        [-1, 0, -1],
        [1, 0, -1],
        [-1, 0, 1],
        [0, 1, 1],
        [0, -1, -1],
        [0, 1, -1],
        [0, -1, 1],
    ]
)
OPPOSITE = [0, 2, 1, 4, 3, 6, 5, 8, 7, 10, 9, 12, 11, 14, 13, 16, 15, 18, 17]
LATTICE_WEIGHTS = [1.0 / 3.0] + [1.0 / 18.0] * 6 + [1.0 / 36.0] * 12
OMEGA = 1.25
FACE_AREA = 0.25


def with_halo(cells, sides, width):
    for axis, dim in sides:
        count = lax.axis_size(axis)
        head = lax.slice_in_dim(cells, 0, width, axis=dim)
        tail = lax.slice_in_dim(cells, cells.shape[dim] - width, cells.shape[dim], axis=dim)
        cells = jnp.concatenate(
            [
                lax.ppermute(tail, axis, [(i, (i + 1) % count) for i in range(count)]),
                cells,
                lax.ppermute(head, axis, [((i + 1) % count, i) for i in range(count)]),
            ],
            axis=dim,
        )
    return cells


def moment(populations, component):
    total = jnp.zeros_like(populations[0])
    for direction in range(19):
        sign = int(DIRECTIONS[direction, component])
        if sign != 0:
            total = total + float(sign) * populations[direction]
    return total


def collide(populations):
    density = jnp.zeros_like(populations[0])
    for direction in range(19):
        density = density + populations[direction]
    velocity = [moment(populations, component) / density for component in range(3)]
    speed_sq = velocity[0] * velocity[0] + velocity[1] * velocity[1] + velocity[2] * velocity[2]
    relaxed = []
    for direction in range(19):
        along = jnp.zeros_like(density)
        for component in range(3):
            sign = int(DIRECTIONS[direction, component])
            if sign != 0:
                along = along + float(sign) * velocity[component]
        equilibrium = (
            LATTICE_WEIGHTS[direction]
            * density
            * (1.0 + 3.0 * along + 4.5 * along * along - 1.5 * speed_sq)
        )
        relaxed.append(populations[direction] - OMEGA * (populations[direction] - equilibrium))
    return jnp.stack(relaxed)


def stream(post_pad, flag_pad, relaxed, populations, solid_flag):
    depth, width_x, width_y = solid_flag.shape
    passed = []
    for direction in range(19):
        step_x = int(DIRECTIONS[direction, 0])
        step_y = int(DIRECTIONS[direction, 1])
        step_z = int(DIRECTIONS[direction, 2])
        source = post_pad[
            direction,
            1 - step_z : 1 - step_z + depth,
            1 - step_x : 1 - step_x + width_x,
            1 - step_y : 1 - step_y + width_y,
        ]
        open_source = flag_pad[
            1 - step_z : 1 - step_z + depth,
            1 - step_x : 1 - step_x + width_x,
            1 - step_y : 1 - step_y + width_y,
        ]
        pulled = open_source * source + (1.0 - open_source) * relaxed[OPPOSITE[direction]]
        passed.append(jnp.where(solid_flag == 1, populations[direction], pulled))
    return jnp.stack(passed)


def relax(inflow, old_pressure, leakage, conductance, neighbour):
    coupled = jnp.zeros_like(inflow)
    total = leakage
    for link in range(conductance.shape[0]):
        coupled = coupled + conductance[link] * old_pressure[neighbour[link]]
        total = total + conductance[link]
    return (inflow + coupled) / total


def exchange_halos(populations, fluid):
    count_x = lax.axis_size("gx")
    count_y = lax.axis_size("gy")
    faces_x = [
        jnp.concatenate([populations[:, :, at, None, :], fluid[None, :, at, None, :]], axis=0)
        for at in (0, -1)
    ]
    x_low = lax.ppermute(faces_x[1], "gx", [(i, (i + 1) % count_x) for i in range(count_x)])
    x_high = lax.ppermute(faces_x[0], "gx", [((i + 1) % count_x, i) for i in range(count_x)])
    faces_y = [
        jnp.concatenate(
            [
                x_low[:, :, :, at, None],
                jnp.concatenate(
                    [populations[:, :, :, at, None], fluid[None, :, :, at, None]], axis=0
                ),
                x_high[:, :, :, at, None],
            ],
            axis=2,
        )
        for at in (0, -1)
    ]
    y_low = lax.ppermute(faces_y[1], "gy", [(j, j + 1) for j in range(count_y - 1)])
    y_high = lax.ppermute(faces_y[0], "gy", [(j + 1, j) for j in range(count_y - 1)])
    return (
        x_low,
        x_high,
        y_low[:, :, 1:-1],
        y_high[:, :, 1:-1],
        y_low[:, :, :1],
        y_low[:, :, -1:],
        y_high[:, :, :1],
        y_high[:, :, -1:],
    )


def on_device(
    populations, solid_flag, cell_patch, patch_zone, old_pressure, leakage, conductance, neighbour
):
    fluid = (1 - solid_flag).astype(jnp.float32)
    halos = exchange_halos(populations, fluid)
    new_populations, momentum_x = lbm_step(populations, solid_flag, halos)
    patch_flux = patch_sums(momentum_x, cell_patch, patch_zone.shape[0])
    zone_dev = old_pressure.shape[0]
    openings = patch_zone.shape[0]
    devices = lax.axis_size("gx") * lax.axis_size("gy")
    capacity = max(2, (2 * openings + devices - 1) // devices)
    owner_block = patch_zone // zone_dev
    local_zone = patch_zone - owner_block * zone_dev
    patch_order = jnp.arange(openings, dtype=jnp.int32)
    earlier_same = (owner_block[:, None] == owner_block[None, :]) & (
        patch_order[:, None] > patch_order[None, :]
    )
    slot_rank = jnp.sum(earlier_same.astype(jnp.int32), axis=1)
    slot_index = owner_block * capacity + slot_rank
    targets = jnp.arange(devices * capacity, dtype=jnp.int32)
    placed = slot_index[:, None] == targets[None, :]
    send_flux = jnp.sum(jnp.where(placed, patch_flux[:, None], 0.0), axis=0)
    send_zone = jnp.sum(jnp.where(placed, local_zone.astype(jnp.float32)[:, None], 0.0), axis=0)
    count_x = lax.axis_size("gx")
    count_y = lax.axis_size("gy")
    outgoing = jnp.stack([send_flux, send_zone]).reshape(2, count_x, count_y * capacity)
    arrived = lax.all_to_all(outgoing, "gx", split_axis=1, concat_axis=1, tiled=True)
    arrived = arrived.reshape(2, count_x, count_y, capacity)
    zones = jnp.arange(zone_dev, dtype=jnp.float32)
    matched = arrived[1][..., None] == zones
    gathered = jnp.sum(jnp.where(matched, arrived[0][..., None], 0.0), axis=(0, 2))
    coupled, total = couple(old_pressure, leakage, conductance, neighbour)
    column = lax.axis_index("gy")
    is_own = (jnp.arange(count_y, dtype=jnp.int32) == column)[:, None]
    numer = gathered + jnp.where(is_own, coupled[None, :], 0.0)
    denom = jnp.where(is_own, total[None, :], 0.0)
    summed = row_sum(jnp.stack([numer, denom]), "gy", count_y)
    row_pressure = summed[0] / summed[1]
    zone_pressure = lax.dynamic_index_in_dim(row_pressure, column, axis=0, keepdims=False)
    answered = jnp.sum(jnp.where(matched, row_pressure[None, :, None, :], 0.0), axis=3)
    returned = lax.all_to_all(
        answered.reshape(count_x, count_y * capacity), "gx", split_axis=0, concat_axis=0, tiled=True
    ).reshape(-1)
    opening_pressure = jnp.sum(jnp.where(placed, returned[None, :], 0.0), axis=1)
    return (new_populations, zone_pressure, opening_pressure)


def row_sum(values, axis, count):
    if count & (count - 1):
        return lax.psum(values, axis)
    step = count // 2
    while step:
        values = values + lax.ppermute(values, axis, [(j, j ^ step) for j in range(count)])
        step //= 2
    return values


def patch_sums(momentum_x, cell_patch, openings):
    depth, width_x, width_y = cell_patch.shape
    rows = depth * width_x
    momentum = momentum_x.reshape(rows, width_y)
    patch = cell_patch.reshape(rows, width_y)
    lanes = 128
    high = patch // lanes
    low = patch - high * lanes
    groups = openings // lanes
    upper = lax.reduce_precision(momentum, exponent_bits=8, mantissa_bits=7)
    rest = momentum - upper
    middle = lax.reduce_precision(rest, exponent_bits=8, mantissa_bits=7)
    lower = rest - middle
    parts = jnp.stack([upper, middle, lower])
    picked = jnp.where(
        high[None, None] == jnp.arange(groups, dtype=jnp.int32)[None, :, None, None],
        parts[:, None],
        0.0,
    ).astype(jnp.bfloat16)
    onehot = (low[:, :, None] == jnp.arange(lanes, dtype=jnp.int32)[None, None, :]).astype(
        jnp.bfloat16
    )
    sums = jnp.einsum("khry,ryl->khl", picked, onehot, preferred_element_type=jnp.float32)
    return FACE_AREA * (sums[0] + sums[1] + sums[2]).reshape(openings)


def couple(old_pressure, leakage, conductance, neighbour):
    zone_dev = old_pressure.shape[0]
    chosen = neighbour[:, :, None] == jnp.arange(zone_dev, dtype=jnp.int32)[None, None, :]
    neighbour_pressure = jnp.sum(jnp.where(chosen, old_pressure[None, None, :], 0.0), axis=2)
    coupled = jnp.zeros_like(old_pressure)
    total = leakage
    for link in range(conductance.shape[0]):
        coupled = coupled + conductance[link] * neighbour_pressure[link]
        total = total + conductance[link]
    return coupled, total


def collide_list(planes):
    density = jnp.zeros_like(planes[0])
    for direction in range(19):
        density = density + planes[direction]
    velocity = []
    for component in range(3):
        total = jnp.zeros_like(planes[0])
        for direction in range(19):
            sign = int(DIRECTIONS[direction, component])
            if sign != 0:
                total = total + float(sign) * planes[direction]
        velocity.append(total / density)
    speed_sq = velocity[0] * velocity[0] + velocity[1] * velocity[1] + velocity[2] * velocity[2]
    relaxed = []
    for direction in range(19):
        along = jnp.zeros_like(density)
        for component in range(3):
            sign = int(DIRECTIONS[direction, component])
            if sign != 0:
                along = along + float(sign) * velocity[component]
        equilibrium = (
            LATTICE_WEIGHTS[direction]
            * density
            * (1.0 + 3.0 * along + 4.5 * along * along - 1.5 * speed_sq)
        )
        relaxed.append(planes[direction] - OMEGA * (planes[direction] - equilibrium))
    return relaxed


def shift_x(plane, step, edge, xi, width_x):
    if step == 1:
        return jnp.where(xi == 0, edge, pltpu.roll(plane, 1, 0))
    if step == -1:
        return jnp.where(xi == width_x - 1, edge, pltpu.roll(plane, width_x - 1, 0))
    return plane


def shift_plane(plane, step_x, step_y, row, column, corner, xi, yi, width_x, width_y):
    moved = shift_x(plane, step_x, row, xi, width_x)
    if step_y == 0:
        return moved
    edge = shift_x(column, step_x, corner, xi, width_x)
    if step_y == 1:
        return jnp.where(yi == 0, edge, pltpu.roll(moved, 1, 1))
    return jnp.where(yi == width_y - 1, edge, pltpu.roll(moved, width_y - 1, 1))


def lbm_kernel(
    pop_ref, solid_ref, xlo_ref, xhi_ref, ylo_ref, yhi_ref,
    cll_ref, chl_ref, clh_ref, chh_ref,
    new_ref, mom_ref, rel_ref,
):
    _, depth, width_x, width_y = pop_ref.shape
    shape = (width_x, width_y)
    xi = lax.broadcasted_iota(jnp.int32, shape, 0)
    yi = lax.broadcasted_iota(jnp.int32, shape, 1)
    for level in range(depth):
        relaxed = collide_list([pop_ref[d, level] for d in range(19)])
        for d in range(19):
            rel_ref[d, level] = relaxed[d]

    def halo(ref):
        values = [ref[d] for d in range(20)]
        return collide_list(values[:19]), values[19]

    xlo, xlo_f = halo(xlo_ref)
    xhi, xhi_f = halo(xhi_ref)
    ylo, ylo_f = halo(ylo_ref)
    yhi, yhi_f = halo(yhi_ref)
    cll, cll_f = halo(cll_ref)
    chl, chl_f = halo(chl_ref)
    clh, clh_f = halo(clh_ref)
    chh, chh_f = halo(chh_ref)

    def pieces(step_x, step_y, level, direction):
        if direction is None:
            x_lo, x_hi, y_lo, y_hi = xlo_f, xhi_f, ylo_f, yhi_f
            c_ll, c_hl, c_lh, c_hh = cll_f, chl_f, clh_f, chh_f
        else:
            x_lo, x_hi, y_lo, y_hi = xlo[direction], xhi[direction], ylo[direction], yhi[direction]
            c_ll, c_hl, c_lh, c_hh = cll[direction], chl[direction], clh[direction], chh[direction]
        row = x_lo[level] if step_x == 1 else x_hi[level]
        column = y_lo[level] if step_y == 1 else y_hi[level]
        if step_y == 1:
            corner = c_ll[level] if step_x == 1 else c_hl[level]
        else:
            corner = c_lh[level] if step_x == 1 else c_hh[level]
        row = jnp.broadcast_to(row, shape)
        column = jnp.broadcast_to(column, shape)
        corner = jnp.broadcast_to(corner, shape)
        return row, column, corner

    for level in range(depth):
        solid = solid_ref[level] == 1
        momentum = jnp.zeros(shape, jnp.float32)
        for d in range(19):
            step_x, step_y, step_z = (int(v) for v in DIRECTIONS[d])
            source_level = level - step_z
            kept = pop_ref[d, level]
            bounced = rel_ref[OPPOSITE[d], level]
            if 0 <= source_level < depth:
                row, column, corner = pieces(step_x, step_y, source_level, d)
                source = shift_plane(
                    rel_ref[d, source_level], step_x, step_y, row, column, corner,
                    xi, yi, width_x, width_y,
                )
                frow, fcolumn, fcorner = pieces(step_x, step_y, source_level, None)
                fluid = 1.0 - solid_ref[source_level].astype(jnp.float32)
                open_source = shift_plane(
                    fluid, step_x, step_y, frow, fcolumn, fcorner,
                    xi, yi, width_x, width_y,
                )
                pulled = jnp.where(open_source > 0.5, source, bounced)
            else:
                pulled = bounced
            value = jnp.where(solid, kept, pulled)
            new_ref[d, level] = value
            if step_x != 0:
                momentum = momentum + float(step_x) * value
        mom_ref[level] = momentum


def lbm_step(populations, solid_flag, halos, interpret=False):
    depth, width_x, width_y = solid_flag.shape
    return pl.pallas_call(
        lbm_kernel,
        out_shape=(
            jax.ShapeDtypeStruct(populations.shape, jnp.float32),
            jax.ShapeDtypeStruct(solid_flag.shape, jnp.float32),
        ),
        scratch_shapes=[pltpu.VMEM(populations.shape, jnp.float32)],
        interpret=interpret,
    )(populations, solid_flag, *halos)


def solution(mesh):
    placed = (
        P(None, None, "gx", "gy"),
        P(None, "gx", "gy"),
        P(None, "gx", "gy"),
        P(("gx", "gy")),
        P(("gx", "gy")),
        P(("gx", "gy")),
        P(None, ("gx", "gy")),
        P(None, ("gx", "gy")),
    )
    return jax.shard_map(
        on_device,
        mesh=mesh,
        in_specs=placed,
        out_specs=(P(None, None, "gx", "gy"), P(("gx", "gy")), P(("gx", "gy"))),
        check_vma=False,
    )
```

```python
import jax
import jax.numpy as jnp
import numpy as np
from jax import lax
from jax.experimental import pallas as pl
from jax.experimental.pallas import tpu as pltpu
from jax.sharding import PartitionSpec as P

DIRECTIONS = np.array(
    [
        [0, 0, 0],
        [1, 0, 0],
        [-1, 0, 0],
        [0, 1, 0],
        [0, -1, 0],
        [0, 0, 1],
        [0, 0, -1],
        [1, 1, 0],
        [-1, -1, 0],
        [1, -1, 0],
        [-1, 1, 0],
        [1, 0, 1],
        [-1, 0, -1],
        [1, 0, -1],
        [-1, 0, 1],
        [0, 1, 1],
        [0, -1, -1],
        [0, 1, -1],
        [0, -1, 1],
    ]
)
OPPOSITE = [0, 2, 1, 4, 3, 6, 5, 8, 7, 10, 9, 12, 11, 14, 13, 16, 15, 18, 17]
LATTICE_WEIGHTS = [1.0 / 3.0] + [1.0 / 18.0] * 6 + [1.0 / 36.0] * 12
OMEGA = 1.25
FACE_AREA = 0.25


def with_halo(cells, sides, width):
    for axis, dim in sides:
        count = lax.axis_size(axis)
        head = lax.slice_in_dim(cells, 0, width, axis=dim)
        tail = lax.slice_in_dim(cells, cells.shape[dim] - width, cells.shape[dim], axis=dim)
        cells = jnp.concatenate(
            [
                lax.ppermute(tail, axis, [(i, (i + 1) % count) for i in range(count)]),
                cells,
                lax.ppermute(head, axis, [((i + 1) % count, i) for i in range(count)]),
            ],
            axis=dim,
        )
    return cells


def moment(populations, component):
    total = jnp.zeros_like(populations[0])
    for direction in range(19):
        sign = int(DIRECTIONS[direction, component])
        if sign != 0:
            total = total + float(sign) * populations[direction]
    return total


def collide(populations):
    density = jnp.zeros_like(populations[0])
    for direction in range(19):
        density = density + populations[direction]
    velocity = [moment(populations, component) / density for component in range(3)]
    speed_sq = velocity[0] * velocity[0] + velocity[1] * velocity[1] + velocity[2] * velocity[2]
    relaxed = []
    for direction in range(19):
        along = jnp.zeros_like(density)
        for component in range(3):
            sign = int(DIRECTIONS[direction, component])
            if sign != 0:
                along = along + float(sign) * velocity[component]
        equilibrium = (
            LATTICE_WEIGHTS[direction]
            * density
            * (1.0 + 3.0 * along + 4.5 * along * along - 1.5 * speed_sq)
        )
        relaxed.append(populations[direction] - OMEGA * (populations[direction] - equilibrium))
    return jnp.stack(relaxed)


def stream(post_pad, flag_pad, relaxed, populations, solid_flag):
    depth, width_x, width_y = solid_flag.shape
    passed = []
    for direction in range(19):
        step_x = int(DIRECTIONS[direction, 0])
        step_y = int(DIRECTIONS[direction, 1])
        step_z = int(DIRECTIONS[direction, 2])
        source = post_pad[
            direction,
            1 - step_z : 1 - step_z + depth,
            1 - step_x : 1 - step_x + width_x,
            1 - step_y : 1 - step_y + width_y,
        ]
        open_source = flag_pad[
            1 - step_z : 1 - step_z + depth,
            1 - step_x : 1 - step_x + width_x,
            1 - step_y : 1 - step_y + width_y,
        ]
        pulled = open_source * source + (1.0 - open_source) * relaxed[OPPOSITE[direction]]
        passed.append(jnp.where(solid_flag == 1, populations[direction], pulled))
    return jnp.stack(passed)


def relax(inflow, old_pressure, leakage, conductance, neighbour):
    coupled = jnp.zeros_like(inflow)
    total = leakage
    for link in range(conductance.shape[0]):
        coupled = coupled + conductance[link] * old_pressure[neighbour[link]]
        total = total + conductance[link]
    return (inflow + coupled) / total


def exchange_halos(populations, fluid):
    count_x = lax.axis_size("gx")
    count_y = lax.axis_size("gy")
    faces_x = [
        jnp.concatenate([populations[:, :, at, None, :], fluid[None, :, at, None, :]], axis=0)
        for at in (0, -1)
    ]
    x_low = lax.ppermute(faces_x[1], "gx", [(i, (i + 1) % count_x) for i in range(count_x)])
    x_high = lax.ppermute(faces_x[0], "gx", [((i + 1) % count_x, i) for i in range(count_x)])
    faces_y = [
        jnp.concatenate(
            [
                x_low[:, :, :, at, None],
                jnp.concatenate(
                    [populations[:, :, :, at, None], fluid[None, :, :, at, None]], axis=0
                ),
                x_high[:, :, :, at, None],
            ],
            axis=2,
        )
        for at in (0, -1)
    ]
    y_low = lax.ppermute(faces_y[1], "gy", [(j, j + 1) for j in range(count_y - 1)])
    y_high = lax.ppermute(faces_y[0], "gy", [(j + 1, j) for j in range(count_y - 1)])
    return (x_low, x_high, y_low, y_high)


def on_device(
    populations, solid_flag, cell_patch, patch_zone, old_pressure, leakage, conductance, neighbour
):
    fluid = (1 - solid_flag).astype(jnp.float32)
    halos = exchange_halos(populations, fluid)
    new_populations, momentum_x = lbm_step(populations, solid_flag, halos)
    patch_flux = patch_sums(momentum_x, cell_patch, patch_zone.shape[0])
    zone_dev = old_pressure.shape[0]
    openings = patch_zone.shape[0]
    devices = lax.axis_size("gx") * lax.axis_size("gy")
    capacity = max(2, (2 * openings + devices - 1) // devices)
    owner_block = patch_zone // zone_dev
    local_zone = patch_zone - owner_block * zone_dev
    patch_order = jnp.arange(openings, dtype=jnp.int32)
    earlier_same = (owner_block[:, None] == owner_block[None, :]) & (
        patch_order[:, None] > patch_order[None, :]
    )
    slot_rank = jnp.sum(earlier_same.astype(jnp.int32), axis=1)
    slot_index = owner_block * capacity + slot_rank
    targets = jnp.arange(devices * capacity, dtype=jnp.int32)
    placed = slot_index[:, None] == targets[None, :]
    send_flux = jnp.sum(jnp.where(placed, patch_flux[:, None], 0.0), axis=0)
    send_zone = jnp.sum(jnp.where(placed, local_zone.astype(jnp.float32)[:, None], 0.0), axis=0)
    count_x = lax.axis_size("gx")
    count_y = lax.axis_size("gy")
    outgoing = jnp.stack([send_flux, send_zone]).reshape(2, count_x, count_y * capacity)
    arrived = lax.all_to_all(outgoing, "gx", split_axis=1, concat_axis=1, tiled=True)
    arrived = arrived.reshape(2, count_x, count_y, capacity)
    zones = jnp.arange(zone_dev, dtype=jnp.float32)
    matched = arrived[1][..., None] == zones
    gathered = jnp.sum(jnp.where(matched, arrived[0][..., None], 0.0), axis=(0, 2))
    coupled, total = couple(old_pressure, leakage, conductance, neighbour)
    column = lax.axis_index("gy")
    is_own = (jnp.arange(count_y, dtype=jnp.int32) == column)[:, None]
    numer = gathered + jnp.where(is_own, coupled[None, :], 0.0)
    denom = jnp.where(is_own, total[None, :], 0.0)
    summed = row_sum(jnp.stack([numer, denom]), "gy", count_y)
    row_pressure = summed[0] / summed[1]
    zone_pressure = lax.dynamic_index_in_dim(row_pressure, column, axis=0, keepdims=False)
    answered = jnp.sum(jnp.where(matched, row_pressure[None, :, None, :], 0.0), axis=3)
    returned = lax.all_to_all(
        answered.reshape(count_x, count_y * capacity), "gx", split_axis=0, concat_axis=0, tiled=True
    ).reshape(-1)
    opening_pressure = jnp.sum(jnp.where(placed, returned[None, :], 0.0), axis=1)
    return (new_populations, zone_pressure, opening_pressure)


def row_sum(values, axis, count):
    if count & (count - 1):
        return lax.psum(values, axis)
    step = count // 2
    while step:
        values = values + lax.ppermute(values, axis, [(j, j ^ step) for j in range(count)])
        step //= 2
    return values


def patch_sums(momentum_x, cell_patch, openings):
    depth, width_x, width_y = cell_patch.shape
    rows = depth * width_x
    momentum = momentum_x.reshape(rows, width_y)
    patch = cell_patch.reshape(rows, width_y)
    lanes = 128
    high = patch // lanes
    low = patch - high * lanes
    groups = openings // lanes
    upper = lax.reduce_precision(momentum, exponent_bits=8, mantissa_bits=7)
    rest = momentum - upper
    middle = lax.reduce_precision(rest, exponent_bits=8, mantissa_bits=7)
    lower = rest - middle
    parts = jnp.stack([upper, middle, lower])
    picked = jnp.where(
        high[None, None] == jnp.arange(groups, dtype=jnp.int32)[None, :, None, None],
        parts[:, None],
        0.0,
    ).astype(jnp.bfloat16)
    onehot = (low[:, :, None] == jnp.arange(lanes, dtype=jnp.int32)[None, None, :]).astype(
        jnp.bfloat16
    )
    sums = jnp.einsum("khry,ryl->khl", picked, onehot, preferred_element_type=jnp.float32)
    return FACE_AREA * (sums[0] + sums[1] + sums[2]).reshape(openings)


def couple(old_pressure, leakage, conductance, neighbour):
    zone_dev = old_pressure.shape[0]
    chosen = neighbour[:, :, None] == jnp.arange(zone_dev, dtype=jnp.int32)[None, None, :]
    neighbour_pressure = jnp.sum(jnp.where(chosen, old_pressure[None, None, :], 0.0), axis=2)
    coupled = jnp.zeros_like(old_pressure)
    total = leakage
    for link in range(conductance.shape[0]):
        coupled = coupled + conductance[link] * neighbour_pressure[link]
        total = total + conductance[link]
    return coupled, total


def collide_list(planes):
    density = jnp.zeros_like(planes[0])
    for direction in range(19):
        density = density + planes[direction]
    velocity = []
    for component in range(3):
        total = jnp.zeros_like(planes[0])
        for direction in range(19):
            sign = int(DIRECTIONS[direction, component])
            if sign != 0:
                total = total + float(sign) * planes[direction]
        velocity.append(total / density)
    speed_sq = velocity[0] * velocity[0] + velocity[1] * velocity[1] + velocity[2] * velocity[2]
    relaxed = []
    for direction in range(19):
        along = jnp.zeros_like(density)
        for component in range(3):
            sign = int(DIRECTIONS[direction, component])
            if sign != 0:
                along = along + float(sign) * velocity[component]
        equilibrium = (
            LATTICE_WEIGHTS[direction]
            * density
            * (1.0 + 3.0 * along + 4.5 * along * along - 1.5 * speed_sq)
        )
        relaxed.append(planes[direction] - OMEGA * (planes[direction] - equilibrium))
    return relaxed


def shift_x(plane, step, edge, xi, width_x):
    if step == 1:
        return jnp.where(xi == 0, edge, pltpu.roll(plane, 1, 0))
    if step == -1:
        return jnp.where(xi == width_x - 1, edge, pltpu.roll(plane, width_x - 1, 0))
    return plane


def shift_plane(plane, step_x, step_y, row, column, corner, xi, yi, width_x, width_y):
    moved = shift_x(plane, step_x, row, xi, width_x)
    if step_y == 0:
        return moved
    edge = shift_x(column, step_x, corner, xi, width_x)
    if step_y == 1:
        return jnp.where(yi == 0, edge, pltpu.roll(moved, 1, 1))
    return jnp.where(yi == width_y - 1, edge, pltpu.roll(moved, width_y - 1, 1))


def lbm_kernel(
    pop_ref, solid_ref, xlo_ref, xhi_ref, ylo_ref, yhi_ref,
    new_ref, mom_ref, rel_ref,
):
    _, depth, width_x, width_y = pop_ref.shape
    shape = (width_x, width_y)
    xi = lax.broadcasted_iota(jnp.int32, shape, 0)
    yi = lax.broadcasted_iota(jnp.int32, shape, 1)
    for level in range(depth):
        relaxed = collide_list([pop_ref[d, level] for d in range(19)])
        for d in range(19):
            rel_ref[d, level] = relaxed[d]

    def halo(ref):
        values = [ref[d] for d in range(20)]
        return collide_list(values[:19]), values[19]

    xlo, xlo_f = halo(xlo_ref)
    xhi, xhi_f = halo(xhi_ref)
    ylo, ylo_f = halo(ylo_ref)
    yhi, yhi_f = halo(yhi_ref)

    def pieces(step_x, step_y, level, direction):
        if direction is None:
            x_lo, x_hi, y_lo, y_hi = xlo_f, xhi_f, ylo_f, yhi_f
        else:
            x_lo, x_hi, y_lo, y_hi = xlo[direction], xhi[direction], ylo[direction], yhi[direction]
        row = x_lo[level] if step_x == 1 else x_hi[level]
        widened = y_lo[level] if step_y == 1 else y_hi[level]
        column = widened[1 : width_x + 1]
        corner = widened[:1] if step_x == 1 else widened[width_x + 1 :]
        row = jnp.broadcast_to(row, shape)
        column = jnp.broadcast_to(column, shape)
        corner = jnp.broadcast_to(corner, shape)
        return row, column, corner

    for level in range(depth):
        solid = solid_ref[level] == 1
        momentum = jnp.zeros(shape, jnp.float32)
        for d in range(19):
            step_x, step_y, step_z = (int(v) for v in DIRECTIONS[d])
            source_level = level - step_z
            kept = pop_ref[d, level]
            bounced = rel_ref[OPPOSITE[d], level]
            if 0 <= source_level < depth:
                row, column, corner = pieces(step_x, step_y, source_level, d)
                source = shift_plane(
                    rel_ref[d, source_level], step_x, step_y, row, column, corner,
                    xi, yi, width_x, width_y,
                )
                frow, fcolumn, fcorner = pieces(step_x, step_y, source_level, None)
                fluid = 1.0 - solid_ref[source_level].astype(jnp.float32)
                open_source = shift_plane(
                    fluid, step_x, step_y, frow, fcolumn, fcorner,
                    xi, yi, width_x, width_y,
                )
                pulled = jnp.where(open_source > 0.5, source, bounced)
            else:
                pulled = bounced
            value = jnp.where(solid, kept, pulled)
            new_ref[d, level] = value
            if step_x != 0:
                momentum = momentum + float(step_x) * value
        mom_ref[level] = momentum


def lbm_step(populations, solid_flag, halos, interpret=False):
    depth, width_x, width_y = solid_flag.shape
    return pl.pallas_call(
        lbm_kernel,
        out_shape=(
            jax.ShapeDtypeStruct(populations.shape, jnp.float32),
            jax.ShapeDtypeStruct(solid_flag.shape, jnp.float32),
        ),
        scratch_shapes=[pltpu.VMEM(populations.shape, jnp.float32)],
        interpret=interpret,
    )(populations, solid_flag, *halos)


def solution(mesh):
    placed = (
        P(None, None, "gx", "gy"),
        P(None, "gx", "gy"),
        P(None, "gx", "gy"),
        P(("gx", "gy")),
        P(("gx", "gy")),
        P(("gx", "gy")),
        P(None, ("gx", "gy")),
        P(None, ("gx", "gy")),
    )
    return jax.shard_map(
        on_device,
        mesh=mesh,
        in_specs=placed,
        out_specs=(P(None, None, "gx", "gy"), P(("gx", "gy")), P(("gx", "gy"))),
        check_vma=False,
    )
```

```python
import jax
import jax.numpy as jnp
import numpy as np
from jax import lax
from jax.experimental import pallas as pl
from jax.experimental.pallas import tpu as pltpu
from jax.sharding import PartitionSpec as P

DIRECTIONS = np.array(
    [
        [0, 0, 0],
        [1, 0, 0],
        [-1, 0, 0],
        [0, 1, 0],
        [0, -1, 0],
        [0, 0, 1],
        [0, 0, -1],
        [1, 1, 0],
        [-1, -1, 0],
        [1, -1, 0],
        [-1, 1, 0],
        [1, 0, 1],
        [-1, 0, -1],
        [1, 0, -1],
        [-1, 0, 1],
        [0, 1, 1],
        [0, -1, -1],
        [0, 1, -1],
        [0, -1, 1],
    ]
)
OPPOSITE = [0, 2, 1, 4, 3, 6, 5, 8, 7, 10, 9, 12, 11, 14, 13, 16, 15, 18, 17]
LATTICE_WEIGHTS = [1.0 / 3.0] + [1.0 / 18.0] * 6 + [1.0 / 36.0] * 12
OMEGA = 1.25
FACE_AREA = 0.25


def with_halo(cells, sides, width):
    for axis, dim in sides:
        count = lax.axis_size(axis)
        head = lax.slice_in_dim(cells, 0, width, axis=dim)
        tail = lax.slice_in_dim(cells, cells.shape[dim] - width, cells.shape[dim], axis=dim)
        cells = jnp.concatenate(
            [
                lax.ppermute(tail, axis, [(i, (i + 1) % count) for i in range(count)]),
                cells,
                lax.ppermute(head, axis, [((i + 1) % count, i) for i in range(count)]),
            ],
            axis=dim,
        )
    return cells


def moment(populations, component):
    total = jnp.zeros_like(populations[0])
    for direction in range(19):
        sign = int(DIRECTIONS[direction, component])
        if sign != 0:
            total = total + float(sign) * populations[direction]
    return total


def collide(populations):
    density = jnp.zeros_like(populations[0])
    for direction in range(19):
        density = density + populations[direction]
    velocity = [moment(populations, component) / density for component in range(3)]
    speed_sq = velocity[0] * velocity[0] + velocity[1] * velocity[1] + velocity[2] * velocity[2]
    relaxed = []
    for direction in range(19):
        along = jnp.zeros_like(density)
        for component in range(3):
            sign = int(DIRECTIONS[direction, component])
            if sign != 0:
                along = along + float(sign) * velocity[component]
        equilibrium = (
            LATTICE_WEIGHTS[direction]
            * density
            * (1.0 + 3.0 * along + 4.5 * along * along - 1.5 * speed_sq)
        )
        relaxed.append(populations[direction] - OMEGA * (populations[direction] - equilibrium))
    return jnp.stack(relaxed)


def stream(post_pad, flag_pad, relaxed, populations, solid_flag):
    depth, width_x, width_y = solid_flag.shape
    passed = []
    for direction in range(19):
        step_x = int(DIRECTIONS[direction, 0])
        step_y = int(DIRECTIONS[direction, 1])
        step_z = int(DIRECTIONS[direction, 2])
        source = post_pad[
            direction,
            1 - step_z : 1 - step_z + depth,
            1 - step_x : 1 - step_x + width_x,
            1 - step_y : 1 - step_y + width_y,
        ]
        open_source = flag_pad[
            1 - step_z : 1 - step_z + depth,
            1 - step_x : 1 - step_x + width_x,
            1 - step_y : 1 - step_y + width_y,
        ]
        pulled = open_source * source + (1.0 - open_source) * relaxed[OPPOSITE[direction]]
        passed.append(jnp.where(solid_flag == 1, populations[direction], pulled))
    return jnp.stack(passed)


def relax(inflow, old_pressure, leakage, conductance, neighbour):
    coupled = jnp.zeros_like(inflow)
    total = leakage
    for link in range(conductance.shape[0]):
        coupled = coupled + conductance[link] * old_pressure[neighbour[link]]
        total = total + conductance[link]
    return (inflow + coupled) / total


def relaxed_face(face):
    return jnp.stack(collide_list([face[d] for d in range(19)]))


def exchange_halos(populations, fluid):
    count_x = lax.axis_size("gx")
    count_y = lax.axis_size("gy")
    faces_x = [
        jnp.concatenate([relaxed_face(populations[:, :, at, None, :]), fluid[None, :, at, None, :]], axis=0)
        for at in (0, -1)
    ]
    x_low = lax.ppermute(faces_x[1], "gx", [(i, (i + 1) % count_x) for i in range(count_x)])
    x_high = lax.ppermute(faces_x[0], "gx", [((i + 1) % count_x, i) for i in range(count_x)])
    faces_y = [
        jnp.concatenate(
            [
                x_low[:, :, :, at, None],
                jnp.concatenate(
                    [relaxed_face(populations[:, :, :, at, None]), fluid[None, :, :, at, None]], axis=0
                ),
                x_high[:, :, :, at, None],
            ],
            axis=2,
        )
        for at in (0, -1)
    ]
    y_low = lax.ppermute(faces_y[1], "gy", [(j, j + 1) for j in range(count_y - 1)])
    y_high = lax.ppermute(faces_y[0], "gy", [(j + 1, j) for j in range(count_y - 1)])
    return (x_low, x_high, y_low, y_high)


def on_device(
    populations, solid_flag, cell_patch, patch_zone, old_pressure, leakage, conductance, neighbour
):
    fluid = (1 - solid_flag).astype(jnp.float32)
    halos = exchange_halos(populations, fluid)
    new_populations, momentum_x = lbm_step(populations, solid_flag, halos)
    patch_flux = patch_sums(momentum_x, cell_patch, patch_zone.shape[0])
    zone_dev = old_pressure.shape[0]
    openings = patch_zone.shape[0]
    devices = lax.axis_size("gx") * lax.axis_size("gy")
    capacity = max(2, (2 * openings + devices - 1) // devices)
    owner_block = patch_zone // zone_dev
    local_zone = patch_zone - owner_block * zone_dev
    patch_order = jnp.arange(openings, dtype=jnp.int32)
    earlier_same = (owner_block[:, None] == owner_block[None, :]) & (
        patch_order[:, None] > patch_order[None, :]
    )
    slot_rank = jnp.sum(earlier_same.astype(jnp.int32), axis=1)
    slot_index = owner_block * capacity + slot_rank
    targets = jnp.arange(devices * capacity, dtype=jnp.int32)
    placed = slot_index[:, None] == targets[None, :]
    send_flux = jnp.sum(jnp.where(placed, patch_flux[:, None], 0.0), axis=0)
    send_zone = jnp.sum(jnp.where(placed, local_zone.astype(jnp.float32)[:, None], 0.0), axis=0)
    count_x = lax.axis_size("gx")
    count_y = lax.axis_size("gy")
    outgoing = jnp.stack([send_flux, send_zone]).reshape(2, count_x, count_y * capacity)
    arrived = lax.all_to_all(outgoing, "gx", split_axis=1, concat_axis=1, tiled=True)
    arrived = arrived.reshape(2, count_x, count_y, capacity)
    zones = jnp.arange(zone_dev, dtype=jnp.float32)
    matched = arrived[1][..., None] == zones
    gathered = jnp.sum(jnp.where(matched, arrived[0][..., None], 0.0), axis=(0, 2))
    coupled, total = couple(old_pressure, leakage, conductance, neighbour)
    column = lax.axis_index("gy")
    is_own = (jnp.arange(count_y, dtype=jnp.int32) == column)[:, None]
    numer = gathered + jnp.where(is_own, coupled[None, :], 0.0)
    denom = jnp.where(is_own, total[None, :], 0.0)
    summed = row_sum(jnp.stack([numer, denom]), "gy", count_y)
    row_pressure = summed[0] / summed[1]
    zone_pressure = lax.dynamic_index_in_dim(row_pressure, column, axis=0, keepdims=False)
    answered = jnp.sum(jnp.where(matched, row_pressure[None, :, None, :], 0.0), axis=3)
    returned = lax.all_to_all(
        answered.reshape(count_x, count_y * capacity), "gx", split_axis=0, concat_axis=0, tiled=True
    ).reshape(-1)
    opening_pressure = jnp.sum(jnp.where(placed, returned[None, :], 0.0), axis=1)
    return (new_populations, zone_pressure, opening_pressure)


def row_sum(values, axis, count):
    if count & (count - 1):
        return lax.psum(values, axis)
    step = count // 2
    while step:
        values = values + lax.ppermute(values, axis, [(j, j ^ step) for j in range(count)])
        step //= 2
    return values


def patch_sums(momentum_x, cell_patch, openings):
    depth, width_x, width_y = cell_patch.shape
    rows = depth * width_x
    momentum = momentum_x.reshape(rows, width_y)
    patch = cell_patch.reshape(rows, width_y)
    lanes = 128
    high = patch // lanes
    low = patch - high * lanes
    groups = openings // lanes
    upper = lax.reduce_precision(momentum, exponent_bits=8, mantissa_bits=7)
    rest = momentum - upper
    middle = lax.reduce_precision(rest, exponent_bits=8, mantissa_bits=7)
    lower = rest - middle
    parts = jnp.stack([upper, middle, lower])
    picked = jnp.where(
        high[None, None] == jnp.arange(groups, dtype=jnp.int32)[None, :, None, None],
        parts[:, None],
        0.0,
    ).astype(jnp.bfloat16)
    onehot = (low[:, :, None] == jnp.arange(lanes, dtype=jnp.int32)[None, None, :]).astype(
        jnp.bfloat16
    )
    sums = jnp.einsum("khry,ryl->khl", picked, onehot, preferred_element_type=jnp.float32)
    return FACE_AREA * (sums[0] + sums[1] + sums[2]).reshape(openings)


def couple(old_pressure, leakage, conductance, neighbour):
    zone_dev = old_pressure.shape[0]
    chosen = neighbour[:, :, None] == jnp.arange(zone_dev, dtype=jnp.int32)[None, None, :]
    neighbour_pressure = jnp.sum(jnp.where(chosen, old_pressure[None, None, :], 0.0), axis=2)
    coupled = jnp.zeros_like(old_pressure)
    total = leakage
    for link in range(conductance.shape[0]):
        coupled = coupled + conductance[link] * neighbour_pressure[link]
        total = total + conductance[link]
    return coupled, total


def collide_list(planes):
    density = jnp.zeros_like(planes[0])
    for direction in range(19):
        density = density + planes[direction]
    velocity = []
    for component in range(3):
        total = jnp.zeros_like(planes[0])
        for direction in range(19):
            sign = int(DIRECTIONS[direction, component])
            if sign != 0:
                total = total + float(sign) * planes[direction]
        velocity.append(total / density)
    speed_sq = velocity[0] * velocity[0] + velocity[1] * velocity[1] + velocity[2] * velocity[2]
    relaxed = []
    for direction in range(19):
        along = jnp.zeros_like(density)
        for component in range(3):
            sign = int(DIRECTIONS[direction, component])
            if sign != 0:
                along = along + float(sign) * velocity[component]
        equilibrium = (
            LATTICE_WEIGHTS[direction]
            * density
            * (1.0 + 3.0 * along + 4.5 * along * along - 1.5 * speed_sq)
        )
        relaxed.append(planes[direction] - OMEGA * (planes[direction] - equilibrium))
    return relaxed


def shift_x(plane, step, edge, xi, width_x):
    if step == 1:
        return jnp.where(xi == 0, edge, pltpu.roll(plane, 1, 0))
    if step == -1:
        return jnp.where(xi == width_x - 1, edge, pltpu.roll(plane, width_x - 1, 0))
    return plane


def shift_plane(plane, step_x, step_y, row, column, corner, xi, yi, width_x, width_y):
    moved = shift_x(plane, step_x, row, xi, width_x)
    if step_y == 0:
        return moved
    edge = shift_x(column, step_x, corner, xi, width_x)
    if step_y == 1:
        return jnp.where(yi == 0, edge, pltpu.roll(moved, 1, 1))
    return jnp.where(yi == width_y - 1, edge, pltpu.roll(moved, width_y - 1, 1))


def lbm_kernel(
    pop_ref, solid_ref, xlo_ref, xhi_ref, ylo_ref, yhi_ref,
    new_ref, mom_ref, rel_ref,
):
    _, depth, width_x, width_y = pop_ref.shape
    shape = (width_x, width_y)
    xi = lax.broadcasted_iota(jnp.int32, shape, 0)
    yi = lax.broadcasted_iota(jnp.int32, shape, 1)
    for level in range(depth):
        relaxed = collide_list([pop_ref[d, level] for d in range(19)])
        for d in range(19):
            rel_ref[d, level] = relaxed[d]

    def halo(ref):
        values = [ref[d] for d in range(20)]
        return values[:19], values[19]

    xlo, xlo_f = halo(xlo_ref)
    xhi, xhi_f = halo(xhi_ref)
    ylo, ylo_f = halo(ylo_ref)
    yhi, yhi_f = halo(yhi_ref)

    def pieces(step_x, step_y, level, direction):
        if direction is None:
            x_lo, x_hi, y_lo, y_hi = xlo_f, xhi_f, ylo_f, yhi_f
        else:
            x_lo, x_hi, y_lo, y_hi = xlo[direction], xhi[direction], ylo[direction], yhi[direction]
        row = x_lo[level] if step_x == 1 else x_hi[level]
        widened = y_lo[level] if step_y == 1 else y_hi[level]
        column = widened[1 : width_x + 1]
        corner = widened[:1] if step_x == 1 else widened[width_x + 1 :]
        row = jnp.broadcast_to(row, shape)
        column = jnp.broadcast_to(column, shape)
        corner = jnp.broadcast_to(corner, shape)
        return row, column, corner

    for level in range(depth):
        solid = solid_ref[level] == 1
        momentum = jnp.zeros(shape, jnp.float32)
        for d in range(19):
            step_x, step_y, step_z = (int(v) for v in DIRECTIONS[d])
            source_level = level - step_z
            kept = pop_ref[d, level]
            bounced = rel_ref[OPPOSITE[d], level]
            if 0 <= source_level < depth:
                row, column, corner = pieces(step_x, step_y, source_level, d)
                source = shift_plane(
                    rel_ref[d, source_level], step_x, step_y, row, column, corner,
                    xi, yi, width_x, width_y,
                )
                frow, fcolumn, fcorner = pieces(step_x, step_y, source_level, None)
                fluid = 1.0 - solid_ref[source_level].astype(jnp.float32)
                open_source = shift_plane(
                    fluid, step_x, step_y, frow, fcolumn, fcorner,
                    xi, yi, width_x, width_y,
                )
                pulled = jnp.where(open_source > 0.5, source, bounced)
            else:
                pulled = bounced
            value = jnp.where(solid, kept, pulled)
            new_ref[d, level] = value
            if step_x != 0:
                momentum = momentum + float(step_x) * value
        mom_ref[level] = momentum


def lbm_step(populations, solid_flag, halos, interpret=False):
    depth, width_x, width_y = solid_flag.shape
    return pl.pallas_call(
        lbm_kernel,
        out_shape=(
            jax.ShapeDtypeStruct(populations.shape, jnp.float32),
            jax.ShapeDtypeStruct(solid_flag.shape, jnp.float32),
        ),
        scratch_shapes=[pltpu.VMEM(populations.shape, jnp.float32)],
        interpret=interpret,
    )(populations, solid_flag, *halos)


def solution(mesh):
    placed = (
        P(None, None, "gx", "gy"),
        P(None, "gx", "gy"),
        P(None, "gx", "gy"),
        P(("gx", "gy")),
        P(("gx", "gy")),
        P(("gx", "gy")),
        P(None, ("gx", "gy")),
        P(None, ("gx", "gy")),
    )
    return jax.shard_map(
        on_device,
        mesh=mesh,
        in_specs=placed,
        out_specs=(P(None, None, "gx", "gy"), P(("gx", "gy")), P(("gx", "gy"))),
        check_vma=False,
    )
```

```python
import jax
import jax.numpy as jnp
import numpy as np
from jax import lax
from jax.experimental import pallas as pl
from jax.experimental.pallas import tpu as pltpu
from jax.sharding import PartitionSpec as P

DIRECTIONS = np.array(
    [
        [0, 0, 0],
        [1, 0, 0],
        [-1, 0, 0],
        [0, 1, 0],
        [0, -1, 0],
        [0, 0, 1],
        [0, 0, -1],
        [1, 1, 0],
        [-1, -1, 0],
        [1, -1, 0],
        [-1, 1, 0],
        [1, 0, 1],
        [-1, 0, -1],
        [1, 0, -1],
        [-1, 0, 1],
        [0, 1, 1],
        [0, -1, -1],
        [0, 1, -1],
        [0, -1, 1],
    ]
)
OPPOSITE = [0, 2, 1, 4, 3, 6, 5, 8, 7, 10, 9, 12, 11, 14, 13, 16, 15, 18, 17]
LATTICE_WEIGHTS = [1.0 / 3.0] + [1.0 / 18.0] * 6 + [1.0 / 36.0] * 12
OMEGA = 1.25
FACE_AREA = 0.25


def with_halo(cells, sides, width):
    for axis, dim in sides:
        count = lax.axis_size(axis)
        head = lax.slice_in_dim(cells, 0, width, axis=dim)
        tail = lax.slice_in_dim(cells, cells.shape[dim] - width, cells.shape[dim], axis=dim)
        cells = jnp.concatenate(
            [
                lax.ppermute(tail, axis, [(i, (i + 1) % count) for i in range(count)]),
                cells,
                lax.ppermute(head, axis, [((i + 1) % count, i) for i in range(count)]),
            ],
            axis=dim,
        )
    return cells


def moment(populations, component):
    total = jnp.zeros_like(populations[0])
    for direction in range(19):
        sign = int(DIRECTIONS[direction, component])
        if sign != 0:
            total = total + float(sign) * populations[direction]
    return total


def collide(populations):
    density = jnp.zeros_like(populations[0])
    for direction in range(19):
        density = density + populations[direction]
    velocity = [moment(populations, component) / density for component in range(3)]
    speed_sq = velocity[0] * velocity[0] + velocity[1] * velocity[1] + velocity[2] * velocity[2]
    relaxed = []
    for direction in range(19):
        along = jnp.zeros_like(density)
        for component in range(3):
            sign = int(DIRECTIONS[direction, component])
            if sign != 0:
                along = along + float(sign) * velocity[component]
        equilibrium = (
            LATTICE_WEIGHTS[direction]
            * density
            * (1.0 + 3.0 * along + 4.5 * along * along - 1.5 * speed_sq)
        )
        relaxed.append(populations[direction] - OMEGA * (populations[direction] - equilibrium))
    return jnp.stack(relaxed)


def stream(post_pad, flag_pad, relaxed, populations, solid_flag):
    depth, width_x, width_y = solid_flag.shape
    passed = []
    for direction in range(19):
        step_x = int(DIRECTIONS[direction, 0])
        step_y = int(DIRECTIONS[direction, 1])
        step_z = int(DIRECTIONS[direction, 2])
        source = post_pad[
            direction,
            1 - step_z : 1 - step_z + depth,
            1 - step_x : 1 - step_x + width_x,
            1 - step_y : 1 - step_y + width_y,
        ]
        open_source = flag_pad[
            1 - step_z : 1 - step_z + depth,
            1 - step_x : 1 - step_x + width_x,
            1 - step_y : 1 - step_y + width_y,
        ]
        pulled = open_source * source + (1.0 - open_source) * relaxed[OPPOSITE[direction]]
        passed.append(jnp.where(solid_flag == 1, populations[direction], pulled))
    return jnp.stack(passed)


def relax(inflow, old_pressure, leakage, conductance, neighbour):
    coupled = jnp.zeros_like(inflow)
    total = leakage
    for link in range(conductance.shape[0]):
        coupled = coupled + conductance[link] * old_pressure[neighbour[link]]
        total = total + conductance[link]
    return (inflow + coupled) / total


def relaxed_face(face):
    shape = (19,) + (1,) * (face.ndim - 1)
    weights = jnp.asarray(np.array(LATTICE_WEIGHTS, np.float32).reshape(shape))
    steps = [jnp.asarray(DIRECTIONS[:, k].astype(np.float32).reshape(shape)) for k in range(3)]
    density = jnp.sum(face, axis=0, keepdims=True)
    velocity = [jnp.sum(step * face, axis=0, keepdims=True) / density for step in steps]
    speed_sq = velocity[0] * velocity[0] + velocity[1] * velocity[1] + velocity[2] * velocity[2]
    along = steps[0] * velocity[0] + steps[1] * velocity[1] + steps[2] * velocity[2]
    equilibrium = weights * density * (1.0 + 3.0 * along + 4.5 * along * along - 1.5 * speed_sq)
    return face - OMEGA * (face - equilibrium)


def exchange_halos(populations, fluid):
    count_x = lax.axis_size("gx")
    count_y = lax.axis_size("gy")
    faces_x = [
        jnp.concatenate([relaxed_face(populations[:, :, at, None, :]), fluid[None, :, at, None, :]], axis=0)
        for at in (0, -1)
    ]
    x_low = lax.ppermute(faces_x[1], "gx", [(i, (i + 1) % count_x) for i in range(count_x)])
    x_high = lax.ppermute(faces_x[0], "gx", [((i + 1) % count_x, i) for i in range(count_x)])
    faces_y = [
        jnp.concatenate(
            [
                x_low[:, :, :, at, None],
                jnp.concatenate(
                    [relaxed_face(populations[:, :, :, at, None]), fluid[None, :, :, at, None]], axis=0
                ),
                x_high[:, :, :, at, None],
            ],
            axis=2,
        )
        for at in (0, -1)
    ]
    y_low = lax.ppermute(faces_y[1], "gy", [(j, j + 1) for j in range(count_y - 1)])
    y_high = lax.ppermute(faces_y[0], "gy", [(j + 1, j) for j in range(count_y - 1)])
    return (x_low, x_high, y_low, y_high)


def on_device(
    populations, solid_flag, cell_patch, patch_zone, old_pressure, leakage, conductance, neighbour
):
    fluid = (1 - solid_flag).astype(jnp.float32)
    halos = exchange_halos(populations, fluid)
    new_populations, momentum_x = lbm_step(populations, solid_flag, halos)
    patch_flux = patch_sums(momentum_x, cell_patch, patch_zone.shape[0])
    zone_dev = old_pressure.shape[0]
    openings = patch_zone.shape[0]
    devices = lax.axis_size("gx") * lax.axis_size("gy")
    capacity = max(2, (2 * openings + devices - 1) // devices)
    owner_block = patch_zone // zone_dev
    local_zone = patch_zone - owner_block * zone_dev
    patch_order = jnp.arange(openings, dtype=jnp.int32)
    earlier_same = (owner_block[:, None] == owner_block[None, :]) & (
        patch_order[:, None] > patch_order[None, :]
    )
    slot_rank = jnp.sum(earlier_same.astype(jnp.int32), axis=1)
    slot_index = owner_block * capacity + slot_rank
    targets = jnp.arange(devices * capacity, dtype=jnp.int32)
    placed = slot_index[:, None] == targets[None, :]
    send_flux = jnp.sum(jnp.where(placed, patch_flux[:, None], 0.0), axis=0)
    send_zone = jnp.sum(jnp.where(placed, local_zone.astype(jnp.float32)[:, None], 0.0), axis=0)
    count_x = lax.axis_size("gx")
    count_y = lax.axis_size("gy")
    outgoing = jnp.stack([send_flux, send_zone]).reshape(2, count_x, count_y * capacity)
    arrived = lax.all_to_all(outgoing, "gx", split_axis=1, concat_axis=1, tiled=True)
    arrived = arrived.reshape(2, count_x, count_y, capacity)
    zones = jnp.arange(zone_dev, dtype=jnp.float32)
    matched = arrived[1][..., None] == zones
    gathered = jnp.sum(jnp.where(matched, arrived[0][..., None], 0.0), axis=(0, 2))
    coupled, total = couple(old_pressure, leakage, conductance, neighbour)
    column = lax.axis_index("gy")
    is_own = (jnp.arange(count_y, dtype=jnp.int32) == column)[:, None]
    numer = gathered + jnp.where(is_own, coupled[None, :], 0.0)
    denom = jnp.where(is_own, total[None, :], 0.0)
    summed = row_sum(jnp.stack([numer, denom]), "gy", count_y)
    row_pressure = summed[0] / summed[1]
    zone_pressure = lax.dynamic_index_in_dim(row_pressure, column, axis=0, keepdims=False)
    answered = jnp.sum(jnp.where(matched, row_pressure[None, :, None, :], 0.0), axis=3)
    returned = lax.all_to_all(
        answered.reshape(count_x, count_y * capacity), "gx", split_axis=0, concat_axis=0, tiled=True
    ).reshape(-1)
    opening_pressure = jnp.sum(jnp.where(placed, returned[None, :], 0.0), axis=1)
    return (new_populations, zone_pressure, opening_pressure)


def row_sum(values, axis, count):
    if count & (count - 1):
        return lax.psum(values, axis)
    step = count // 2
    while step:
        values = values + lax.ppermute(values, axis, [(j, j ^ step) for j in range(count)])
        step //= 2
    return values


def patch_sums(momentum_x, cell_patch, openings):
    depth, width_x, width_y = cell_patch.shape
    rows = depth * width_x
    momentum = momentum_x.reshape(rows, width_y)
    patch = cell_patch.reshape(rows, width_y)
    lanes = 128
    high = patch // lanes
    low = patch - high * lanes
    groups = openings // lanes
    upper = lax.reduce_precision(momentum, exponent_bits=8, mantissa_bits=7)
    rest = momentum - upper
    middle = lax.reduce_precision(rest, exponent_bits=8, mantissa_bits=7)
    lower = rest - middle
    parts = jnp.stack([upper, middle, lower])
    picked = jnp.where(
        high[None, None] == jnp.arange(groups, dtype=jnp.int32)[None, :, None, None],
        parts[:, None],
        0.0,
    ).astype(jnp.bfloat16)
    onehot = (low[:, :, None] == jnp.arange(lanes, dtype=jnp.int32)[None, None, :]).astype(
        jnp.bfloat16
    )
    sums = jnp.einsum("khry,ryl->khl", picked, onehot, preferred_element_type=jnp.float32)
    return FACE_AREA * (sums[0] + sums[1] + sums[2]).reshape(openings)


def couple(old_pressure, leakage, conductance, neighbour):
    zone_dev = old_pressure.shape[0]
    chosen = neighbour[:, :, None] == jnp.arange(zone_dev, dtype=jnp.int32)[None, None, :]
    neighbour_pressure = jnp.sum(jnp.where(chosen, old_pressure[None, None, :], 0.0), axis=2)
    coupled = jnp.zeros_like(old_pressure)
    total = leakage
    for link in range(conductance.shape[0]):
        coupled = coupled + conductance[link] * neighbour_pressure[link]
        total = total + conductance[link]
    return coupled, total


def collide_list(planes):
    density = jnp.zeros_like(planes[0])
    for direction in range(19):
        density = density + planes[direction]
    velocity = []
    for component in range(3):
        total = jnp.zeros_like(planes[0])
        for direction in range(19):
            sign = int(DIRECTIONS[direction, component])
            if sign != 0:
                total = total + float(sign) * planes[direction]
        velocity.append(total / density)
    speed_sq = velocity[0] * velocity[0] + velocity[1] * velocity[1] + velocity[2] * velocity[2]
    relaxed = []
    for direction in range(19):
        along = jnp.zeros_like(density)
        for component in range(3):
            sign = int(DIRECTIONS[direction, component])
            if sign != 0:
                along = along + float(sign) * velocity[component]
        equilibrium = (
            LATTICE_WEIGHTS[direction]
            * density
            * (1.0 + 3.0 * along + 4.5 * along * along - 1.5 * speed_sq)
        )
        relaxed.append(planes[direction] - OMEGA * (planes[direction] - equilibrium))
    return relaxed


def shift_x(plane, step, edge, xi, width_x):
    if step == 1:
        return jnp.where(xi == 0, edge, pltpu.roll(plane, 1, 0))
    if step == -1:
        return jnp.where(xi == width_x - 1, edge, pltpu.roll(plane, width_x - 1, 0))
    return plane


def shift_plane(plane, step_x, step_y, row, column, corner, xi, yi, width_x, width_y):
    moved = shift_x(plane, step_x, row, xi, width_x)
    if step_y == 0:
        return moved
    edge = shift_x(column, step_x, corner, xi, width_x)
    if step_y == 1:
        return jnp.where(yi == 0, edge, pltpu.roll(moved, 1, 1))
    return jnp.where(yi == width_y - 1, edge, pltpu.roll(moved, width_y - 1, 1))


def lbm_kernel(
    pop_ref, solid_ref, xlo_ref, xhi_ref, ylo_ref, yhi_ref,
    new_ref, mom_ref, rel_ref,
):
    _, depth, width_x, width_y = pop_ref.shape
    shape = (width_x, width_y)
    xi = lax.broadcasted_iota(jnp.int32, shape, 0)
    yi = lax.broadcasted_iota(jnp.int32, shape, 1)
    for level in range(depth):
        relaxed = collide_list([pop_ref[d, level] for d in range(19)])
        for d in range(19):
            rel_ref[d, level] = relaxed[d]

    def halo(ref):
        values = [ref[d] for d in range(20)]
        return values[:19], values[19]

    xlo, xlo_f = halo(xlo_ref)
    xhi, xhi_f = halo(xhi_ref)
    ylo, ylo_f = halo(ylo_ref)
    yhi, yhi_f = halo(yhi_ref)

    def pieces(step_x, step_y, level, direction):
        if direction is None:
            x_lo, x_hi, y_lo, y_hi = xlo_f, xhi_f, ylo_f, yhi_f
        else:
            x_lo, x_hi, y_lo, y_hi = xlo[direction], xhi[direction], ylo[direction], yhi[direction]
        row = x_lo[level] if step_x == 1 else x_hi[level]
        widened = y_lo[level] if step_y == 1 else y_hi[level]
        column = widened[1 : width_x + 1]
        corner = widened[:1] if step_x == 1 else widened[width_x + 1 :]
        row = jnp.broadcast_to(row, shape)
        column = jnp.broadcast_to(column, shape)
        corner = jnp.broadcast_to(corner, shape)
        return row, column, corner

    for level in range(depth):
        solid = solid_ref[level] == 1
        momentum = jnp.zeros(shape, jnp.float32)
        for d in range(19):
            step_x, step_y, step_z = (int(v) for v in DIRECTIONS[d])
            source_level = level - step_z
            kept = pop_ref[d, level]
            bounced = rel_ref[OPPOSITE[d], level]
            if 0 <= source_level < depth:
                row, column, corner = pieces(step_x, step_y, source_level, d)
                source = shift_plane(
                    rel_ref[d, source_level], step_x, step_y, row, column, corner,
                    xi, yi, width_x, width_y,
                )
                frow, fcolumn, fcorner = pieces(step_x, step_y, source_level, None)
                fluid = 1.0 - solid_ref[source_level].astype(jnp.float32)
                open_source = shift_plane(
                    fluid, step_x, step_y, frow, fcolumn, fcorner,
                    xi, yi, width_x, width_y,
                )
                pulled = jnp.where(open_source > 0.5, source, bounced)
            else:
                pulled = bounced
            value = jnp.where(solid, kept, pulled)
            new_ref[d, level] = value
            if step_x != 0:
                momentum = momentum + float(step_x) * value
        mom_ref[level] = momentum


def lbm_step(populations, solid_flag, halos, interpret=False):
    depth, width_x, width_y = solid_flag.shape
    return pl.pallas_call(
        lbm_kernel,
        out_shape=(
            jax.ShapeDtypeStruct(populations.shape, jnp.float32),
            jax.ShapeDtypeStruct(solid_flag.shape, jnp.float32),
        ),
        scratch_shapes=[pltpu.VMEM(populations.shape, jnp.float32)],
        interpret=interpret,
    )(populations, solid_flag, *halos)


def solution(mesh):
    placed = (
        P(None, None, "gx", "gy"),
        P(None, "gx", "gy"),
        P(None, "gx", "gy"),
        P(("gx", "gy")),
        P(("gx", "gy")),
        P(("gx", "gy")),
        P(None, ("gx", "gy")),
        P(None, ("gx", "gy")),
    )
    return jax.shard_map(
        on_device,
        mesh=mesh,
        in_specs=placed,
        out_specs=(P(None, None, "gx", "gy"), P(("gx", "gy")), P(("gx", "gy"))),
        check_vma=False,
    )
```

```python
import jax
import jax.numpy as jnp
import numpy as np
from jax import lax
from jax.experimental import pallas as pl
from jax.experimental.pallas import tpu as pltpu
from jax.sharding import PartitionSpec as P

DIRECTIONS = np.array(
    [
        [0, 0, 0],
        [1, 0, 0],
        [-1, 0, 0],
        [0, 1, 0],
        [0, -1, 0],
        [0, 0, 1],
        [0, 0, -1],
        [1, 1, 0],
        [-1, -1, 0],
        [1, -1, 0],
        [-1, 1, 0],
        [1, 0, 1],
        [-1, 0, -1],
        [1, 0, -1],
        [-1, 0, 1],
        [0, 1, 1],
        [0, -1, -1],
        [0, 1, -1],
        [0, -1, 1],
    ]
)
OPPOSITE = [0, 2, 1, 4, 3, 6, 5, 8, 7, 10, 9, 12, 11, 14, 13, 16, 15, 18, 17]
LATTICE_WEIGHTS = [1.0 / 3.0] + [1.0 / 18.0] * 6 + [1.0 / 36.0] * 12
OMEGA = 1.25
FACE_AREA = 0.25


def with_halo(cells, sides, width):
    for axis, dim in sides:
        count = lax.axis_size(axis)
        head = lax.slice_in_dim(cells, 0, width, axis=dim)
        tail = lax.slice_in_dim(cells, cells.shape[dim] - width, cells.shape[dim], axis=dim)
        cells = jnp.concatenate(
            [
                lax.ppermute(tail, axis, [(i, (i + 1) % count) for i in range(count)]),
                cells,
                lax.ppermute(head, axis, [((i + 1) % count, i) for i in range(count)]),
            ],
            axis=dim,
        )
    return cells


def moment(populations, component):
    total = jnp.zeros_like(populations[0])
    for direction in range(19):
        sign = int(DIRECTIONS[direction, component])
        if sign != 0:
            total = total + float(sign) * populations[direction]
    return total


def collide(populations):
    density = jnp.zeros_like(populations[0])
    for direction in range(19):
        density = density + populations[direction]
    velocity = [moment(populations, component) / density for component in range(3)]
    speed_sq = velocity[0] * velocity[0] + velocity[1] * velocity[1] + velocity[2] * velocity[2]
    relaxed = []
    for direction in range(19):
        along = jnp.zeros_like(density)
        for component in range(3):
            sign = int(DIRECTIONS[direction, component])
            if sign != 0:
                along = along + float(sign) * velocity[component]
        equilibrium = (
            LATTICE_WEIGHTS[direction]
            * density
            * (1.0 + 3.0 * along + 4.5 * along * along - 1.5 * speed_sq)
        )
        relaxed.append(populations[direction] - OMEGA * (populations[direction] - equilibrium))
    return jnp.stack(relaxed)


def stream(post_pad, flag_pad, relaxed, populations, solid_flag):
    depth, width_x, width_y = solid_flag.shape
    passed = []
    for direction in range(19):
        step_x = int(DIRECTIONS[direction, 0])
        step_y = int(DIRECTIONS[direction, 1])
        step_z = int(DIRECTIONS[direction, 2])
        source = post_pad[
            direction,
            1 - step_z : 1 - step_z + depth,
            1 - step_x : 1 - step_x + width_x,
            1 - step_y : 1 - step_y + width_y,
        ]
        open_source = flag_pad[
            1 - step_z : 1 - step_z + depth,
            1 - step_x : 1 - step_x + width_x,
            1 - step_y : 1 - step_y + width_y,
        ]
        pulled = open_source * source + (1.0 - open_source) * relaxed[OPPOSITE[direction]]
        passed.append(jnp.where(solid_flag == 1, populations[direction], pulled))
    return jnp.stack(passed)


def relax(inflow, old_pressure, leakage, conductance, neighbour):
    coupled = jnp.zeros_like(inflow)
    total = leakage
    for link in range(conductance.shape[0]):
        coupled = coupled + conductance[link] * old_pressure[neighbour[link]]
        total = total + conductance[link]
    return (inflow + coupled) / total


def marked(face, solid):
    first = jnp.where(solid == 1, -face[0], face[0])
    return jnp.concatenate([first[None], face[1:]], axis=0)


def exchange_halos(populations, solid_flag):
    count_x = lax.axis_size("gx")
    count_y = lax.axis_size("gy")
    faces_x = [marked(populations[:, :, at, None, :], solid_flag[:, at, None, :]) for at in (0, -1)]
    x_low = lax.ppermute(faces_x[1], "gx", [(i, (i + 1) % count_x) for i in range(count_x)])
    x_high = lax.ppermute(faces_x[0], "gx", [((i + 1) % count_x, i) for i in range(count_x)])
    faces_y = [
        jnp.concatenate(
            [
                x_low[:, :, :, at, None],
                marked(populations[:, :, :, at, None], solid_flag[:, :, at, None]),
                x_high[:, :, :, at, None],
            ],
            axis=2,
        )
        for at in (0, -1)
    ]
    y_low = lax.ppermute(faces_y[1], "gy", [(j, j + 1) for j in range(count_y - 1)])
    y_high = lax.ppermute(faces_y[0], "gy", [(j + 1, j) for j in range(count_y - 1)])
    return (x_low, x_high, y_low, y_high)


def on_device(
    populations, solid_flag, cell_patch, patch_zone, old_pressure, leakage, conductance, neighbour
):
    halos = exchange_halos(populations, solid_flag)
    new_populations, momentum_x = lbm_step(populations, solid_flag, halos)
    patch_flux = patch_sums(momentum_x, cell_patch, patch_zone.shape[0])
    zone_dev = old_pressure.shape[0]
    openings = patch_zone.shape[0]
    devices = lax.axis_size("gx") * lax.axis_size("gy")
    capacity = max(2, (2 * openings + devices - 1) // devices)
    owner_block = patch_zone // zone_dev
    local_zone = patch_zone - owner_block * zone_dev
    patch_order = jnp.arange(openings, dtype=jnp.int32)
    earlier_same = (owner_block[:, None] == owner_block[None, :]) & (
        patch_order[:, None] > patch_order[None, :]
    )
    slot_rank = jnp.sum(earlier_same.astype(jnp.int32), axis=1)
    slot_index = owner_block * capacity + slot_rank
    targets = jnp.arange(devices * capacity, dtype=jnp.int32)
    placed = slot_index[:, None] == targets[None, :]
    send_flux = jnp.sum(jnp.where(placed, patch_flux[:, None], 0.0), axis=0)
    send_zone = jnp.sum(jnp.where(placed, local_zone.astype(jnp.float32)[:, None], 0.0), axis=0)
    count_x = lax.axis_size("gx")
    count_y = lax.axis_size("gy")
    outgoing = jnp.stack([send_flux, send_zone]).reshape(2, count_x, count_y * capacity)
    arrived = lax.all_to_all(outgoing, "gx", split_axis=1, concat_axis=1, tiled=True)
    arrived = arrived.reshape(2, count_x, count_y, capacity)
    zones = jnp.arange(zone_dev, dtype=jnp.float32)
    matched = arrived[1][..., None] == zones
    gathered = jnp.sum(jnp.where(matched, arrived[0][..., None], 0.0), axis=(0, 2))
    coupled, total = couple(old_pressure, leakage, conductance, neighbour)
    column = lax.axis_index("gy")
    is_own = (jnp.arange(count_y, dtype=jnp.int32) == column)[:, None]
    numer = gathered + jnp.where(is_own, coupled[None, :], 0.0)
    denom = jnp.where(is_own, total[None, :], 0.0)
    summed = row_sum(jnp.stack([numer, denom]), "gy", count_y)
    row_pressure = summed[0] / summed[1]
    zone_pressure = lax.dynamic_index_in_dim(row_pressure, column, axis=0, keepdims=False)
    answered = jnp.sum(jnp.where(matched, row_pressure[None, :, None, :], 0.0), axis=3)
    returned = lax.all_to_all(
        answered.reshape(count_x, count_y * capacity), "gx", split_axis=0, concat_axis=0, tiled=True
    ).reshape(-1)
    opening_pressure = jnp.sum(jnp.where(placed, returned[None, :], 0.0), axis=1)
    return (new_populations, zone_pressure, opening_pressure)


def row_sum(values, axis, count):
    if count & (count - 1):
        return lax.psum(values, axis)
    step = count // 2
    while step:
        values = values + lax.ppermute(values, axis, [(j, j ^ step) for j in range(count)])
        step //= 2
    return values


def patch_sums(momentum_x, cell_patch, openings):
    depth, width_x, width_y = cell_patch.shape
    rows = depth * width_x
    momentum = momentum_x.reshape(rows, width_y)
    patch = cell_patch.reshape(rows, width_y)
    lanes = 128
    high = patch // lanes
    low = patch - high * lanes
    groups = openings // lanes
    upper = lax.reduce_precision(momentum, exponent_bits=8, mantissa_bits=7)
    rest = momentum - upper
    middle = lax.reduce_precision(rest, exponent_bits=8, mantissa_bits=7)
    lower = rest - middle
    parts = jnp.stack([upper, middle, lower])
    picked = jnp.where(
        high[None, None] == jnp.arange(groups, dtype=jnp.int32)[None, :, None, None],
        parts[:, None],
        0.0,
    ).astype(jnp.bfloat16)
    onehot = (low[:, :, None] == jnp.arange(lanes, dtype=jnp.int32)[None, None, :]).astype(
        jnp.bfloat16
    )
    sums = jnp.einsum("khry,ryl->khl", picked, onehot, preferred_element_type=jnp.float32)
    return FACE_AREA * (sums[0] + sums[1] + sums[2]).reshape(openings)


def couple(old_pressure, leakage, conductance, neighbour):
    zone_dev = old_pressure.shape[0]
    chosen = neighbour[:, :, None] == jnp.arange(zone_dev, dtype=jnp.int32)[None, None, :]
    neighbour_pressure = jnp.sum(jnp.where(chosen, old_pressure[None, None, :], 0.0), axis=2)
    coupled = jnp.zeros_like(old_pressure)
    total = leakage
    for link in range(conductance.shape[0]):
        coupled = coupled + conductance[link] * neighbour_pressure[link]
        total = total + conductance[link]
    return coupled, total


def collide_list(planes):
    density = jnp.zeros_like(planes[0])
    for direction in range(19):
        density = density + planes[direction]
    velocity = []
    for component in range(3):
        total = jnp.zeros_like(planes[0])
        for direction in range(19):
            sign = int(DIRECTIONS[direction, component])
            if sign != 0:
                total = total + float(sign) * planes[direction]
        velocity.append(total / density)
    speed_sq = velocity[0] * velocity[0] + velocity[1] * velocity[1] + velocity[2] * velocity[2]
    relaxed = []
    for direction in range(19):
        along = jnp.zeros_like(density)
        for component in range(3):
            sign = int(DIRECTIONS[direction, component])
            if sign != 0:
                along = along + float(sign) * velocity[component]
        equilibrium = (
            LATTICE_WEIGHTS[direction]
            * density
            * (1.0 + 3.0 * along + 4.5 * along * along - 1.5 * speed_sq)
        )
        relaxed.append(planes[direction] - OMEGA * (planes[direction] - equilibrium))
    return relaxed


def shift_x(plane, step, edge, xi, width_x):
    if step == 1:
        return jnp.where(xi == 0, edge, pltpu.roll(plane, 1, 0))
    if step == -1:
        return jnp.where(xi == width_x - 1, edge, pltpu.roll(plane, width_x - 1, 0))
    return plane


def shift_plane(plane, step_x, step_y, row, column, corner, xi, yi, width_x, width_y):
    moved = shift_x(plane, step_x, row, xi, width_x)
    if step_y == 0:
        return moved
    edge = shift_x(column, step_x, corner, xi, width_x)
    if step_y == 1:
        return jnp.where(yi == 0, edge, pltpu.roll(moved, 1, 1))
    return jnp.where(yi == width_y - 1, edge, pltpu.roll(moved, width_y - 1, 1))


def lbm_kernel(
    pop_ref, solid_ref, xlo_ref, xhi_ref, ylo_ref, yhi_ref,
    new_ref, mom_ref, rel_ref,
):
    _, depth, width_x, width_y = pop_ref.shape
    shape = (width_x, width_y)
    xi = lax.broadcasted_iota(jnp.int32, shape, 0)
    yi = lax.broadcasted_iota(jnp.int32, shape, 1)
    for level in range(depth):
        relaxed = collide_list([pop_ref[d, level] for d in range(19)])
        for d in range(19):
            rel_ref[d, level] = relaxed[d]

    def halo(ref):
        values = [ref[d] for d in range(19)]
        fluid = (values[0] > 0.0).astype(jnp.float32)
        values[0] = jnp.abs(values[0])
        return collide_list(values), fluid

    xlo, xlo_f = halo(xlo_ref)
    xhi, xhi_f = halo(xhi_ref)
    ylo, ylo_f = halo(ylo_ref)
    yhi, yhi_f = halo(yhi_ref)

    def pieces(step_x, step_y, level, direction):
        if direction is None:
            x_lo, x_hi, y_lo, y_hi = xlo_f, xhi_f, ylo_f, yhi_f
        else:
            x_lo, x_hi, y_lo, y_hi = xlo[direction], xhi[direction], ylo[direction], yhi[direction]
        row = x_lo[level] if step_x == 1 else x_hi[level]
        widened = y_lo[level] if step_y == 1 else y_hi[level]
        column = widened[1 : width_x + 1]
        corner = widened[:1] if step_x == 1 else widened[width_x + 1 :]
        row = jnp.broadcast_to(row, shape)
        column = jnp.broadcast_to(column, shape)
        corner = jnp.broadcast_to(corner, shape)
        return row, column, corner

    for level in range(depth):
        solid = solid_ref[level] == 1
        momentum = jnp.zeros(shape, jnp.float32)
        for d in range(19):
            step_x, step_y, step_z = (int(v) for v in DIRECTIONS[d])
            source_level = level - step_z
            kept = pop_ref[d, level]
            bounced = rel_ref[OPPOSITE[d], level]
            if 0 <= source_level < depth:
                row, column, corner = pieces(step_x, step_y, source_level, d)
                source = shift_plane(
                    rel_ref[d, source_level], step_x, step_y, row, column, corner,
                    xi, yi, width_x, width_y,
                )
                frow, fcolumn, fcorner = pieces(step_x, step_y, source_level, None)
                fluid = 1.0 - solid_ref[source_level].astype(jnp.float32)
                open_source = shift_plane(
                    fluid, step_x, step_y, frow, fcolumn, fcorner,
                    xi, yi, width_x, width_y,
                )
                pulled = jnp.where(open_source > 0.5, source, bounced)
            else:
                pulled = bounced
            value = jnp.where(solid, kept, pulled)
            new_ref[d, level] = value
            if step_x != 0:
                momentum = momentum + float(step_x) * value
        mom_ref[level] = momentum


def lbm_step(populations, solid_flag, halos, interpret=False):
    depth, width_x, width_y = solid_flag.shape
    return pl.pallas_call(
        lbm_kernel,
        out_shape=(
            jax.ShapeDtypeStruct(populations.shape, jnp.float32),
            jax.ShapeDtypeStruct(solid_flag.shape, jnp.float32),
        ),
        scratch_shapes=[pltpu.VMEM(populations.shape, jnp.float32)],
        interpret=interpret,
    )(populations, solid_flag, *halos)


def solution(mesh):
    placed = (
        P(None, None, "gx", "gy"),
        P(None, "gx", "gy"),
        P(None, "gx", "gy"),
        P(("gx", "gy")),
        P(("gx", "gy")),
        P(("gx", "gy")),
        P(None, ("gx", "gy")),
        P(None, ("gx", "gy")),
    )
    return jax.shard_map(
        on_device,
        mesh=mesh,
        in_specs=placed,
        out_specs=(P(None, None, "gx", "gy"), P(("gx", "gy")), P(("gx", "gy"))),
        check_vma=False,
    )
```
